32 devices in a mesh: gz: 2 (over x), gy: 4 (over z), gx: 4 (over y, core).
Axes of the slice: x: 2, y: 2, z: 4, core: 2. Of those that a mesh axis runs over, the one named last changes fastest.
Arguments:
- earlier_window_curl_state: float32 [2, 16, 512, 512], P(None, 'gz', 'gy', 'gx'), may hold values from -6 to 6
- material_resistivity_inverse: float32 [16, 512, 512], P('gz', 'gy', 'gx'), may hold values from 0.5 to 5
- winding_current_pattern: float32 [2, 512, 512], P(None, 'gy', 'gx'), may hold values from -8 to 8
- winding_axial_centre: int32 [1], replicated, may hold values from 0 to 15
- specimen_presence_flags: int32 [2, 64, 64], replicated, may hold values 0 or 1
- specimen_kelvin_values: float32 [16, 512, 384], P('gz', 'gy'), may hold values from -4 to 4
Outputs:
- potential_out: float32 [2, 16, 512, 512], P(None, 'gz', 'gy', 'gx')
- temperature_out: float32 [16, 512, 384], P('gz', 'gy')
The draws below stay inside these ranges and needn't reach their ends.
All inputs are finite; a program needn't handle non-finite values.
Results may differ from the reference program's by a relative error of at most 0.00002.
Values sent between devices are 32-bit elements; how exact they have to be, the bound alone decides.
No kernel may reach another device: no remote copies, remote signals or barrier semaphores. Data moves between devices by JAX's collectives and lax.ppermute only.
A program may use at most 128 MiB of HBM per device.

```python
import math
import jax
import jax.numpy as jnp

MB = 8
STEPS = 4
AXIAL_CELL_COUNT = 16
TRANS_ROW_COUNT = 512
NX = 512
SPECIMEN_COLUMNS = 384
COILW = 4


def touch_ends(result, key, least, largest):
    extent = result.shape
    spot = [jax.random.randint(jax.random.fold_in(key, axis), (), 0, extent[axis]) for axis in range(len(extent))]
    result = result.at[tuple(spot)].set(least)
    longest = extent.index(max(extent))
    spot[longest] = (spot[longest] + 1) % extent[longest]
    return result.at[tuple(spot)].set(largest)


def block_levels(rng, shape, shards, low, largest):
    def one(axis_at, parts):
        heights = jax.random.uniform(jax.random.fold_in(jax.random.fold_in(rng, 6), axis_at), (parts,), jnp.float32, low / len(shards), largest / len(shards))
        return jnp.repeat(jnp.exp(heights), shape[axis_at] // parts).reshape((-1,) + (1,) * (len(shape) - axis_at - 1))

    factor_of = one(*shards[0])
    for cut in shards[1:]:
        factor_of = factor_of * one(*cut)
    return factor_of


def bell_draw(own_key, shape, width, limit, split=(), held_as=jnp.bfloat16):
    gain = block_levels(own_key, shape, split, -0.22, 0.18) if split else 1.0
    entries = jax.random.normal(own_key, shape, jnp.float32) * width * gain
    return jnp.minimum(jnp.maximum(entries, -limit), limit).astype(held_as)


def setup_inputs(seed: int = 0) -> dict:
    streams_of = jax.random.split(jax.random.key(seed), 7)
    earlier_window_curl_state = bell_draw(streams_of[0], (2, AXIAL_CELL_COUNT, TRANS_ROW_COUNT, NX), 1.0, 6.0, ((1, 2), (2, 4), (3, 4)), jnp.float32)
    material_resistivity_inverse = jnp.clip(jnp.exp(math.log(5.0) - 2.3025851 * jax.random.uniform(streams_of[1], (AXIAL_CELL_COUNT, TRANS_ROW_COUNT, NX), jnp.float32) ** block_levels(streams_of[1], (AXIAL_CELL_COUNT, TRANS_ROW_COUNT, NX), ((0, 2), (1, 4), (2, 4)), -0.2, 0.2)), 0.5, 5.0)
    winding_current_pattern = bell_draw(streams_of[2], (2, TRANS_ROW_COUNT, NX), 2.0, 8.0, ((1, 4), (2, 4)), jnp.float32)
    winding_axial_centre = jax.random.randint(streams_of[3], (1,), 0, AXIAL_CELL_COUNT).astype(jnp.int32)
    specimen_presence_flags = touch_ends((jax.random.randint(streams_of[4], (AXIAL_CELL_COUNT // MB, TRANS_ROW_COUNT // MB, NX // MB), 0, 4) < 3).astype(jnp.int32), jax.random.fold_in(streams_of[4], 1), 0, 1)
    specimen_kelvin_values = bell_draw(streams_of[5], (AXIAL_CELL_COUNT, TRANS_ROW_COUNT, SPECIMEN_COLUMNS), 1.0, 4.0, ((0, 2), (1, 4)), jnp.float32)
    return {"earlier_window_curl_state": earlier_window_curl_state, "material_resistivity_inverse": material_resistivity_inverse, "winding_current_pattern": winding_current_pattern, "winding_axial_centre": winding_axial_centre, "specimen_presence_flags": specimen_presence_flags, "specimen_kelvin_values": specimen_kelvin_values}


WEIGHTS = (0.8, 1.0, 1.25)
SHIFT = 0.2
HEATING = 0.02
CONDUCT = 0.16
SOFTEN = 0.25


def expand_blocks(blocks):
    cells = jnp.repeat(blocks, MB, axis=0)
    cells = jnp.repeat(cells, MB, axis=1)
    return jnp.repeat(cells, MB, axis=2).astype(jnp.float32)


def neighbours(bordered_segment):
    total = bordered_segment[:, 2:, 1:-1, 1:-1] + bordered_segment[:, :-2, 1:-1, 1:-1]
    total = total + bordered_segment[:, 1:-1, 2:, 1:-1] + bordered_segment[:, 1:-1, :-2, 1:-1]
    return total + bordered_segment[:, 1:-1, 1:-1, 2:] + bordered_segment[:, 1:-1, 1:-1, :-2]


def relax(magnetic_curl_state, beside, source, coupling, factor):
    diagonal = 6.0 + SHIFT
    real_res = source[0] - (diagonal * magnetic_curl_state[0] - coupling * magnetic_curl_state[1] - beside[0])
    imag_res = source[1] - (diagonal * magnetic_curl_state[1] + coupling * magnetic_curl_state[0] - beside[1])
    scaled = factor / (diagonal * diagonal + coupling * coupling)
    return jnp.stack([magnetic_curl_state[0] + scaled * (diagonal * real_res + coupling * imag_res),
                      magnetic_curl_state[1] + scaled * (diagonal * imag_res - coupling * real_res)])


def six_faces(array):
    return [array[2:, 1:-1, 1:-1], array[:-2, 1:-1, 1:-1], array[1:-1, 2:, 1:-1],
            array[1:-1, :-2, 1:-1], array[1:-1, 1:-1, 2:], array[1:-1, 1:-1, :-2]]


def diffusivity_coefficient(bordered_segment, bordered_segment_flags, ohmic_dissipation):
    centre = bordered_segment[1:-1, 1:-1, 1:-1]
    centre_mask = bordered_segment_flags[1:-1, 1:-1, 1:-1]
    centre_kappa = 1.0 / (1.0 + SOFTEN * centre * centre)
    flux = jnp.zeros_like(centre)
    for other, other_mask in zip(six_faces(bordered_segment), six_faces(bordered_segment_flags)):
        kappa = 1.0 / (1.0 + SOFTEN * other * other)
        flux = flux + other_mask * (centre_kappa + kappa) * (other - centre)
    return centre + 0.5 * CONDUCT * centre_mask * flux + ohmic_dissipation


def reference(earlier_window_curl_state, material_resistivity_inverse, winding_current_pattern, winding_axial_centre, specimen_presence_flags, specimen_kelvin_values):
    cell_mask = expand_blocks(specimen_presence_flags)
    coupling = cell_mask * material_resistivity_inverse
    axial = (jnp.arange(AXIAL_CELL_COUNT).astype(jnp.float32) - winding_axial_centre[0].astype(jnp.float32)) / COILW
    profile = 1.0 / (1.0 + axial * axial)
    source = profile[None, :, None, None] * winding_current_pattern[:, None, :, :]
    magnetic_curl_state = earlier_window_curl_state
    for factor in WEIGHTS:
        bordered_segment = jnp.pad(magnetic_curl_state, ((0, 0), (1, 1), (1, 1), (1, 1)))
        magnetic_curl_state = relax(magnetic_curl_state, neighbours(bordered_segment), source, coupling, factor)
    offset = NX - SPECIMEN_COLUMNS
    ohmic_dissipation = (HEATING * coupling * (magnetic_curl_state[0] * magnetic_curl_state[0] + magnetic_curl_state[1] * magnetic_curl_state[1]))[:, :, offset:]
    bordered_segment_flags = jnp.pad(cell_mask[:, :, offset:], 1)
    segment_kelvin = specimen_kelvin_values
    for number in range(STEPS):
        segment_kelvin = diffusivity_coefficient(jnp.pad(segment_kelvin, 1), bordered_segment_flags, ohmic_dissipation)
    return magnetic_curl_state, segment_kelvin
```

```python
import jax
import jax.numpy as jnp
from jax import lax
from jax.experimental import pallas as pl
from jax.experimental.pallas import tpu as pltpu
from jax.sharding import PartitionSpec as P

MB = 8
STEPS = 4


WEIGHTS = (0.8, 1.0, 1.25)
SHIFT = 0.2
HEATING = 0.02
CONDUCT = 0.16
SOFTEN = 0.25


def expand_blocks(blocks):
    cells = jnp.repeat(blocks, MB, axis=0)
    cells = jnp.repeat(cells, MB, axis=1)
    return jnp.repeat(cells, MB, axis=2).astype(jnp.float32)


def _shifts(a, lo_row, hi_row, xlo_t, xhi_t):
    ny, nx = a.shape
    row = lax.broadcasted_iota(jnp.int32, (ny, nx), 0)
    col = lax.broadcasted_iota(jnp.int32, (ny, nx), 1)
    y_up = jnp.where(row == ny - 1, jnp.broadcast_to(hi_row, (ny, nx)), pltpu.roll(a, ny - 1, 0))
    y_dn = jnp.where(row == 0, jnp.broadcast_to(lo_row, (ny, nx)), pltpu.roll(a, 1, 0))
    srow = lax.broadcasted_iota(jnp.int32, (nx, ny), 0)
    edge = jnp.where(srow == 0, xlo_t, jnp.where(srow == nx - 1, xhi_t, 0.0)).T
    x_up = jnp.where(col == nx - 1, edge, pltpu.roll(a, nx - 1, 1))
    x_dn = jnp.where(col == 0, edge, pltpu.roll(a, 1, 1))
    return y_up, y_dn, x_up, x_dn


def _write_faces(new, z, depth, oz0, oz1, oy0, oy1, ox0, ox1, lead=()):
    ny = new.shape[0]
    if z == 0:
        oz0[lead] = new
    if z == depth - 1:
        oz1[lead] = new
    oy0[lead + (pl.ds(z, 1),)] = new[0:1, :]
    oy1[lead + (pl.ds(z, 1),)] = new[ny - 1 : ny, :]
    t = new.T
    ox0[lead + (pl.ds(z, 1),)] = t[0:1, :]
    ox1[lead + (pl.ds(z, 1),)] = t[-1:, :]


def _em_kernel(factor, last, prof, f, cpl, w, zlo, zhi, ylo, yhi, xlo, xhi, *outs):
    depth = f.shape[1]
    diagonal = 6.0 + SHIFT
    if last:
        (o, heat) = outs
    else:
        (o, oz0, oz1, oy0, oy1, ox0, ox1) = outs
    for z in range(depth):
        beside = []
        cur = [f[c, z] for c in range(2)]
        for c in range(2):
            a = cur[c]
            z_up = f[c, z + 1] if z + 1 < depth else zhi[c]
            z_dn = f[c, z - 1] if z > 0 else zlo[c]
            y_up, y_dn, x_up, x_dn = _shifts(
                a, ylo[c, pl.ds(z, 1), :], yhi[c, pl.ds(z, 1), :],
                jnp.broadcast_to(xlo[c, pl.ds(z, 1), :], a.shape[::-1]),
                jnp.broadcast_to(xhi[c, pl.ds(z, 1), :], a.shape[::-1]),
            )
            total = z_up + z_dn
            total = total + y_up + y_dn
            beside.append(total + x_up + x_dn)
        k = cpl[z]
        s0 = prof[z] * w[0]
        s1 = prof[z] * w[1]
        real_res = s0 - (diagonal * cur[0] - k * cur[1] - beside[0])
        imag_res = s1 - (diagonal * cur[1] + k * cur[0] - beside[1])
        scaled = factor / (diagonal * diagonal + k * k)
        n0 = cur[0] + scaled * (diagonal * real_res + k * imag_res)
        n1 = cur[1] + scaled * (diagonal * imag_res - k * real_res)
        o[0, z] = n0
        o[1, z] = n1
        if last:
            heat[z] = HEATING * k * (n0 * n0 + n1 * n1)
        else:
            for c, n in ((0, n0), (1, n1)):
                _write_faces(n, z, depth, oz0, oz1, oy0, oy1, ox0, ox1, lead=(c,))


def _heat_kernel(t, q, m, mzlo, mzhi, mylo, myhi, mxlo, mxhi,
                 tzlo, tzhi, tylo, tyhi, txlo, txhi, o, oz0, oz1, oy0, oy1, ox0, ox1):
    depth = t.shape[0]
    for z in range(depth):
        c = t[z]
        shape = c.shape
        z_up = t[z + 1] if z + 1 < depth else tzhi[...]
        z_dn = t[z - 1] if z > 0 else tzlo[...]
        mz_up = m[z + 1] if z + 1 < depth else mzhi[...]
        mz_dn = m[z - 1] if z > 0 else mzlo[...]
        y_up, y_dn, x_up, x_dn = _shifts(
            c, tylo[pl.ds(z, 1), :], tyhi[pl.ds(z, 1), :],
            jnp.broadcast_to(txlo[pl.ds(z, 1), :], shape[::-1]),
            jnp.broadcast_to(txhi[pl.ds(z, 1), :], shape[::-1]),
        )
        my_up, my_dn, mx_up, mx_dn = _shifts(
            m[z], mylo[pl.ds(z, 1), :], myhi[pl.ds(z, 1), :],
            jnp.broadcast_to(mxlo[pl.ds(z, 1), :], shape[::-1]),
            jnp.broadcast_to(mxhi[pl.ds(z, 1), :], shape[::-1]),
        )
        centre_kappa = 1.0 / (1.0 + SOFTEN * c * c)
        flux = jnp.zeros_like(c)
        for other, other_mask in (
            (z_up, mz_up), (z_dn, mz_dn), (y_up, my_up), (y_dn, my_dn), (x_up, mx_up), (x_dn, mx_dn)
        ):
            kappa = 1.0 / (1.0 + SOFTEN * other * other)
            flux = flux + other_mask * (centre_kappa + kappa) * (other - c)
        new = c + 0.5 * CONDUCT * m[z] * flux + q[z]
        o[z] = new
        _write_faces(new, z, depth, oz0, oz1, oy0, oy1, ox0, ox1)


def _vmem_call(kernel, out_shape, n_in, smem_first=False):
    specs = [pl.BlockSpec(memory_space=pltpu.VMEM)] * n_in
    if smem_first:
        specs[0] = pl.BlockSpec(memory_space=pltpu.SMEM)
    return pl.pallas_call(
        kernel,
        out_shape=out_shape,
        in_specs=specs,
        out_specs=[pl.BlockSpec(memory_space=pltpu.VMEM)] * len(out_shape),
    )


def _faces(a, lead):
    return (
        a[lead + (0,)], a[lead + (-1,)],
        a[lead + (slice(None), 0, slice(None))], a[lead + (slice(None), -1, slice(None))],
        a[lead + (slice(None), slice(None), 0)], a[lead + (slice(None), slice(None), -1)],
    )


def _exchange(faces, axes, pairs):
    received = []
    for (lo_face, hi_face), axis, (up, down) in zip(
        ((faces[0], faces[1]), (faces[2], faces[3]), (faces[4], faces[5])), axes, pairs
    ):
        received.append(lax.ppermute(hi_face, axis, up))
        received.append(lax.ppermute(lo_face, axis, down))
    return received


def _line_pairs(n, first=0):
    up = [(i, i + 1) for i in range(first, n - 1)]
    down = [(j, i) for i, j in up]
    return up, down


def on_device(
    earlier_window_curl_state,
    material_resistivity_inverse,
    winding_current_pattern,
    winding_axial_centre,
    specimen_presence_flags,
    specimen_kelvin_values,
):
    depth, height, breadth = material_resistivity_inverse.shape
    n_gz, n_gy, n_gx = lax.axis_size("gz"), lax.axis_size("gy"), lax.axis_size("gx")
    z_total = depth * n_gz
    x_total = breadth * n_gx
    gz_i, gy_i, gx_i = lax.axis_index("gz"), lax.axis_index("gy"), lax.axis_index("gx")
    z_start = gz_i * depth
    y_start = gy_i * height
    x_start = gx_i * breadth
    own_blocks = lax.dynamic_slice(
        specimen_presence_flags,
        (z_start // MB, y_start // MB, x_start // MB),
        (depth // MB, height // MB, breadth // MB),
    )
    coupling = expand_blocks(own_blocks) * material_resistivity_inverse
    coil_width = z_total // 4
    axial = (
        (z_start + jnp.arange(depth)).astype(jnp.float32)
        - winding_axial_centre[0].astype(jnp.float32)
    ) / coil_width
    profile = 1.0 / (1.0 + axial * axial)

    axes = ("gz", "gy", "gx")
    pairs = (_line_pairs(n_gz), _line_pairs(n_gy), _line_pairs(n_gx))
    field = earlier_window_curl_state
    faces = _faces(field, (slice(None),))
    fshape = jax.ShapeDtypeStruct(field.shape, jnp.float32)
    zf = jax.ShapeDtypeStruct((2, height, breadth), jnp.float32)
    yf = jax.ShapeDtypeStruct((2, depth, breadth), jnp.float32)
    xf = jax.ShapeDtypeStruct((2, depth, height), jnp.float32)
    qshape = jax.ShapeDtypeStruct((depth, height, breadth), jnp.float32)
    for i, factor in enumerate(WEIGHTS):
        last = i == len(WEIGHTS) - 1
        received = _exchange(faces, axes, pairs)
        outs = (fshape, qshape) if last else (fshape, zf, zf, yf, yf, xf, xf)
        res = _vmem_call(
            lambda *r, factor=factor, last=last: _em_kernel(factor, last, *r), outs, 10, True
        )(profile, field, coupling, winding_current_pattern, *received)
        if last:
            field, heat = res
        else:
            field, faces = res[0], tuple(res[1:])

    specimen_columns = specimen_kelvin_values.shape[2]
    offset = x_total - specimen_columns
    assert offset % breadth == 0 and specimen_columns % breadth == 0
    first_owner = offset // breadth
    j_start = x_start - offset
    j_clamped = jnp.maximum(j_start, 0)
    kelvin = lax.dynamic_slice_in_dim(specimen_kelvin_values, j_clamped, breadth, 2)

    window = jnp.pad(specimen_presence_flags[:, :, offset // MB :], 1)
    blocks = lax.dynamic_slice(
        window,
        (z_start // MB, y_start // MB, j_clamped // MB),
        (depth // MB + 2, height // MB + 2, breadth // MB + 2),
    )
    m_ext = expand_blocks(blocks)[MB - 1 : MB + 1 + depth, MB - 1 : MB + 1 + height, MB - 1 : MB + 1 + breadth]
    m_own = m_ext[1:-1, 1:-1, 1:-1]
    m_faces = (
        m_ext[0, 1:-1, 1:-1], m_ext[-1, 1:-1, 1:-1],
        m_ext[1:-1, 0, 1:-1], m_ext[1:-1, -1, 1:-1],
        m_ext[1:-1, 1:-1, 0], m_ext[1:-1, 1:-1, -1],
    )
    t_pairs = (_line_pairs(n_gz), _line_pairs(n_gy), _line_pairs(n_gx, first_owner))
    t_faces = _faces(kelvin, ())
    tshape = jax.ShapeDtypeStruct(kelvin.shape, jnp.float32)
    tz = jax.ShapeDtypeStruct((height, breadth), jnp.float32)
    ty = jax.ShapeDtypeStruct((depth, breadth), jnp.float32)
    tx = jax.ShapeDtypeStruct((depth, height), jnp.float32)
    heat_call = _vmem_call(_heat_kernel, (tshape, tz, tz, ty, ty, tx, tx), 15)
    for number in range(STEPS):
        received = _exchange(t_faces, axes, t_pairs)
        res = heat_call(kelvin, heat, m_own, *m_faces, *received)
        kelvin, t_faces = res[0], tuple(res[1:])
    gathered = lax.all_gather(kelvin, "gx", axis=2, tiled=True)
    segment_kelvin = gathered[:, :, first_owner * breadth :]
    return (field, segment_kelvin)


def solution(mesh):
    placed = (
        P(None, "gz", "gy", "gx"),
        P("gz", "gy", "gx"),
        P(None, "gy", "gx"),
        P(),
        P(),
        P("gz", "gy", None),
    )
    return jax.shard_map(
        on_device,
        mesh=mesh,
        in_specs=placed,
        out_specs=(P(None, "gz", "gy", "gx"), P("gz", "gy", None)),
        check_vma=False,
    )
```

```python
import jax
import jax.numpy as jnp
from jax import lax
from jax.experimental import pallas as pl
from jax.experimental.pallas import tpu as pltpu
from jax.sharding import PartitionSpec as P

MB = 8
STEPS = 4


WEIGHTS = (0.8, 1.0, 1.25)
SHIFT = 0.2
HEATING = 0.02
CONDUCT = 0.16
SOFTEN = 0.25

H = MB


def _rolls(a):
    rows, lanes = a.shape
    return (
        pltpu.roll(a, rows - 1, 0), pltpu.roll(a, 1, 0),
        pltpu.roll(a, lanes - 1, 1), pltpu.roll(a, 1, 1),
    )


def _em_kernel(factor, last, depth, prof, f, cpl, w, inside, zlo, zhi, *outs):
    diagonal = 6.0 + SHIFT
    if last:
        (heat, own) = outs
        ny, nx = own.shape[2], own.shape[3]
    else:
        (o, oz0, oz1) = outs
    keep = inside[...] > 0.0
    for z in range(depth):
        cur = [f[c * depth + z] for c in range(2)]
        beside = []
        for c in range(2):
            z_up = f[c * depth + z + 1] if z + 1 < depth else zhi[c]
            z_dn = f[c * depth + z - 1] if z > 0 else zlo[c]
            y_up, y_dn, x_up, x_dn = _rolls(cur[c])
            total = z_up + z_dn
            total = total + y_up + y_dn
            beside.append(total + x_up + x_dn)
        k = cpl[z]
        s0 = prof[z] * w[0]
        s1 = prof[z] * w[1]
        real_res = s0 - (diagonal * cur[0] - k * cur[1] - beside[0])
        imag_res = s1 - (diagonal * cur[1] + k * cur[0] - beside[1])
        scaled = factor / (diagonal * diagonal + k * k)
        n0 = jnp.where(keep, cur[0] + scaled * (diagonal * real_res + k * imag_res), 0.0)
        n1 = jnp.where(keep, cur[1] + scaled * (diagonal * imag_res - k * real_res), 0.0)
        if last:
            heat[z] = HEATING * k * (n0 * n0 + n1 * n1)
            own[0, z] = n0[0:ny, 0:nx]
            own[1, z] = n1[0:ny, 0:nx]
        else:
            o[z] = n0
            o[depth + z] = n1
            if z == 0:
                oz0[0] = n0
                oz0[1] = n1
            if z == depth - 1:
                oz1[0] = n0
                oz1[1] = n1


def _heat_kernel(last, depth, t, q, m, tzlo, tzhi, *outs):
    if last:
        (own,) = outs
        ny, nx = own.shape[1], own.shape[2]
    else:
        (o, oz0, oz1) = outs
    for z in range(depth):
        c = t[z]
        z_up = t[z + 1] if z + 1 < depth else tzhi[...]
        z_dn = t[z - 1] if z > 0 else tzlo[...]
        y_up, y_dn, x_up, x_dn = _rolls(c)
        mc = m[z + 1]
        my_up, my_dn, mx_up, mx_dn = _rolls(mc)
        centre_kappa = 1.0 / (1.0 + SOFTEN * c * c)
        flux = jnp.zeros_like(c)
        for other, other_mask in (
            (z_up, m[z + 2]), (z_dn, m[z]), (y_up, my_up), (y_dn, my_dn), (x_up, mx_up), (x_dn, mx_dn)
        ):
            kappa = 1.0 / (1.0 + SOFTEN * other * other)
            flux = flux + other_mask * (centre_kappa + kappa) * (other - c)
        new = c + 0.5 * CONDUCT * mc * flux + q[z]
        if last:
            own[z] = new[0:ny, 0:nx]
        else:
            o[z] = new
            if z == 0:
                oz0[...] = new
            if z == depth - 1:
                oz1[...] = new


def _vmem_call(kernel, out_shape, n_in, smem_first=False):
    specs = [pl.BlockSpec(memory_space=pltpu.VMEM)] * n_in
    if smem_first:
        specs[0] = pl.BlockSpec(memory_space=pltpu.SMEM)
    return pl.pallas_call(
        kernel,
        out_shape=out_shape,
        in_specs=specs,
        out_specs=[pl.BlockSpec(memory_space=pltpu.VMEM)] * len(out_shape),
    )


def _line_pairs(n, first=0):
    up = [(i, i + 1) for i in range(first, n - 1)]
    down = [(j, i) for i, j in up]
    return up, down


def _frame_index(start, own, total):
    nb, tb, hb = own // MB, total // MB, H // MB
    body = jnp.arange(nb + hb)
    tail = jnp.arange(-hb, 0)
    gap = jnp.full((tb - nb - 2 * hb,), -(10 ** 6), jnp.int32)
    return start // MB + jnp.concatenate([body, gap, tail]).astype(jnp.int32)


def _expand(blocks):
    cells = jnp.repeat(blocks, MB, axis=0)
    cells = jnp.repeat(cells, MB, axis=1)
    return jnp.repeat(cells, MB, axis=2).astype(jnp.float32)


def _pick(flags, zi, yi, xi):
    ok = [(i >= 0) & (i < n) for i, n in zip((zi, yi, xi), flags.shape)]
    sel = jnp.take(flags, jnp.clip(zi, 0, flags.shape[0] - 1), axis=0)
    sel = jnp.take(sel, jnp.clip(yi, 0, flags.shape[1] - 1), axis=1)
    sel = jnp.take(sel, jnp.clip(xi, 0, flags.shape[2] - 1), axis=2)
    valid = ok[0][:, None, None] & ok[1][None, :, None] & ok[2][None, None, :]
    return jnp.where(valid, sel, 0)


def on_device(
    earlier_window_curl_state,
    material_resistivity_inverse,
    winding_current_pattern,
    winding_axial_centre,
    specimen_presence_flags,
    specimen_kelvin_values,
):
    depth, height, breadth = material_resistivity_inverse.shape
    n_gz, n_gy, n_gx = lax.axis_size("gz"), lax.axis_size("gy"), lax.axis_size("gx")
    z_total, y_total, x_total = depth * n_gz, height * n_gy, breadth * n_gx
    gz_i, gy_i, gx_i = lax.axis_index("gz"), lax.axis_index("gy"), lax.axis_index("gx")
    z_start, y_start, x_start = gz_i * depth, gy_i * height, gx_i * breadth
    rows = height + 2 * H
    lanes = -(-(breadth + 2 * H) // 128) * 128
    gap = lanes - breadth - 2 * H
    specimen_columns = specimen_kelvin_values.shape[2]
    offset = x_total - specimen_columns
    assert offset % breadth == 0 and depth % MB == 0 and height % MB == 0 and breadth % MB == 0
    first_owner = offset // breadth

    coil_width = z_total // 4
    axial = (
        (z_start + jnp.arange(depth)).astype(jnp.float32)
        - winding_axial_centre[0].astype(jnp.float32)
    ) / coil_width
    profile = 1.0 / (1.0 + axial * axial)

    stack = jnp.concatenate(
        [earlier_window_curl_state.reshape(2 * depth, height, breadth), material_resistivity_inverse,
         winding_current_pattern], axis=0)
    up_x, down_x = _line_pairs(n_gx)
    from_left = lax.ppermute(jnp.swapaxes(stack[:, :, breadth - H:], 1, 2), "gx", up_x)
    from_right = lax.ppermute(jnp.swapaxes(stack[:, :, :H], 1, 2), "gx", down_x)
    nch = stack.shape[0]
    xext = jnp.concatenate(
        [stack, jnp.swapaxes(from_right, 1, 2), jnp.zeros((nch, height, gap), jnp.float32),
         jnp.swapaxes(from_left, 1, 2)], axis=2)

    j_start = x_start - offset
    kpad = jnp.pad(specimen_kelvin_values, ((0, 0), (0, 0), (H, H)))
    t_body = lax.dynamic_slice_in_dim(kpad, j_start + H, breadth + H, 2)
    t_tail = lax.dynamic_slice_in_dim(kpad, j_start, H, 2)
    t_x = jnp.concatenate([t_body, jnp.zeros((depth, height, gap), jnp.float32), t_tail], axis=2)

    ystack = jnp.concatenate([xext, t_x], axis=0)
    up_y, down_y = _line_pairs(n_gy)
    from_above = lax.ppermute(ystack[:, height - H:, :], "gy", up_y)
    from_below = lax.ppermute(ystack[:, :H, :], "gy", down_y)
    frame = jnp.concatenate([ystack, from_below, from_above], axis=1)
    field = frame[: 2 * depth]
    material = frame[2 * depth: 3 * depth]
    winding = frame[3 * depth: 3 * depth + 2]
    kelvin = frame[3 * depth + 2:]

    yi = _frame_index(y_start, height, rows)
    xi = _frame_index(x_start, breadth, lanes)
    ycell = jnp.repeat(yi, MB) * MB + jnp.tile(jnp.arange(MB), rows // MB)
    xcell = jnp.repeat(xi, MB) * MB + jnp.tile(jnp.arange(MB), lanes // MB)
    inside = (((ycell >= 0) & (ycell < y_total))[:, None]
              & ((xcell >= 0) & (xcell < x_total))[None, :]).astype(jnp.float32)
    zb = z_start // MB + jnp.arange(depth // MB)
    coupling = _expand(_pick(specimen_presence_flags, zb, yi, xi)) * material
    tz = z_start // MB + jnp.arange(-1, depth // MB + 1)
    tb = _pick(specimen_presence_flags, tz, yi, xi)
    tb = jnp.where((xi >= offset // MB)[None, None, :], tb, 0)
    t_mask = _expand(tb)[MB - 1: MB + 1 + depth]

    up_z, down_z = _line_pairs(n_gz)
    fshape = jax.ShapeDtypeStruct((2 * depth, rows, lanes), jnp.float32)
    plane2 = jax.ShapeDtypeStruct((2, rows, lanes), jnp.float32)
    qshape = jax.ShapeDtypeStruct((depth, rows, lanes), jnp.float32)
    oshape = jax.ShapeDtypeStruct((2, depth, height, breadth), jnp.float32)
    lo_plane = field[jnp.array([0, depth])]
    hi_plane = field[jnp.array([depth - 1, 2 * depth - 1])]
    for i, factor in enumerate(WEIGHTS):
        last = i == len(WEIGHTS) - 1
        zlo = lax.ppermute(hi_plane, "gz", up_z)
        zhi = lax.ppermute(lo_plane, "gz", down_z)
        outs = (qshape, oshape) if last else (fshape, plane2, plane2)
        res = _vmem_call(
            lambda *r, factor=factor, last=last: _em_kernel(factor, last, depth, *r), outs, 7, True
        )(profile, field, coupling, winding, inside, zlo, zhi)
        if last:
            heat, field_out = res
        else:
            field, lo_plane, hi_plane = res

    tshape = jax.ShapeDtypeStruct((depth, rows, lanes), jnp.float32)
    tplane = jax.ShapeDtypeStruct((rows, lanes), jnp.float32)
    town = jax.ShapeDtypeStruct((depth, height, breadth), jnp.float32)
    lo_t, hi_t = kelvin[0], kelvin[depth - 1]
    for number in range(STEPS):
        last = number == STEPS - 1
        tzlo = lax.ppermute(hi_t, "gz", up_z)
        tzhi = lax.ppermute(lo_t, "gz", down_z)
        outs = (town,) if last else (tshape, tplane, tplane)
        res = _vmem_call(
            lambda *r, last=last: _heat_kernel(last, depth, *r), outs, 5
        )(kelvin, heat, t_mask, tzlo, tzhi)
        if last:
            (own_t,) = res
        else:
            kelvin, lo_t, hi_t = res

    owners = list(range(first_owner, n_gx))
    held = [own_t]
    for s in range(1, n_gx):
        held.append(lax.ppermute(own_t, "gx", [(k, (k + s) % n_gx) for k in owners]))
    held = jnp.stack(held)
    pieces = [lax.dynamic_index_in_dim(held, (gx_i - k) % n_gx, 0, keepdims=False) for k in owners]
    segment_kelvin = jnp.concatenate(pieces, axis=2)
    return (field_out, segment_kelvin)


def solution(mesh):
    placed = (
        P(None, "gz", "gy", "gx"),
        P("gz", "gy", "gx"),
        P(None, "gy", "gx"),
        P(),
        P(),
        P("gz", "gy", None),
    )
    return jax.shard_map(
        on_device,
        mesh=mesh,
        in_specs=placed,
        out_specs=(P(None, "gz", "gy", "gx"), P("gz", "gy", None)),
        check_vma=False,
    )
```

```python
import jax
import jax.numpy as jnp
from jax import lax
from jax.experimental import pallas as pl
from jax.experimental.pallas import tpu as pltpu
from jax.sharding import PartitionSpec as P

MB = 8
STEPS = 4


WEIGHTS = (0.8, 1.0, 1.25)
SHIFT = 0.2
HEATING = 0.02
CONDUCT = 0.16
SOFTEN = 0.25

H = MB


def _rolls(a):
    rows, lanes = a.shape
    return (
        pltpu.roll(a, rows - 1, 0), pltpu.roll(a, 1, 0),
        pltpu.roll(a, lanes - 1, 1), pltpu.roll(a, 1, 1),
    )


def _selectors(pos, rows, lanes, height, breadth, x_first_block):
    shift = MB.bit_length() - 1
    r = lax.shift_right_logical(lax.broadcasted_iota(jnp.int32, (rows, 128), 0), shift)
    b = lax.broadcasted_iota(jnp.int32, (rows, 128), 1)
    ty = pos[1] + jnp.where(r < (height + H) // MB, r, r - rows // MB)
    sy = (b == ty).astype(jnp.float32)
    l = lax.shift_right_logical(lax.broadcasted_iota(jnp.int32, (lanes, 128), 0), shift)
    bx = lax.broadcasted_iota(jnp.int32, (lanes, 128), 1)
    far = jnp.where(l >= (lanes - H) // MB, l - lanes // MB, -(10 ** 6))
    tx = pos[2] + jnp.where(l < (breadth + H) // MB, l, far)
    sx = ((bx == tx) & (bx >= x_first_block)).astype(jnp.float32)
    return sy, sx


def _cells(fl, zb, sy, sx):
    a = jnp.dot(sy, fl[zb], preferred_element_type=jnp.float32)
    return lax.dot_general(a, sx, (((1,), (1,)), ((), ())), preferred_element_type=jnp.float32)


def _inside(pos, rows, lanes, height, breadth, y_total, x_total):
    r = lax.broadcasted_iota(jnp.int32, (rows, lanes), 0)
    l = lax.broadcasted_iota(jnp.int32, (rows, lanes), 1)
    y = pos[1] * MB + jnp.where(r < height + H, r, r - rows)
    far = jnp.where(l >= lanes - H, l - lanes, -(10 ** 6))
    x = pos[2] * MB + jnp.where(l < breadth + H, l, far)
    return (y >= 0) & (y < y_total) & (x >= 0) & (x < x_total)


def _em_kernel(factor, last, depth, totals, pos, prof, fl, f, mat, w, zlo, zhi, *outs):
    diagonal = 6.0 + SHIFT
    if last:
        (heat, own) = outs
    else:
        (o, oz0, oz1) = outs
    height, breadth, y_total, x_total = totals
    rows, lanes = f.shape[1], f.shape[2]
    keep = _inside(pos, rows, lanes, height, breadth, y_total, x_total)
    sy, sx = _selectors(pos, rows, lanes, height, breadth, 0)
    masks = [_cells(fl, pos[0] + zo, sy, sx) for zo in range(depth // MB)]
    for z in range(depth):
        cur = [f[c * depth + z] for c in range(2)]
        beside = []
        for c in range(2):
            z_up = f[c * depth + z + 1] if z + 1 < depth else zhi[c]
            z_dn = f[c * depth + z - 1] if z > 0 else zlo[c]
            y_up, y_dn, x_up, x_dn = _rolls(cur[c])
            total = z_up + z_dn
            total = total + y_up + y_dn
            beside.append(total + x_up + x_dn)
        k = masks[z // MB] * mat[z]
        s0 = prof[z] * w[0]
        s1 = prof[z] * w[1]
        real_res = s0 - (diagonal * cur[0] - k * cur[1] - beside[0])
        imag_res = s1 - (diagonal * cur[1] + k * cur[0] - beside[1])
        scaled = factor / (diagonal * diagonal + k * k)
        n0 = jnp.where(keep, cur[0] + scaled * (diagonal * real_res + k * imag_res), 0.0)
        n1 = jnp.where(keep, cur[1] + scaled * (diagonal * imag_res - k * real_res), 0.0)
        if last:
            heat[z] = HEATING * k * (n0 * n0 + n1 * n1)
            own[0, z] = n0[0:height, 0:breadth]
            own[1, z] = n1[0:height, 0:breadth]
        else:
            o[z] = n0
            o[depth + z] = n1
            if z == 0:
                oz0[0] = n0
                oz0[1] = n1
            if z == depth - 1:
                oz1[0] = n0
                oz1[1] = n1


def _heat_kernel(last, depth, totals, pos, fl, t, q, tzlo, tzhi, *outs):
    if last:
        (own,) = outs
    else:
        (o, oz0, oz1) = outs
    height, breadth, x_first_block = totals
    rows, lanes = t.shape[1], t.shape[2]
    sy, sx = _selectors(pos, rows, lanes, height, breadth, x_first_block)
    zb_total = fl.shape[0]
    below = pos[0] - 1
    above = pos[0] + depth // MB
    m_below = _cells(fl, jnp.maximum(below, 0), sy, sx) * jnp.where(below >= 0, 1.0, 0.0)
    m_above = _cells(fl, jnp.minimum(above, zb_total - 1), sy, sx) * jnp.where(
        above < zb_total, 1.0, 0.0)
    m_own = [_cells(fl, pos[0] + zo, sy, sx) for zo in range(depth // MB)]
    planes = [m_below] + [m_own[z // MB] for z in range(depth)] + [m_above]
    temps = [tzlo[...]] + [t[z] for z in range(depth)] + [tzhi[...]]
    kaps = [1.0 / (1.0 + SOFTEN * v * v) for v in temps]
    for z in range(depth):
        c = temps[z + 1]
        centre_kappa = kaps[z + 1]
        y_up, y_dn, x_up, x_dn = _rolls(c)
        ky_up, ky_dn, kx_up, kx_dn = _rolls(centre_kappa)
        mc = planes[z + 1]
        my_up, my_dn, mx_up, mx_dn = _rolls(mc)
        flux = jnp.zeros_like(c)
        for other, kappa, other_mask in (
            (temps[z + 2], kaps[z + 2], planes[z + 2]), (temps[z], kaps[z], planes[z]),
            (y_up, ky_up, my_up), (y_dn, ky_dn, my_dn), (x_up, kx_up, mx_up), (x_dn, kx_dn, mx_dn),
        ):
            flux = flux + other_mask * (centre_kappa + kappa) * (other - c)
        new = c + 0.5 * CONDUCT * mc * flux + q[z]
        if last:
            own[z] = new[0:height, 0:breadth]
        else:
            o[z] = new
            if z == 0:
                oz0[...] = new
            if z == depth - 1:
                oz1[...] = new


def _vmem_call(kernel, out_shape, n_in, n_smem=0):
    specs = [pl.BlockSpec(memory_space=pltpu.SMEM)] * n_smem
    specs += [pl.BlockSpec(memory_space=pltpu.VMEM)] * (n_in - n_smem)
    return pl.pallas_call(
        kernel,
        out_shape=out_shape,
        in_specs=specs,
        out_specs=[pl.BlockSpec(memory_space=pltpu.VMEM)] * len(out_shape),
    )


def _line_pairs(n, first=0):
    up = [(i, i + 1) for i in range(first, n - 1)]
    down = [(j, i) for i, j in up]
    return up, down


def on_device(
    earlier_window_curl_state,
    material_resistivity_inverse,
    winding_current_pattern,
    winding_axial_centre,
    specimen_presence_flags,
    specimen_kelvin_values,
):
    depth, height, breadth = material_resistivity_inverse.shape
    n_gz, n_gy, n_gx = lax.axis_size("gz"), lax.axis_size("gy"), lax.axis_size("gx")
    z_total, y_total, x_total = depth * n_gz, height * n_gy, breadth * n_gx
    gz_i, gy_i, gx_i = lax.axis_index("gz"), lax.axis_index("gy"), lax.axis_index("gx")
    z_start, y_start, x_start = gz_i * depth, gy_i * height, gx_i * breadth
    rows = height + 2 * H
    lanes = -(-(breadth + 2 * H) // 128) * 128
    gap = lanes - breadth - 2 * H
    specimen_columns = specimen_kelvin_values.shape[2]
    offset = x_total - specimen_columns
    assert offset % breadth == 0 and depth % MB == 0 and height % MB == 0 and breadth % MB == 0
    first_owner = offset // breadth

    coil_width = z_total // 4
    axial = (
        (z_start + jnp.arange(depth)).astype(jnp.float32)
        - winding_axial_centre[0].astype(jnp.float32)
    ) / coil_width
    profile = 1.0 / (1.0 + axial * axial)

    stack = jnp.concatenate(
        [earlier_window_curl_state.reshape(2 * depth, height, breadth), material_resistivity_inverse,
         winding_current_pattern], axis=0)
    up_x, down_x = _line_pairs(n_gx)
    from_left = lax.ppermute(jnp.swapaxes(stack[:, :, breadth - H:], 1, 2), "gx", up_x)
    from_right = lax.ppermute(jnp.swapaxes(stack[:, :, :H], 1, 2), "gx", down_x)
    nch = stack.shape[0]
    xext = jnp.concatenate(
        [stack, jnp.swapaxes(from_right, 1, 2), jnp.zeros((nch, height, gap), jnp.float32),
         jnp.swapaxes(from_left, 1, 2)], axis=2)

    j_start = x_start - offset
    kpad = jnp.pad(specimen_kelvin_values, ((0, 0), (0, 0), (H, H)))
    t_body = lax.dynamic_slice_in_dim(kpad, j_start + H, breadth + H, 2)
    t_tail = lax.dynamic_slice_in_dim(kpad, j_start, H, 2)
    t_x = jnp.concatenate([t_body, jnp.zeros((depth, height, gap), jnp.float32), t_tail], axis=2)

    ystack = jnp.concatenate([xext, t_x], axis=0)
    up_y, down_y = _line_pairs(n_gy)
    from_above = lax.ppermute(ystack[:, height - H:, :], "gy", up_y)
    from_below = lax.ppermute(ystack[:, :H, :], "gy", down_y)
    frame = jnp.concatenate([ystack, from_below, from_above], axis=1)
    field = frame[: 2 * depth]
    material = frame[2 * depth: 3 * depth]
    winding = frame[3 * depth: 3 * depth + 2]
    kelvin = frame[3 * depth + 2:]

    fb = specimen_presence_flags.shape
    flags = jnp.pad(specimen_presence_flags.astype(jnp.float32),
                    ((0, 0), (0, 128 - fb[1]), (0, 128 - fb[2])))
    pos = jnp.stack([z_start // MB, y_start // MB, x_start // MB]).astype(jnp.int32)

    up_z, down_z = _line_pairs(n_gz)
    fshape = jax.ShapeDtypeStruct((2 * depth, rows, lanes), jnp.float32)
    plane2 = jax.ShapeDtypeStruct((2, rows, lanes), jnp.float32)
    qshape = jax.ShapeDtypeStruct((depth, rows, lanes), jnp.float32)
    oshape = jax.ShapeDtypeStruct((2, depth, height, breadth), jnp.float32)
    lo_plane = field[jnp.array([0, depth])]
    hi_plane = field[jnp.array([depth - 1, 2 * depth - 1])]
    for i, factor in enumerate(WEIGHTS):
        last = i == len(WEIGHTS) - 1
        zlo = lax.ppermute(hi_plane, "gz", up_z)
        zhi = lax.ppermute(lo_plane, "gz", down_z)
        outs = (qshape, oshape) if last else (fshape, plane2, plane2)
        res = _vmem_call(
            lambda *r, factor=factor, last=last: _em_kernel(
                factor, last, depth, (height, breadth, y_total, x_total), *r), outs, 8, 2
        )(pos, profile, flags, field, material, winding, zlo, zhi)
        if last:
            heat, field_out = res
        else:
            field, lo_plane, hi_plane = res

    tshape = jax.ShapeDtypeStruct((depth, rows, lanes), jnp.float32)
    tplane = jax.ShapeDtypeStruct((rows, lanes), jnp.float32)
    town = jax.ShapeDtypeStruct((depth, height, breadth), jnp.float32)
    lo_t, hi_t = kelvin[0], kelvin[depth - 1]
    for number in range(STEPS):
        last = number == STEPS - 1
        tzlo = lax.ppermute(hi_t, "gz", up_z)
        tzhi = lax.ppermute(lo_t, "gz", down_z)
        outs = (town,) if last else (tshape, tplane, tplane)
        res = _vmem_call(
            lambda *r, last=last: _heat_kernel(
                last, depth, (height, breadth, offset // MB), *r), outs, 6, 1
        )(pos, flags, kelvin, heat, tzlo, tzhi)
        if last:
            (own_t,) = res
        else:
            kelvin, lo_t, hi_t = res

    owners = list(range(first_owner, n_gx))
    held = [own_t]
    for s in range(1, n_gx):
        held.append(lax.ppermute(own_t, "gx", [(k, (k + s) % n_gx) for k in owners]))
    held = jnp.stack(held)
    pieces = [lax.dynamic_index_in_dim(held, (gx_i - k) % n_gx, 0, keepdims=False) for k in owners]
    segment_kelvin = jnp.concatenate(pieces, axis=2)
    return (field_out, segment_kelvin)


def solution(mesh):
    placed = (
        P(None, "gz", "gy", "gx"),
        P("gz", "gy", "gx"),
        P(None, "gy", "gx"),
        P(),
        P(),
        P("gz", "gy", None),
    )
    return jax.shard_map(
        on_device,
        mesh=mesh,
        in_specs=placed,
        out_specs=(P(None, "gz", "gy", "gx"), P("gz", "gy", None)),
        check_vma=False,
    )
```

```python
import jax
import jax.numpy as jnp
from jax import lax
from jax.experimental import pallas as pl
from jax.experimental.pallas import tpu as pltpu
from jax.sharding import PartitionSpec as P

MB = 8
STEPS = 4


WEIGHTS = (0.8, 1.0, 1.25)
SHIFT = 0.2
HEATING = 0.02
CONDUCT = 0.16
SOFTEN = 0.25

H = MB


def _rolls(a):
    rows, lanes = a.shape
    return (
        pltpu.roll(a, rows - 1, 0), pltpu.roll(a, 1, 0),
        pltpu.roll(a, lanes - 1, 1), pltpu.roll(a, 1, 1),
    )


def _selectors(pos, rows, lanes, height, breadth, x_first_block):
    shift = MB.bit_length() - 1
    r = lax.shift_right_logical(lax.broadcasted_iota(jnp.int32, (rows, 128), 0), shift)
    b = lax.broadcasted_iota(jnp.int32, (rows, 128), 1)
    ty = pos[1] + jnp.where(r < (height + H) // MB, r, r - rows // MB)
    sy = (b == ty).astype(jnp.float32)
    l = lax.shift_right_logical(lax.broadcasted_iota(jnp.int32, (lanes, 128), 0), shift)
    bx = lax.broadcasted_iota(jnp.int32, (lanes, 128), 1)
    far = jnp.where(l >= (lanes - H) // MB, l - lanes // MB, -(10 ** 6))
    tx = pos[2] + jnp.where(l < (breadth + H) // MB, l, far)
    sx = ((bx == tx) & (bx >= x_first_block)).astype(jnp.float32)
    return sy, sx


def _cells(fl, zb, sy, sx):
    a = jnp.dot(sy, fl[zb], preferred_element_type=jnp.float32)
    return lax.dot_general(a, sx, (((1,), (1,)), ((), ())), preferred_element_type=jnp.float32)


def _inside(pos, rows, lanes, height, breadth, y_total, x_total):
    r = lax.broadcasted_iota(jnp.int32, (rows, lanes), 0)
    l = lax.broadcasted_iota(jnp.int32, (rows, lanes), 1)
    y = pos[1] * MB + jnp.where(r < height + H, r, r - rows)
    far = jnp.where(l >= lanes - H, l - lanes, -(10 ** 6))
    x = pos[2] * MB + jnp.where(l < breadth + H, l, far)
    return (y >= 0) & (y < y_total) & (x >= 0) & (x < x_total)


def _em_kernel(factor, last, depth, totals, pos, prof, fl, f, mat, w, zlo, zhi, *outs):
    diagonal = 6.0 + SHIFT
    if last:
        (heat, own) = outs
    else:
        (o, oz0, oz1) = outs
    height, breadth, y_total, x_total = totals
    rows, lanes = f.shape[1], f.shape[2]
    keep = _inside(pos, rows, lanes, height, breadth, y_total, x_total)
    sy, sx = _selectors(pos, rows, lanes, height, breadth, 0)
    masks = [_cells(fl, pos[0] + zo, sy, sx) for zo in range(depth // MB)]
    for z in range(depth):
        cur = [f[c * depth + z] for c in range(2)]
        beside = []
        for c in range(2):
            z_up = f[c * depth + z + 1] if z + 1 < depth else zhi[c]
            z_dn = f[c * depth + z - 1] if z > 0 else zlo[c]
            y_up, y_dn, x_up, x_dn = _rolls(cur[c])
            total = z_up + z_dn
            total = total + y_up + y_dn
            beside.append(total + x_up + x_dn)
        k = masks[z // MB] * mat[z]
        s0 = prof[z] * w[0]
        s1 = prof[z] * w[1]
        real_res = s0 - (diagonal * cur[0] - k * cur[1] - beside[0])
        imag_res = s1 - (diagonal * cur[1] + k * cur[0] - beside[1])
        scaled = factor / (diagonal * diagonal + k * k)
        n0 = jnp.where(keep, cur[0] + scaled * (diagonal * real_res + k * imag_res), 0.0)
        n1 = jnp.where(keep, cur[1] + scaled * (diagonal * imag_res - k * real_res), 0.0)
        if last:
            heat[z] = HEATING * k * (n0 * n0 + n1 * n1)
            own[0, z] = n0[0:height, 0:breadth]
            own[1, z] = n1[0:height, 0:breadth]
        else:
            o[z] = n0
            o[depth + z] = n1
            if z == 0:
                oz0[0] = n0
                oz0[1] = n1
            if z == depth - 1:
                oz1[0] = n0
                oz1[1] = n1


def _heat_kernel(last, depth, totals, pos, fl, t, q, tzlo, tzhi, *outs):
    if last:
        (own,) = outs
    else:
        (o, oz0, oz1) = outs
    height, breadth, x_first_block = totals
    rows, lanes = t.shape[1], t.shape[2]
    sy, sx = _selectors(pos, rows, lanes, height, breadth, x_first_block)
    zb_total = fl.shape[0]
    below = pos[0] - 1
    above = pos[0] + depth // MB
    m_below = _cells(fl, jnp.maximum(below, 0), sy, sx) * jnp.where(below >= 0, 1.0, 0.0)
    m_above = _cells(fl, jnp.minimum(above, zb_total - 1), sy, sx) * jnp.where(
        above < zb_total, 1.0, 0.0)
    m_own = [_cells(fl, pos[0] + zo, sy, sx) for zo in range(depth // MB)]
    planes = [m_below] + [m_own[z // MB] for z in range(depth)] + [m_above]
    temps = [tzlo[...]] + [t[z] for z in range(depth)] + [tzhi[...]]
    kaps = [1.0 / (1.0 + SOFTEN * v * v) for v in temps]
    for z in range(depth):
        c = temps[z + 1]
        centre_kappa = kaps[z + 1]
        y_up, y_dn, x_up, x_dn = _rolls(c)
        ky_up, ky_dn, kx_up, kx_dn = _rolls(centre_kappa)
        mc = planes[z + 1]
        my_up, my_dn, mx_up, mx_dn = _rolls(mc)
        flux = jnp.zeros_like(c)
        for other, kappa, other_mask in (
            (temps[z + 2], kaps[z + 2], planes[z + 2]), (temps[z], kaps[z], planes[z]),
            (y_up, ky_up, my_up), (y_dn, ky_dn, my_dn), (x_up, kx_up, mx_up), (x_dn, kx_dn, mx_dn),
        ):
            flux = flux + other_mask * (centre_kappa + kappa) * (other - c)
        new = c + 0.5 * CONDUCT * mc * flux + q[z]
        if last:
            own[z] = new[0:height, 0:breadth]
        else:
            o[z] = new
            if z == 0:
                oz0[...] = new
            if z == depth - 1:
                oz1[...] = new


def _vmem_call(kernel, out_shape, n_in, n_smem=0):
    specs = [pl.BlockSpec(memory_space=pltpu.SMEM)] * n_smem
    specs += [pl.BlockSpec(memory_space=pltpu.VMEM)] * (n_in - n_smem)
    return pl.pallas_call(
        kernel,
        out_shape=out_shape,
        in_specs=specs,
        out_specs=[pl.BlockSpec(memory_space=pltpu.VMEM)] * len(out_shape),
    )


def _line_pairs(n, first=0):
    up = [(i, i + 1) for i in range(first, n - 1)]
    down = [(j, i) for i, j in up]
    return up, down


def _broadcast_blocks(own, me, n, first):
    if (n, first) == (4, 1):
        r1 = lax.ppermute(own, "gx", [(2, 0), (3, 1), (1, 2)])
        a = jnp.where((me == 0) | (me == 2), r1, own)
        b = jnp.where((me == 1) | (me == 0), r1, own)
        r2 = lax.ppermute(jnp.stack([a, b]), "gx", [(0, 1), (1, 0), (2, 3), (3, 2)])
        b1 = jnp.where(me == 1, own, jnp.where(me == 2, r1, r2[0]))
        b2 = jnp.where(me == 0, r1, jnp.where(me == 1, r2[0], jnp.where(me == 2, own, r2[1])))
        b3 = jnp.where(me == 0, r2[1], jnp.where(me == 1, r1, jnp.where(me == 2, r2[0], own)))
        return jnp.concatenate([b1, b2, b3], axis=2)
    owners = list(range(first, n))
    held = [own]
    for s in range(1, n):
        held.append(lax.ppermute(own, "gx", [(k, (k + s) % n) for k in owners]))
    held = jnp.stack(held)
    pieces = [lax.dynamic_index_in_dim(held, (me - k) % n, 0, keepdims=False) for k in owners]
    return jnp.concatenate(pieces, axis=2)


def on_device(
    earlier_window_curl_state,
    material_resistivity_inverse,
    winding_current_pattern,
    winding_axial_centre,
    specimen_presence_flags,
    specimen_kelvin_values,
):
    depth, height, breadth = material_resistivity_inverse.shape
    n_gz, n_gy, n_gx = lax.axis_size("gz"), lax.axis_size("gy"), lax.axis_size("gx")
    z_total, y_total, x_total = depth * n_gz, height * n_gy, breadth * n_gx
    gz_i, gy_i, gx_i = lax.axis_index("gz"), lax.axis_index("gy"), lax.axis_index("gx")
    z_start, y_start, x_start = gz_i * depth, gy_i * height, gx_i * breadth
    rows = height + 2 * H
    lanes = -(-(breadth + 2 * H) // 128) * 128
    gap = lanes - breadth - 2 * H
    specimen_columns = specimen_kelvin_values.shape[2]
    offset = x_total - specimen_columns
    assert offset % breadth == 0 and depth % MB == 0 and height % MB == 0 and breadth % MB == 0
    first_owner = offset // breadth

    coil_width = z_total // 4
    axial = (
        (z_start + jnp.arange(depth)).astype(jnp.float32)
        - winding_axial_centre[0].astype(jnp.float32)
    ) / coil_width
    profile = 1.0 / (1.0 + axial * axial)

    stack = jnp.concatenate(
        [earlier_window_curl_state.reshape(2 * depth, height, breadth), material_resistivity_inverse,
         winding_current_pattern], axis=0)
    up_x, down_x = _line_pairs(n_gx)
    from_left = lax.ppermute(jnp.swapaxes(stack[:, :, breadth - H:], 1, 2), "gx", up_x)
    from_right = lax.ppermute(jnp.swapaxes(stack[:, :, :H], 1, 2), "gx", down_x)
    nch = stack.shape[0]
    xext = jnp.concatenate(
        [stack, jnp.swapaxes(from_right, 1, 2), jnp.zeros((nch, height, gap), jnp.float32),
         jnp.swapaxes(from_left, 1, 2)], axis=2)

    j_start = x_start - offset
    kpad = jnp.pad(specimen_kelvin_values, ((0, 0), (0, 0), (H, H)))
    t_body = lax.dynamic_slice_in_dim(kpad, j_start + H, breadth + H, 2)
    t_tail = lax.dynamic_slice_in_dim(kpad, j_start, H, 2)
    t_x = jnp.concatenate([t_body, jnp.zeros((depth, height, gap), jnp.float32), t_tail], axis=2)

    ystack = jnp.concatenate([xext, t_x], axis=0)
    up_y, down_y = _line_pairs(n_gy)
    from_above = lax.ppermute(ystack[:, height - H:, :], "gy", up_y)
    from_below = lax.ppermute(ystack[:, :H, :], "gy", down_y)
    frame = jnp.concatenate([ystack, from_below, from_above], axis=1)
    field = frame[: 2 * depth]
    material = frame[2 * depth: 3 * depth]
    winding = frame[3 * depth: 3 * depth + 2]
    kelvin = frame[3 * depth + 2:]

    fb = specimen_presence_flags.shape
    flags = jnp.pad(specimen_presence_flags.astype(jnp.float32),
                    ((0, 0), (0, 128 - fb[1]), (0, 128 - fb[2])))
    pos = jnp.stack([z_start // MB, y_start // MB, x_start // MB]).astype(jnp.int32)

    up_z, down_z = _line_pairs(n_gz)
    fshape = jax.ShapeDtypeStruct((2 * depth, rows, lanes), jnp.float32)
    plane2 = jax.ShapeDtypeStruct((2, rows, lanes), jnp.float32)
    qshape = jax.ShapeDtypeStruct((depth, rows, lanes), jnp.float32)
    oshape = jax.ShapeDtypeStruct((2, depth, height, breadth), jnp.float32)
    lo_plane = field[jnp.array([0, depth])]
    hi_plane = field[jnp.array([depth - 1, 2 * depth - 1])]
    for i, factor in enumerate(WEIGHTS):
        last = i == len(WEIGHTS) - 1
        zlo = lax.ppermute(hi_plane, "gz", up_z)
        zhi = lax.ppermute(lo_plane, "gz", down_z)
        outs = (qshape, oshape) if last else (fshape, plane2, plane2)
        res = _vmem_call(
            lambda *r, factor=factor, last=last: _em_kernel(
                factor, last, depth, (height, breadth, y_total, x_total), *r), outs, 8, 2
        )(pos, profile, flags, field, material, winding, zlo, zhi)
        if last:
            heat, field_out = res
        else:
            field, lo_plane, hi_plane = res

    tshape = jax.ShapeDtypeStruct((depth, rows, lanes), jnp.float32)
    tplane = jax.ShapeDtypeStruct((rows, lanes), jnp.float32)
    town = jax.ShapeDtypeStruct((depth, height, breadth), jnp.float32)
    lo_t, hi_t = kelvin[0], kelvin[depth - 1]
    for number in range(STEPS):
        last = number == STEPS - 1
        tzlo = lax.ppermute(hi_t, "gz", up_z)
        tzhi = lax.ppermute(lo_t, "gz", down_z)
        outs = (town,) if last else (tshape, tplane, tplane)
        res = _vmem_call(
            lambda *r, last=last: _heat_kernel(
                last, depth, (height, breadth, offset // MB), *r), outs, 6, 1
        )(pos, flags, kelvin, heat, tzlo, tzhi)
        if last:
            (own_t,) = res
        else:
            kelvin, lo_t, hi_t = res

    segment_kelvin = _broadcast_blocks(own_t, gx_i, n_gx, first_owner)
    return (field_out, segment_kelvin)


def solution(mesh):
    placed = (
        P(None, "gz", "gy", "gx"),
        P("gz", "gy", "gx"),
        P(None, "gy", "gx"),
        P(),
        P(),
        P("gz", "gy", None),
    )
    return jax.shard_map(
        on_device,
        mesh=mesh,
        in_specs=placed,
        out_specs=(P(None, "gz", "gy", "gx"), P("gz", "gy", None)),
        check_vma=False,
    )
```

```python
import jax
import jax.numpy as jnp
from jax import lax
from jax.experimental import pallas as pl
from jax.experimental.pallas import tpu as pltpu
from jax.sharding import PartitionSpec as P

MB = 8
STEPS = 4


WEIGHTS = (0.8, 1.0, 1.25)
SHIFT = 0.2
HEATING = 0.02
CONDUCT = 0.16
SOFTEN = 0.25

H = MB


def _rolls(a):
    rows, lanes = a.shape
    return (
        pltpu.roll(a, rows - 1, 0), pltpu.roll(a, 1, 0),
        pltpu.roll(a, lanes - 1, 1), pltpu.roll(a, 1, 1),
    )


def _selectors(pos, rows, lanes, height, breadth, x_first_block):
    shift = MB.bit_length() - 1
    r = lax.shift_right_logical(lax.broadcasted_iota(jnp.int32, (rows, 128), 0), shift)
    b = lax.broadcasted_iota(jnp.int32, (rows, 128), 1)
    ty = pos[1] + jnp.where(r < (height + H) // MB, r, r - rows // MB)
    sy = (b == ty).astype(jnp.float32)
    l = lax.shift_right_logical(lax.broadcasted_iota(jnp.int32, (lanes, 128), 0), shift)
    bx = lax.broadcasted_iota(jnp.int32, (lanes, 128), 1)
    far = jnp.where(l >= (lanes - H) // MB, l - lanes // MB, -(10 ** 6))
    tx = pos[2] + jnp.where(l < (breadth + H) // MB, l, far)
    sx = ((bx == tx) & (bx >= x_first_block)).astype(jnp.float32)
    return sy, sx


def _cells(fl, zb, sy, sx):
    a = jnp.dot(sy, fl[zb], preferred_element_type=jnp.float32)
    return lax.dot_general(a, sx, (((1,), (1,)), ((), ())), preferred_element_type=jnp.float32)


def _inside(pos, rows, lanes, height, breadth, y_total, x_total):
    r = lax.broadcasted_iota(jnp.int32, (rows, lanes), 0)
    l = lax.broadcasted_iota(jnp.int32, (rows, lanes), 1)
    y = pos[1] * MB + jnp.where(r < height + H, r, r - rows)
    far = jnp.where(l >= lanes - H, l - lanes, -(10 ** 6))
    x = pos[2] * MB + jnp.where(l < breadth + H, l, far)
    return (y >= 0) & (y < y_total) & (x >= 0) & (x < x_total)


def _em_planes(factor, zs, depth, totals, pos, prof, fl, get_f, mat_at, w, put):
    diagonal = 6.0 + SHIFT
    height, breadth, y_total, x_total = totals
    rows, lanes = w.shape[1], w.shape[2]
    keep = _inside(pos, rows, lanes, height, breadth, y_total, x_total)
    sy, sx = _selectors(pos, rows, lanes, height, breadth, 0)
    masks = {}
    for z in zs:
        if z // MB not in masks:
            masks[z // MB] = _cells(fl, pos[0] + z // MB, sy, sx)
        cur = [get_f(c, z) for c in range(2)]
        beside = []
        for c in range(2):
            y_up, y_dn, x_up, x_dn = _rolls(cur[c])
            total = get_f(c, z + 1) + get_f(c, z - 1)
            total = total + y_up + y_dn
            beside.append(total + x_up + x_dn)
        k = masks[z // MB] * mat_at(z)
        s0 = prof[z] * w[0]
        s1 = prof[z] * w[1]
        real_res = s0 - (diagonal * cur[0] - k * cur[1] - beside[0])
        imag_res = s1 - (diagonal * cur[1] + k * cur[0] - beside[1])
        scaled = factor / (diagonal * diagonal + k * k)
        n0 = jnp.where(keep, cur[0] + scaled * (diagonal * real_res + k * imag_res), 0.0)
        n1 = jnp.where(keep, cur[1] + scaled * (diagonal * imag_res - k * real_res), 0.0)
        put(z, n0, n1, HEATING * k * (n0 * n0 + n1 * n1))


def _em_inner(factor, last, depth, totals, pos, prof, fl, f, p0, p7, mat, w, *outs):
    height, breadth = totals[0], totals[1]

    def get_f(c, z):
        if z == 0:
            return p0[c]
        if z == depth - 1:
            return p7[c]
        return f[c * depth + z]

    def put(z, n0, n1, q):
        if last:
            outs[0][z] = q
            outs[1][0, z] = n0[0:height, 0:breadth]
            outs[1][1, z] = n1[0:height, 0:breadth]
        else:
            outs[0][z] = n0
            outs[0][depth + z] = n1

    if not last:
        zero = jnp.zeros(w.shape[1:], jnp.float32)
        for c in range(2):
            outs[0][c * depth] = zero
            outs[0][c * depth + depth - 1] = zero
    _em_planes(factor, range(1, depth - 1), depth, totals, pos, prof, fl, get_f,
               lambda z: mat[z], w, put)


def _em_outer(factor, last, depth, totals, pos, prof, fl, f1, f9, f6, f14, p0, p7, m0, m7, w,
              zlo, zhi, *outs):
    height, breadth = totals[0], totals[1]
    near = {(0, 1): f1, (1, 1): f9, (0, depth - 2): f6, (1, depth - 2): f14}

    def get_f(c, z):
        if z == -1:
            return zlo[c]
        if z == depth:
            return zhi[c]
        if z == 0:
            return p0[c]
        if z == depth - 1:
            return p7[c]
        return near[(c, z)][0]

    def put(z, n0, n1, q):
        j = 0 if z == 0 else 1
        if last:
            outs[0][j] = q
            outs[1][0, j] = n0[0:height, 0:breadth]
            outs[1][1, j] = n1[0:height, 0:breadth]
        else:
            outs[j][0] = n0
            outs[j][1] = n1

    _em_planes(factor, (0, depth - 1), depth, totals, pos, prof, fl, get_f,
               lambda z: (m0 if z == 0 else m7)[0], w, put)


def _heat_planes(zs, depth, totals, pos, fl, get_t, heat_at, put):
    height, breadth, x_first_block = totals
    rows, lanes = get_t(zs[0]).shape
    sy, sx = _selectors(pos, rows, lanes, height, breadth, x_first_block)
    zb_total = fl.shape[0]
    cache = {}

    def mask(z):
        blk = -1 if z < 0 else z // MB
        if blk not in cache:
            zb = pos[0] + blk
            ok = jnp.where((zb >= 0) & (zb < zb_total), 1.0, 0.0)
            cache[blk] = _cells(fl, jnp.clip(zb, 0, zb_total - 1), sy, sx) * ok
        return cache[blk]

    kap_cache = {}

    def kap(z):
        if z not in kap_cache:
            v = get_t(z)
            kap_cache[z] = 1.0 / (1.0 + SOFTEN * v * v)
        return kap_cache[z]

    for z in zs:
        c = get_t(z)
        centre_kappa = kap(z)
        y_up, y_dn, x_up, x_dn = _rolls(c)
        ky_up, ky_dn, kx_up, kx_dn = _rolls(centre_kappa)
        mc = mask(z)
        my_up, my_dn, mx_up, mx_dn = _rolls(mc)
        flux = jnp.zeros_like(c)
        for other, kappa, other_mask in (
            (get_t(z + 1), kap(z + 1), mask(z + 1)), (get_t(z - 1), kap(z - 1), mask(z - 1)),
            (y_up, ky_up, my_up), (y_dn, ky_dn, my_dn), (x_up, kx_up, mx_up), (x_dn, kx_dn, mx_dn),
        ):
            flux = flux + other_mask * (centre_kappa + kappa) * (other - c)
        put(z, c + 0.5 * CONDUCT * mc * flux + heat_at(z))


def _heat_inner(last, depth, totals, pos, fl, t, t0, t7, q, *outs):
    height, breadth = totals[0], totals[1]

    def get_t(z):
        if z == 0:
            return t0[...]
        if z == depth - 1:
            return t7[...]
        return t[z]

    def put(z, new):
        if last:
            outs[0][z] = new[0:height, 0:breadth]
        else:
            outs[0][z] = new

    if not last:
        zero = jnp.zeros(t0.shape, jnp.float32)
        outs[0][0] = zero
        outs[0][depth - 1] = zero
    _heat_planes(list(range(1, depth - 1)), depth, totals, pos, fl, get_t, lambda z: q[z], put)


def _heat_outer(last, depth, totals, pos, fl, t1, t6, t0, t7, qb, tzlo, tzhi, *outs):
    height, breadth = totals[0], totals[1]

    def get_t(z):
        return {-1: tzlo, 0: t0, 1: t1, depth - 2: t6, depth - 1: t7, depth: tzhi}[z][...].reshape(
            t0.shape)

    def put(z, new):
        j = 0 if z == 0 else 1
        if last:
            outs[0][j] = new[0:height, 0:breadth]
        else:
            outs[j][...] = new

    _heat_planes([0, depth - 1], depth, totals, pos, fl, get_t,
                 lambda z: qb[0 if z == 0 else 1], put)


def _plane(idx, rows, lanes):
    return pl.BlockSpec((1, rows, lanes), lambda i: (idx, 0, 0))


def _call(kernel, out_shape, specs, flops, nbytes):
    smem = pl.BlockSpec(memory_space=pltpu.SMEM)
    vmem = pl.BlockSpec(memory_space=pltpu.VMEM)
    return pl.pallas_call(
        kernel,
        out_shape=out_shape,
        grid=(1,),
        in_specs=[smem if x == "s" else vmem if x == "v" else x for x in specs],
        out_specs=[vmem] * len(out_shape),
        cost_estimate=pl.CostEstimate(flops=flops, transcendentals=0, bytes_accessed=nbytes),
    )


def _line_pairs(n, first=0):
    up = [(i, i + 1) for i in range(first, n - 1)]
    down = [(j, i) for i, j in up]
    return up, down


def _broadcast_blocks(own, me, n, first):
    if (n, first) == (4, 1):
        r1 = lax.ppermute(own, "gx", [(2, 0), (3, 1), (1, 2)])
        a = jnp.where((me == 0) | (me == 2), r1, own)
        b = jnp.where((me == 1) | (me == 0), r1, own)
        r2 = lax.ppermute(jnp.stack([a, b]), "gx", [(0, 1), (1, 0), (2, 3), (3, 2)])
        b1 = jnp.where(me == 1, own, jnp.where(me == 2, r1, r2[0]))
        b2 = jnp.where(me == 0, r1, jnp.where(me == 1, r2[0], jnp.where(me == 2, own, r2[1])))
        b3 = jnp.where(me == 0, r2[1], jnp.where(me == 1, r1, jnp.where(me == 2, r2[0], own)))
        return jnp.concatenate([b1, b2, b3], axis=2)
    owners = list(range(first, n))
    held = [own]
    for s in range(1, n):
        held.append(lax.ppermute(own, "gx", [(k, (k + s) % n) for k in owners]))
    held = jnp.stack(held)
    pieces = [lax.dynamic_index_in_dim(held, (me - k) % n, 0, keepdims=False) for k in owners]
    return jnp.concatenate(pieces, axis=2)


def on_device(
    earlier_window_curl_state,
    material_resistivity_inverse,
    winding_current_pattern,
    winding_axial_centre,
    specimen_presence_flags,
    specimen_kelvin_values,
):
    depth, height, breadth = material_resistivity_inverse.shape
    n_gz, n_gy, n_gx = lax.axis_size("gz"), lax.axis_size("gy"), lax.axis_size("gx")
    z_total, y_total, x_total = depth * n_gz, height * n_gy, breadth * n_gx
    gz_i, gy_i, gx_i = lax.axis_index("gz"), lax.axis_index("gy"), lax.axis_index("gx")
    z_start, y_start, x_start = gz_i * depth, gy_i * height, gx_i * breadth
    rows = height + 2 * H
    lanes = -(-(breadth + 2 * H) // 128) * 128
    gap = lanes - breadth - 2 * H
    specimen_columns = specimen_kelvin_values.shape[2]
    offset = x_total - specimen_columns
    assert offset % breadth == 0 and depth % MB == 0 and height % MB == 0 and breadth % MB == 0
    first_owner = offset // breadth

    coil_width = z_total // 4
    axial = (
        (z_start + jnp.arange(depth)).astype(jnp.float32)
        - winding_axial_centre[0].astype(jnp.float32)
    ) / coil_width
    profile = 1.0 / (1.0 + axial * axial)

    stack = jnp.concatenate(
        [earlier_window_curl_state.reshape(2 * depth, height, breadth), material_resistivity_inverse,
         winding_current_pattern], axis=0)
    up_x, down_x = _line_pairs(n_gx)
    from_left = lax.ppermute(jnp.swapaxes(stack[:, :, breadth - H:], 1, 2), "gx", up_x)
    from_right = lax.ppermute(jnp.swapaxes(stack[:, :, :H], 1, 2), "gx", down_x)
    nch = stack.shape[0]
    xext = jnp.concatenate(
        [stack, jnp.swapaxes(from_right, 1, 2), jnp.zeros((nch, height, gap), jnp.float32),
         jnp.swapaxes(from_left, 1, 2)], axis=2)

    j_start = x_start - offset
    kpad = jnp.pad(specimen_kelvin_values, ((0, 0), (0, 0), (H, H)))
    t_body = lax.dynamic_slice_in_dim(kpad, j_start + H, breadth + H, 2)
    t_tail = lax.dynamic_slice_in_dim(kpad, j_start, H, 2)
    t_x = jnp.concatenate([t_body, jnp.zeros((depth, height, gap), jnp.float32), t_tail], axis=2)

    ystack = jnp.concatenate([xext, t_x], axis=0)
    up_y, down_y = _line_pairs(n_gy)
    from_above = lax.ppermute(ystack[:, height - H:, :], "gy", up_y)
    from_below = lax.ppermute(ystack[:, :H, :], "gy", down_y)
    frame = jnp.concatenate([ystack, from_below, from_above], axis=1)
    field = frame[: 2 * depth]
    material = frame[2 * depth: 3 * depth]
    winding = frame[3 * depth: 3 * depth + 2]
    kelvin = frame[3 * depth + 2:]

    fb = specimen_presence_flags.shape
    flags = jnp.pad(specimen_presence_flags.astype(jnp.float32),
                    ((0, 0), (0, 128 - fb[1]), (0, 128 - fb[2])))
    pos = jnp.stack([z_start // MB, y_start // MB, x_start // MB]).astype(jnp.int32)

    assert depth >= 3
    up_z, down_z = _line_pairs(n_gz)
    f32 = jnp.float32
    fshape = jax.ShapeDtypeStruct((2 * depth, rows, lanes), f32)
    plane2 = jax.ShapeDtypeStruct((2, rows, lanes), f32)
    qshape = jax.ShapeDtypeStruct((depth, rows, lanes), f32)
    oshape = jax.ShapeDtypeStruct((2, depth, height, breadth), f32)
    obshape = jax.ShapeDtypeStruct((2, 2, height, breadth), f32)
    em_totals = (height, breadth, y_total, x_total)
    cells = rows * lanes
    near = [_plane(i, rows, lanes) for i in (1, depth + 1, depth - 2, 2 * depth - 2)]
    mat_planes = [_plane(0, rows, lanes), _plane(depth - 1, rows, lanes)]
    p0 = field[jnp.array([0, depth])]
    p7 = field[jnp.array([depth - 1, 2 * depth - 1])]
    for i, factor in enumerate(WEIGHTS):
        last = i == len(WEIGHTS) - 1
        zlo = lax.ppermute(p7, "gz", up_z)
        zhi = lax.ppermute(p0, "gz", down_z)
        outs = (qshape, oshape) if last else (fshape,)
        inner = _call(
            lambda *r, factor=factor, last=last: _em_inner(factor, last, depth, em_totals, *r),
            outs, ["s", "s", "v", "v", "v", "v", "v", "v"],
            60 * 2 * (depth - 2) * cells, 4 * (5 * depth + 6) * cells,
        )(pos, profile, flags, field, p0, p7, material, winding)
        outs = (plane2, obshape) if last else (plane2, plane2)
        outer = _call(
            lambda *r, factor=factor, last=last: _em_outer(factor, last, depth, em_totals, *r),
            outs, ["s", "s", "v"] + near + ["v", "v"] + mat_planes + ["v", "v", "v"],
            60 * 2 * 2 * cells, 4 * 20 * cells,
        )(pos, profile, flags, field, field, field, field, p0, p7, material, material, winding,
          zlo, zhi)
        if last:
            heat, field_out = inner
            heat_b, own_b = outer
        else:
            (field,) = inner
            p0, p7 = outer
    field_out = field_out.at[:, 0].set(own_b[:, 0]).at[:, depth - 1].set(own_b[:, 1])

    tshape = jax.ShapeDtypeStruct((depth, rows, lanes), f32)
    tplane = jax.ShapeDtypeStruct((rows, lanes), f32)
    town = jax.ShapeDtypeStruct((depth, height, breadth), f32)
    tbshape = jax.ShapeDtypeStruct((2, height, breadth), f32)
    t_totals = (height, breadth, offset // MB)
    t_near = [_plane(1, rows, lanes), _plane(depth - 2, rows, lanes)]
    t0, t7 = kelvin[0], kelvin[depth - 1]
    for number in range(STEPS):
        last = number == STEPS - 1
        tzlo = lax.ppermute(t7, "gz", up_z)
        tzhi = lax.ppermute(t0, "gz", down_z)
        inner = _call(
            lambda *r, last=last: _heat_inner(last, depth, t_totals, *r),
            (town,) if last else (tshape,), ["s", "v", "v", "v", "v", "v"],
            80 * (depth - 2) * cells, 4 * (3 * depth + 2) * cells,
        )(pos, flags, kelvin, t0, t7, heat)
        outer = _call(
            lambda *r, last=last: _heat_outer(last, depth, t_totals, *r),
            (tbshape,) if last else (tplane, tplane), ["s", "v"] + t_near + ["v"] * 5,
            80 * 2 * cells, 4 * 12 * cells,
        )(pos, flags, kelvin, kelvin, t0, t7, heat_b, tzlo, tzhi)
        if last:
            (own_t,) = inner
            (own_tb,) = outer
        else:
            (kelvin,) = inner
            t0, t7 = outer
    own_t = own_t.at[0].set(own_tb[0]).at[depth - 1].set(own_tb[1])

    segment_kelvin = _broadcast_blocks(own_t, gx_i, n_gx, first_owner)
    return (field_out, segment_kelvin)


def solution(mesh):
    placed = (
        P(None, "gz", "gy", "gx"),
        P("gz", "gy", "gx"),
        P(None, "gy", "gx"),
        P(),
        P(),
        P("gz", "gy", None),
    )
    return jax.shard_map(
        on_device,
        mesh=mesh,
        in_specs=placed,
        out_specs=(P(None, "gz", "gy", "gx"), P("gz", "gy", None)),
        check_vma=False,
    )
```

```python
import jax
import jax.numpy as jnp
from jax import lax
from jax.experimental import pallas as pl
from jax.experimental.pallas import tpu as pltpu
from jax.sharding import PartitionSpec as P

MB = 8
STEPS = 4


WEIGHTS = (0.8, 1.0, 1.25)
SHIFT = 0.2
HEATING = 0.02
CONDUCT = 0.16
SOFTEN = 0.25

H = MB


def _rolls(a):
    rows, lanes = a.shape
    return (
        pltpu.roll(a, rows - 1, 0), pltpu.roll(a, 1, 0),
        pltpu.roll(a, lanes - 1, 1), pltpu.roll(a, 1, 1),
    )


def _selectors(pos, rows, lanes, height, breadth, x_first_block):
    shift = MB.bit_length() - 1
    r = lax.shift_right_logical(lax.broadcasted_iota(jnp.int32, (rows, 128), 0), shift)
    b = lax.broadcasted_iota(jnp.int32, (rows, 128), 1)
    ty = pos[1] + jnp.where(r < (height + H) // MB, r, r - rows // MB)
    sy = (b == ty).astype(jnp.float32)
    l = lax.shift_right_logical(lax.broadcasted_iota(jnp.int32, (lanes, 128), 0), shift)
    bx = lax.broadcasted_iota(jnp.int32, (lanes, 128), 1)
    far = jnp.where(l >= (lanes - H) // MB, l - lanes // MB, -(10 ** 6))
    tx = pos[2] + jnp.where(l < (breadth + H) // MB, l, far)
    sx = ((bx == tx) & (bx >= x_first_block)).astype(jnp.float32)
    return sy, sx


def _cells(fl, zb, sy, sx):
    a = jnp.dot(sy, fl[zb], preferred_element_type=jnp.float32)
    return lax.dot_general(a, sx, (((1,), (1,)), ((), ())), preferred_element_type=jnp.float32)


def _inside(pos, rows, lanes, height, breadth, y_total, x_total):
    r = lax.broadcasted_iota(jnp.int32, (rows, lanes), 0)
    l = lax.broadcasted_iota(jnp.int32, (rows, lanes), 1)
    y = pos[1] * MB + jnp.where(r < height + H, r, r - rows)
    far = jnp.where(l >= lanes - H, l - lanes, -(10 ** 6))
    x = pos[2] * MB + jnp.where(l < breadth + H, l, far)
    return (y >= 0) & (y < y_total) & (x >= 0) & (x < x_total)


def _em_kernel(factor, last, depth, totals, pos, prof, fl, fa0, f0, fb0, fa1, f1, fb1, mat,
               w0, w1, zlo, zhi, *rest):
    diagonal = 6.0 + SHIFT
    if last:
        (heat, own, mask_s, keep_s) = rest
    else:
        (o0, o1, oz0, oz1, mask_s, keep_s) = rest
    height, breadth, y_total, x_total = totals
    rows, lanes = keep_s.shape
    z = pl.program_id(0)

    @pl.when(z == 0)
    def _():
        keep_s[...] = _inside(pos, rows, lanes, height, breadth, y_total, x_total).astype(
            jnp.float32)
        sy, sx = _selectors(pos, rows, lanes, height, breadth, 0)
        for zo in range(depth // MB):
            mask_s[zo] = _cells(fl, pos[0] + zo, sy, sx)

    planes = ((fa0, f0, fb0), (fa1, f1, fb1))
    cur = [planes[c][1][0] for c in range(2)]
    beside = []
    for c in range(2):
        z_up = jnp.where(z == depth - 1, zhi[c], planes[c][2][0])
        z_dn = jnp.where(z == 0, zlo[c], planes[c][0][0])
        y_up, y_dn, x_up, x_dn = _rolls(cur[c])
        total = z_up + z_dn
        total = total + y_up + y_dn
        beside.append(total + x_up + x_dn)
    k = mask_s[lax.shift_right_logical(z, MB.bit_length() - 1)] * mat[0]
    s0 = prof[z] * w0[0]
    s1 = prof[z] * w1[0]
    real_res = s0 - (diagonal * cur[0] - k * cur[1] - beside[0])
    imag_res = s1 - (diagonal * cur[1] + k * cur[0] - beside[1])
    scaled = factor / (diagonal * diagonal + k * k)
    keep = keep_s[...] > 0.0
    n0 = jnp.where(keep, cur[0] + scaled * (diagonal * real_res + k * imag_res), 0.0)
    n1 = jnp.where(keep, cur[1] + scaled * (diagonal * imag_res - k * real_res), 0.0)
    if last:
        heat[0] = HEATING * k * (n0 * n0 + n1 * n1)
        own[0, 0] = n0[0:height, 0:breadth]
        own[1, 0] = n1[0:height, 0:breadth]
    else:
        o0[0] = n0
        o1[0] = n1

        @pl.when(z == 0)
        def _():
            oz0[0] = n0
            oz0[1] = n1

        @pl.when(z == depth - 1)
        def _():
            oz1[0] = n0
            oz1[1] = n1


def _heat_kernel(last, depth, totals, pos, fl, ta, t, tb, q, tzlo, tzhi, *rest):
    if last:
        (own, mask_s) = rest
    else:
        (o, oz0, oz1, mask_s) = rest
    height, breadth, x_first_block = totals
    rows, lanes = tzlo.shape
    z = pl.program_id(0)
    shift = MB.bit_length() - 1

    @pl.when(z == 0)
    def _():
        sy, sx = _selectors(pos, rows, lanes, height, breadth, x_first_block)
        zb_total = fl.shape[0]
        for j in range(depth // MB + 2):
            zb = pos[0] + j - 1
            ok = jnp.where((zb >= 0) & (zb < zb_total), 1.0, 0.0)
            mask_s[j] = _cells(fl, jnp.clip(zb, 0, zb_total - 1), sy, sx) * ok

    c = t[0]
    up = jnp.where(z == depth - 1, tzhi[...], tb[0])
    dn = jnp.where(z == 0, tzlo[...], ta[0])
    centre_kappa = 1.0 / (1.0 + SOFTEN * c * c)
    y_up, y_dn, x_up, x_dn = _rolls(c)
    ky_up, ky_dn, kx_up, kx_dn = _rolls(centre_kappa)
    mc = mask_s[lax.shift_right_logical(z + MB, shift)]
    my_up, my_dn, mx_up, mx_dn = _rolls(mc)
    flux = jnp.zeros_like(c)
    for other, kappa, other_mask in (
        (up, 1.0 / (1.0 + SOFTEN * up * up), mask_s[lax.shift_right_logical(z + 1 + MB, shift)]),
        (dn, 1.0 / (1.0 + SOFTEN * dn * dn), mask_s[lax.shift_right_logical(z - 1 + MB, shift)]),
        (y_up, ky_up, my_up), (y_dn, ky_dn, my_dn), (x_up, kx_up, mx_up), (x_dn, kx_dn, mx_dn),
    ):
        flux = flux + other_mask * (centre_kappa + kappa) * (other - c)
    new = c + 0.5 * CONDUCT * mc * flux + q[0]
    if last:
        own[0] = new[0:height, 0:breadth]
    else:
        o[0] = new

        @pl.when(z == 0)
        def _():
            oz0[...] = new

        @pl.when(z == depth - 1)
        def _():
            oz1[...] = new


def _plane_specs(base, depth, rows, lanes):
    def at(d):
        return pl.BlockSpec(
            (1, rows, lanes), lambda z: (base + jnp.clip(z + d, 0, depth - 1), 0, 0))
    return [at(-1), at(0), at(1)]


def _fixed(shape, idx=None):
    n = len(shape)
    if idx is None:
        return pl.BlockSpec(shape, lambda z: (0,) * n)
    return pl.BlockSpec(shape, lambda z: (idx,) + (0,) * (n - 1))


def _line_pairs(n, first=0):
    up = [(i, i + 1) for i in range(first, n - 1)]
    down = [(j, i) for i, j in up]
    return up, down


def _broadcast_blocks(own, me, n, first):
    if (n, first) == (4, 1):
        r1 = lax.ppermute(own, "gx", [(2, 0), (3, 1), (1, 2)])
        a = jnp.where((me == 0) | (me == 2), r1, own)
        b = jnp.where((me == 1) | (me == 0), r1, own)
        r2 = lax.ppermute(jnp.stack([a, b]), "gx", [(0, 1), (1, 0), (2, 3), (3, 2)])
        b1 = jnp.where(me == 1, own, jnp.where(me == 2, r1, r2[0]))
        b2 = jnp.where(me == 0, r1, jnp.where(me == 1, r2[0], jnp.where(me == 2, own, r2[1])))
        b3 = jnp.where(me == 0, r2[1], jnp.where(me == 1, r1, jnp.where(me == 2, r2[0], own)))
        return jnp.concatenate([b1, b2, b3], axis=2)
    owners = list(range(first, n))
    held = [own]
    for s in range(1, n):
        held.append(lax.ppermute(own, "gx", [(k, (k + s) % n) for k in owners]))
    held = jnp.stack(held)
    pieces = [lax.dynamic_index_in_dim(held, (me - k) % n, 0, keepdims=False) for k in owners]
    return jnp.concatenate(pieces, axis=2)


def on_device(
    earlier_window_curl_state,
    material_resistivity_inverse,
    winding_current_pattern,
    winding_axial_centre,
    specimen_presence_flags,
    specimen_kelvin_values,
):
    depth, height, breadth = material_resistivity_inverse.shape
    n_gz, n_gy, n_gx = lax.axis_size("gz"), lax.axis_size("gy"), lax.axis_size("gx")
    z_total, y_total, x_total = depth * n_gz, height * n_gy, breadth * n_gx
    gz_i, gy_i, gx_i = lax.axis_index("gz"), lax.axis_index("gy"), lax.axis_index("gx")
    z_start, y_start, x_start = gz_i * depth, gy_i * height, gx_i * breadth
    rows = height + 2 * H
    lanes = -(-(breadth + 2 * H) // 128) * 128
    gap = lanes - breadth - 2 * H
    specimen_columns = specimen_kelvin_values.shape[2]
    offset = x_total - specimen_columns
    assert offset % breadth == 0 and depth % MB == 0 and height % MB == 0 and breadth % MB == 0
    first_owner = offset // breadth

    coil_width = z_total // 4
    axial = (
        (z_start + jnp.arange(depth)).astype(jnp.float32)
        - winding_axial_centre[0].astype(jnp.float32)
    ) / coil_width
    profile = 1.0 / (1.0 + axial * axial)

    stack = jnp.concatenate(
        [earlier_window_curl_state.reshape(2 * depth, height, breadth), material_resistivity_inverse,
         winding_current_pattern], axis=0)
    up_x, down_x = _line_pairs(n_gx)
    from_left = lax.ppermute(jnp.swapaxes(stack[:, :, breadth - H:], 1, 2), "gx", up_x)
    from_right = lax.ppermute(jnp.swapaxes(stack[:, :, :H], 1, 2), "gx", down_x)
    nch = stack.shape[0]
    xext = jnp.concatenate(
        [stack, jnp.swapaxes(from_right, 1, 2), jnp.zeros((nch, height, gap), jnp.float32),
         jnp.swapaxes(from_left, 1, 2)], axis=2)

    j_start = x_start - offset
    kpad = jnp.pad(specimen_kelvin_values, ((0, 0), (0, 0), (H, H)))
    t_body = lax.dynamic_slice_in_dim(kpad, j_start + H, breadth + H, 2)
    t_tail = lax.dynamic_slice_in_dim(kpad, j_start, H, 2)
    t_x = jnp.concatenate([t_body, jnp.zeros((depth, height, gap), jnp.float32), t_tail], axis=2)

    ystack = jnp.concatenate([xext, t_x], axis=0)
    up_y, down_y = _line_pairs(n_gy)
    from_above = lax.ppermute(ystack[:, height - H:, :], "gy", up_y)
    from_below = lax.ppermute(ystack[:, :H, :], "gy", down_y)
    frame = jnp.concatenate([ystack, from_below, from_above], axis=1)

    fb = specimen_presence_flags.shape
    flags = jnp.pad(specimen_presence_flags.astype(jnp.float32),
                    ((0, 0), (0, 128 - fb[1]), (0, 128 - fb[2])))
    pos = jnp.stack([z_start // MB, y_start // MB, x_start // MB]).astype(jnp.int32)

    up_z, down_z = _line_pairs(n_gz)
    f32 = jnp.float32
    smem = pl.BlockSpec(memory_space=pltpu.SMEM)
    plane = jax.ShapeDtypeStruct((depth, rows, lanes), f32)
    plane2 = jax.ShapeDtypeStruct((2, rows, lanes), f32)
    oshape = jax.ShapeDtypeStruct((2, depth, height, breadth), f32)
    at_z = pl.BlockSpec((1, rows, lanes), lambda z: (z, 0, 0))
    fl_spec = _fixed(flags.shape)
    em_totals = (height, breadth, y_total, x_total)
    arrays = (frame, frame)
    bases = (0, depth)
    lo_plane = frame[jnp.array([0, depth])]
    hi_plane = frame[jnp.array([depth - 1, 2 * depth - 1])]
    for i, factor in enumerate(WEIGHTS):
        last = i == len(WEIGHTS) - 1
        zlo = lax.ppermute(hi_plane, "gz", up_z)
        zhi = lax.ppermute(lo_plane, "gz", down_z)
        if last:
            outs = (plane, oshape)
            out_specs = [at_z, pl.BlockSpec((2, 1, height, breadth), lambda z: (0, z, 0, 0))]
        else:
            outs = (plane, plane, plane2, plane2)
            out_specs = [at_z, at_z, _fixed((2, rows, lanes)), _fixed((2, rows, lanes))]
        in_specs = ([smem, smem, fl_spec] + _plane_specs(bases[0], depth, rows, lanes)
                    + _plane_specs(bases[1], depth, rows, lanes)
                    + [pl.BlockSpec((1, rows, lanes), lambda z: (2 * depth + z, 0, 0)),
                       _fixed((1, rows, lanes), 3 * depth), _fixed((1, rows, lanes), 3 * depth + 1),
                       _fixed((2, rows, lanes)), _fixed((2, rows, lanes))])
        res = pl.pallas_call(
            lambda *r, factor=factor, last=last: _em_kernel(factor, last, depth, em_totals, *r),
            out_shape=outs,
            grid=(depth,),
            in_specs=in_specs,
            out_specs=out_specs,
            scratch_shapes=[pltpu.VMEM((depth // MB, rows, lanes), f32),
                            pltpu.VMEM((rows, lanes), f32)],
        )(pos, profile, flags, arrays[0], arrays[0], arrays[0], arrays[1], arrays[1], arrays[1],
          frame, frame, frame, zlo, zhi)
        if last:
            heat, field_out = res
        else:
            f0, f1, lo_plane, hi_plane = res
            arrays, bases = (f0, f1), (0, 0)

    tplane = jax.ShapeDtypeStruct((rows, lanes), f32)
    town = jax.ShapeDtypeStruct((depth, height, breadth), f32)
    t_totals = (height, breadth, offset // MB)
    kelvin, t_base = frame, 3 * depth + 2
    lo_t, hi_t = frame[t_base], frame[t_base + depth - 1]
    for number in range(STEPS):
        last = number == STEPS - 1
        tzlo = lax.ppermute(hi_t, "gz", up_z)
        tzhi = lax.ppermute(lo_t, "gz", down_z)
        if last:
            outs = (town,)
            out_specs = [pl.BlockSpec((1, height, breadth), lambda z: (z, 0, 0))]
        else:
            outs = (plane, tplane, tplane)
            out_specs = [at_z, _fixed((rows, lanes)), _fixed((rows, lanes))]
        res = pl.pallas_call(
            lambda *r, last=last: _heat_kernel(last, depth, t_totals, *r),
            out_shape=outs,
            grid=(depth,),
            in_specs=[smem, fl_spec] + _plane_specs(t_base, depth, rows, lanes)
            + [at_z, _fixed((rows, lanes)), _fixed((rows, lanes))],
            out_specs=out_specs,
            scratch_shapes=[pltpu.VMEM((depth // MB + 2, rows, lanes), f32)],
        )(pos, flags, kelvin, kelvin, kelvin, heat, tzlo, tzhi)
        if last:
            (own_t,) = res
        else:
            kelvin, lo_t, hi_t = res
            t_base = 0

    segment_kelvin = _broadcast_blocks(own_t, gx_i, n_gx, first_owner)
    return (field_out, segment_kelvin)


def solution(mesh):
    placed = (
        P(None, "gz", "gy", "gx"),
        P("gz", "gy", "gx"),
        P(None, "gy", "gx"),
        P(),
        P(),
        P("gz", "gy", None),
    )
    return jax.shard_map(
        on_device,
        mesh=mesh,
        in_specs=placed,
        out_specs=(P(None, "gz", "gy", "gx"), P("gz", "gy", None)),
        check_vma=False,
    )
```

```python
import jax
import jax.numpy as jnp
from jax import lax
from jax.experimental import pallas as pl
from jax.experimental.pallas import tpu as pltpu
from jax.sharding import PartitionSpec as P

MB = 8
STEPS = 4


WEIGHTS = (0.8, 1.0, 1.25)
SHIFT = 0.2
HEATING = 0.02
CONDUCT = 0.16
SOFTEN = 0.25

H = MB


def _rolls(a):
    rows, lanes = a.shape
    return (
        pltpu.roll(a, rows - 1, 0), pltpu.roll(a, 1, 0),
        pltpu.roll(a, lanes - 1, 1), pltpu.roll(a, 1, 1),
    )


def _selectors(pos, rows, lanes, height, breadth, x_first_block):
    shift = MB.bit_length() - 1
    r = lax.shift_right_logical(lax.broadcasted_iota(jnp.int32, (rows, 128), 0), shift)
    b = lax.broadcasted_iota(jnp.int32, (rows, 128), 1)
    ty = pos[1] + jnp.where(r < (height + H) // MB, r, r - rows // MB)
    sy = (b == ty).astype(jnp.float32)
    l = lax.shift_right_logical(lax.broadcasted_iota(jnp.int32, (lanes, 128), 0), shift)
    bx = lax.broadcasted_iota(jnp.int32, (lanes, 128), 1)
    far = jnp.where(l >= (lanes - H) // MB, l - lanes // MB, -(10 ** 6))
    tx = pos[2] + jnp.where(l < (breadth + H) // MB, l, far)
    sx = ((bx == tx) & (bx >= x_first_block)).astype(jnp.float32)
    return sy, sx


def _cells(fl, zb, sy, sx):
    a = jnp.dot(sy, fl[zb], preferred_element_type=jnp.float32)
    return lax.dot_general(a, sx, (((1,), (1,)), ((), ())), preferred_element_type=jnp.float32)


def _inside(pos, rows, lanes, height, breadth, y_total, x_total):
    r = lax.broadcasted_iota(jnp.int32, (rows, lanes), 0)
    l = lax.broadcasted_iota(jnp.int32, (rows, lanes), 1)
    y = pos[1] * MB + jnp.where(r < height + H, r, r - rows)
    far = jnp.where(l >= lanes - H, l - lanes, -(10 ** 6))
    x = pos[2] * MB + jnp.where(l < breadth + H, l, far)
    return (y >= 0) & (y < y_total) & (x >= 0) & (x < x_total)


def _em_kernel(factor, last, pair, depth, totals, pos, prof, fl, f, mat, w, zlo, zhi, *outs):
    diagonal = 6.0 + SHIFT
    if last:
        (heat, own) = outs
    elif pair:
        (o, oz0) = outs
        oz1 = None
    else:
        (o, oz0, oz1) = outs
    bottom = pos[0] == 0
    height, breadth, y_total, x_total = totals
    rows, lanes = f.shape[1], f.shape[2]
    keep = _inside(pos, rows, lanes, height, breadth, y_total, x_total)
    sy, sx = _selectors(pos, rows, lanes, height, breadth, 0)
    masks = [_cells(fl, pos[0] + zo, sy, sx) for zo in range(depth // MB)]
    for z in range(depth):
        cur = [f[c * depth + z] for c in range(2)]
        beside = []
        for c in range(2):
            if z + 1 < depth:
                z_up = f[c * depth + z + 1]
            else:
                z_up = jnp.where(bottom, zhi[c], 0.0) if pair else zhi[c]
            if z > 0:
                z_dn = f[c * depth + z - 1]
            else:
                z_dn = jnp.where(bottom, 0.0, zlo[c]) if pair else zlo[c]
            y_up, y_dn, x_up, x_dn = _rolls(cur[c])
            total = z_up + z_dn
            total = total + y_up + y_dn
            beside.append(total + x_up + x_dn)
        k = masks[z // MB] * mat[z]
        s0 = prof[z] * w[0]
        s1 = prof[z] * w[1]
        real_res = s0 - (diagonal * cur[0] - k * cur[1] - beside[0])
        imag_res = s1 - (diagonal * cur[1] + k * cur[0] - beside[1])
        scaled = factor / (diagonal * diagonal + k * k)
        n0 = jnp.where(keep, cur[0] + scaled * (diagonal * real_res + k * imag_res), 0.0)
        n1 = jnp.where(keep, cur[1] + scaled * (diagonal * imag_res - k * real_res), 0.0)
        if last:
            heat[z] = HEATING * k * (n0 * n0 + n1 * n1)
            own[0, z] = n0[0:height, 0:breadth]
            own[1, z] = n1[0:height, 0:breadth]
        else:
            o[z] = n0
            o[depth + z] = n1
            if z == 0:
                oz0[0] = n0
                oz0[1] = n1
            if z == depth - 1 and pair:
                oz0[0] = jnp.where(bottom, n0, oz0[0])
                oz0[1] = jnp.where(bottom, n1, oz0[1])
            elif z == depth - 1:
                oz1[0] = n0
                oz1[1] = n1


def _heat_kernel(last, pair, depth, totals, pos, fl, t, q, tzlo, tzhi, *outs):
    if last:
        (own,) = outs
    elif pair:
        (o, oz0) = outs
        oz1 = None
    else:
        (o, oz0, oz1) = outs
    bottom = pos[0] == 0
    height, breadth, x_first_block = totals
    rows, lanes = t.shape[1], t.shape[2]
    sy, sx = _selectors(pos, rows, lanes, height, breadth, x_first_block)
    zb_total = fl.shape[0]
    below = pos[0] - 1
    above = pos[0] + depth // MB
    m_below = _cells(fl, jnp.maximum(below, 0), sy, sx) * jnp.where(below >= 0, 1.0, 0.0)
    m_above = _cells(fl, jnp.minimum(above, zb_total - 1), sy, sx) * jnp.where(
        above < zb_total, 1.0, 0.0)
    m_own = [_cells(fl, pos[0] + zo, sy, sx) for zo in range(depth // MB)]
    planes = [m_below] + [m_own[z // MB] for z in range(depth)] + [m_above]
    if pair:
        below_t = jnp.where(bottom, 0.0, tzlo[...])
        above_t = jnp.where(bottom, tzhi[...], 0.0)
    else:
        below_t, above_t = tzlo[...], tzhi[...]
    temps = [below_t] + [t[z] for z in range(depth)] + [above_t]
    kaps = [1.0 / (1.0 + SOFTEN * v * v) for v in temps]
    for z in range(depth):
        c = temps[z + 1]
        centre_kappa = kaps[z + 1]
        y_up, y_dn, x_up, x_dn = _rolls(c)
        ky_up, ky_dn, kx_up, kx_dn = _rolls(centre_kappa)
        mc = planes[z + 1]
        my_up, my_dn, mx_up, mx_dn = _rolls(mc)
        flux = jnp.zeros_like(c)
        for other, kappa, other_mask in (
            (temps[z + 2], kaps[z + 2], planes[z + 2]), (temps[z], kaps[z], planes[z]),
            (y_up, ky_up, my_up), (y_dn, ky_dn, my_dn), (x_up, kx_up, mx_up), (x_dn, kx_dn, mx_dn),
        ):
            flux = flux + other_mask * (centre_kappa + kappa) * (other - c)
        new = c + 0.5 * CONDUCT * mc * flux + q[z]
        if last:
            own[z] = new[0:height, 0:breadth]
        else:
            o[z] = new
            if z == 0:
                oz0[...] = new
            if z == depth - 1 and pair:
                oz0[...] = jnp.where(bottom, new, oz0[...])
            elif z == depth - 1:
                oz1[...] = new


def _vmem_call(kernel, out_shape, n_in, n_smem=0):
    specs = [pl.BlockSpec(memory_space=pltpu.SMEM)] * n_smem
    specs += [pl.BlockSpec(memory_space=pltpu.VMEM)] * (n_in - n_smem)
    return pl.pallas_call(
        kernel,
        out_shape=out_shape,
        in_specs=specs,
        out_specs=[pl.BlockSpec(memory_space=pltpu.VMEM)] * len(out_shape),
    )


def _line_pairs(n, first=0):
    up = [(i, i + 1) for i in range(first, n - 1)]
    down = [(j, i) for i, j in up]
    return up, down


def _broadcast_blocks(own, me, n, first):
    if (n, first) == (4, 1):
        r1 = lax.ppermute(own, "gx", [(2, 0), (3, 1), (1, 2)])
        a = jnp.where((me == 0) | (me == 2), r1, own)
        b = jnp.where((me == 1) | (me == 0), r1, own)
        r2 = lax.ppermute(jnp.stack([a, b]), "gx", [(0, 1), (1, 0), (2, 3), (3, 2)])
        b1 = jnp.where(me == 1, own, jnp.where(me == 2, r1, r2[0]))
        b2 = jnp.where(me == 0, r1, jnp.where(me == 1, r2[0], jnp.where(me == 2, own, r2[1])))
        b3 = jnp.where(me == 0, r2[1], jnp.where(me == 1, r1, jnp.where(me == 2, r2[0], own)))
        return jnp.concatenate([b1, b2, b3], axis=2)
    owners = list(range(first, n))
    held = [own]
    for s in range(1, n):
        held.append(lax.ppermute(own, "gx", [(k, (k + s) % n) for k in owners]))
    held = jnp.stack(held)
    pieces = [lax.dynamic_index_in_dim(held, (me - k) % n, 0, keepdims=False) for k in owners]
    return jnp.concatenate(pieces, axis=2)


def on_device(
    earlier_window_curl_state,
    material_resistivity_inverse,
    winding_current_pattern,
    winding_axial_centre,
    specimen_presence_flags,
    specimen_kelvin_values,
):
    depth, height, breadth = material_resistivity_inverse.shape
    n_gz, n_gy, n_gx = lax.axis_size("gz"), lax.axis_size("gy"), lax.axis_size("gx")
    z_total, y_total, x_total = depth * n_gz, height * n_gy, breadth * n_gx
    gz_i, gy_i, gx_i = lax.axis_index("gz"), lax.axis_index("gy"), lax.axis_index("gx")
    z_start, y_start, x_start = gz_i * depth, gy_i * height, gx_i * breadth
    rows = height + 2 * H
    lanes = -(-(breadth + 2 * H) // 128) * 128
    gap = lanes - breadth - 2 * H
    specimen_columns = specimen_kelvin_values.shape[2]
    offset = x_total - specimen_columns
    assert offset % breadth == 0 and depth % MB == 0 and height % MB == 0 and breadth % MB == 0
    first_owner = offset // breadth

    coil_width = z_total // 4
    axial = (
        (z_start + jnp.arange(depth)).astype(jnp.float32)
        - winding_axial_centre[0].astype(jnp.float32)
    ) / coil_width
    profile = 1.0 / (1.0 + axial * axial)

    stack = jnp.concatenate(
        [earlier_window_curl_state.reshape(2 * depth, height, breadth), material_resistivity_inverse,
         winding_current_pattern], axis=0)
    up_x, down_x = _line_pairs(n_gx)
    from_left = lax.ppermute(jnp.swapaxes(stack[:, :, breadth - H:], 1, 2), "gx", up_x)
    from_right = lax.ppermute(jnp.swapaxes(stack[:, :, :H], 1, 2), "gx", down_x)
    nch = stack.shape[0]
    xext = jnp.concatenate(
        [stack, jnp.swapaxes(from_right, 1, 2), jnp.zeros((nch, height, gap), jnp.float32),
         jnp.swapaxes(from_left, 1, 2)], axis=2)

    j_start = x_start - offset
    kpad = jnp.pad(specimen_kelvin_values, ((0, 0), (0, 0), (H, H)))
    t_body = lax.dynamic_slice_in_dim(kpad, j_start + H, breadth + H, 2)
    t_tail = lax.dynamic_slice_in_dim(kpad, j_start, H, 2)
    t_x = jnp.concatenate([t_body, jnp.zeros((depth, height, gap), jnp.float32), t_tail], axis=2)

    ystack = jnp.concatenate([xext, t_x], axis=0)
    up_y, down_y = _line_pairs(n_gy)
    from_above = lax.ppermute(ystack[:, height - H:, :], "gy", up_y)
    from_below = lax.ppermute(ystack[:, :H, :], "gy", down_y)
    frame = jnp.concatenate([ystack, from_below, from_above], axis=1)
    field = frame[: 2 * depth]
    material = frame[2 * depth: 3 * depth]
    winding = frame[3 * depth: 3 * depth + 2]
    kelvin = frame[3 * depth + 2:]

    fb = specimen_presence_flags.shape
    flags = jnp.pad(specimen_presence_flags.astype(jnp.float32),
                    ((0, 0), (0, 128 - fb[1]), (0, 128 - fb[2])))
    pos = jnp.stack([z_start // MB, y_start // MB, x_start // MB]).astype(jnp.int32)

    up_z, down_z = _line_pairs(n_gz)
    fshape = jax.ShapeDtypeStruct((2 * depth, rows, lanes), jnp.float32)
    plane2 = jax.ShapeDtypeStruct((2, rows, lanes), jnp.float32)
    qshape = jax.ShapeDtypeStruct((depth, rows, lanes), jnp.float32)
    oshape = jax.ShapeDtypeStruct((2, depth, height, breadth), jnp.float32)
    lo_plane = field[jnp.array([0, depth])]
    hi_plane = field[jnp.array([depth - 1, 2 * depth - 1])]
    pair = n_gz == 2
    both = [(0, 1), (1, 0)]
    if pair:
        send = jnp.where(gz_i == 0, hi_plane, lo_plane)
    for i, factor in enumerate(WEIGHTS):
        last = i == len(WEIGHTS) - 1
        if pair:
            zlo = zhi = lax.ppermute(send, "gz", both)
        else:
            zlo = lax.ppermute(hi_plane, "gz", up_z)
            zhi = lax.ppermute(lo_plane, "gz", down_z)
        outs = (qshape, oshape) if last else (fshape, plane2) if pair else (fshape, plane2, plane2)
        res = _vmem_call(
            lambda *r, factor=factor, last=last: _em_kernel(
                factor, last, pair, depth, (height, breadth, y_total, x_total), *r), outs, 8, 2
        )(pos, profile, flags, field, material, winding, zlo, zhi)
        if last:
            heat, field_out = res
        elif pair:
            field, send = res
        else:
            field, lo_plane, hi_plane = res

    tshape = jax.ShapeDtypeStruct((depth, rows, lanes), jnp.float32)
    tplane = jax.ShapeDtypeStruct((rows, lanes), jnp.float32)
    town = jax.ShapeDtypeStruct((depth, height, breadth), jnp.float32)
    lo_t, hi_t = kelvin[0], kelvin[depth - 1]
    if pair:
        send_t = jnp.where(gz_i == 0, hi_t, lo_t)
    for number in range(STEPS):
        last = number == STEPS - 1
        if pair:
            tzlo = tzhi = lax.ppermute(send_t, "gz", both)
        else:
            tzlo = lax.ppermute(hi_t, "gz", up_z)
            tzhi = lax.ppermute(lo_t, "gz", down_z)
        outs = (town,) if last else (tshape, tplane) if pair else (tshape, tplane, tplane)
        res = _vmem_call(
            lambda *r, last=last: _heat_kernel(
                last, pair, depth, (height, breadth, offset // MB), *r), outs, 6, 1
        )(pos, flags, kelvin, heat, tzlo, tzhi)
        if last:
            (own_t,) = res
        elif pair:
            kelvin, send_t = res
        else:
            kelvin, lo_t, hi_t = res

    segment_kelvin = _broadcast_blocks(own_t, gx_i, n_gx, first_owner)
    return (field_out, segment_kelvin)


def solution(mesh):
    placed = (
        P(None, "gz", "gy", "gx"),
        P("gz", "gy", "gx"),
        P(None, "gy", "gx"),
        P(),
        P(),
        P("gz", "gy", None),
    )
    return jax.shard_map(
        on_device,
        mesh=mesh,
        in_specs=placed,
        out_specs=(P(None, "gz", "gy", "gx"), P("gz", "gy", None)),
        check_vma=False,
    )
```

```python
import jax
import jax.numpy as jnp
from jax import lax
from jax.experimental import pallas as pl
from jax.experimental.pallas import tpu as pltpu
from jax.sharding import PartitionSpec as P

MB = 8
STEPS = 4


WEIGHTS = (0.8, 1.0, 1.25)
SHIFT = 0.2
HEATING = 0.02
CONDUCT = 0.16
SOFTEN = 0.25

H = MB


def _rolls(a):
    rows, lanes = a.shape
    return (
        pltpu.roll(a, rows - 1, 0), pltpu.roll(a, 1, 0),
        pltpu.roll(a, lanes - 1, 1), pltpu.roll(a, 1, 1),
    )


def _selectors(pos, rows, lanes, height, breadth, x_first_block):
    shift = MB.bit_length() - 1
    r = lax.shift_right_logical(lax.broadcasted_iota(jnp.int32, (rows, 128), 0), shift)
    b = lax.broadcasted_iota(jnp.int32, (rows, 128), 1)
    ty = pos[1] + jnp.where(r < (height + H) // MB, r, r - rows // MB)
    sy = (b == ty).astype(jnp.float32)
    l = lax.shift_right_logical(lax.broadcasted_iota(jnp.int32, (lanes, 128), 0), shift)
    bx = lax.broadcasted_iota(jnp.int32, (lanes, 128), 1)
    far = jnp.where(l >= (lanes - H) // MB, l - lanes // MB, -(10 ** 6))
    tx = pos[2] + jnp.where(l < (breadth + H) // MB, l, far)
    sx = ((bx == tx) & (bx >= x_first_block)).astype(jnp.float32)
    return sy, sx


def _cells(fl, zb, sy, sx):
    a = jnp.dot(sy, fl[zb], preferred_element_type=jnp.float32)
    return lax.dot_general(a, sx, (((1,), (1,)), ((), ())), preferred_element_type=jnp.float32)


def _inside(pos, rows, lanes, height, breadth, y_total, x_total):
    r = lax.broadcasted_iota(jnp.int32, (rows, lanes), 0)
    l = lax.broadcasted_iota(jnp.int32, (rows, lanes), 1)
    y = pos[1] * MB + jnp.where(r < height + H, r, r - rows)
    far = jnp.where(l >= lanes - H, l - lanes, -(10 ** 6))
    x = pos[2] * MB + jnp.where(l < breadth + H, l, far)
    return (y >= 0) & (y < y_total) & (x >= 0) & (x < x_total)


def _em_kernel(factor, last, pair, depth, totals, pos, prof, fl, f, mat, w, zlo, zhi, *outs):
    diagonal = 6.0 + SHIFT
    if last:
        (heat, own) = outs
    elif pair:
        (o, oz0) = outs
        oz1 = None
    else:
        (o, oz0, oz1) = outs
    bottom = pos[0] == 0
    height, breadth, y_total, x_total = totals
    rows, lanes = f.shape[1], f.shape[2]
    keep = _inside(pos, rows, lanes, height, breadth, y_total, x_total)
    sy, sx = _selectors(pos, rows, lanes, height, breadth, 0)
    masks = [_cells(fl, pos[0] + zo, sy, sx) for zo in range(depth // MB)]
    for z in range(depth):
        cur = [f[c * depth + z] for c in range(2)]
        beside = []
        for c in range(2):
            if z + 1 < depth:
                z_up = f[c * depth + z + 1]
            else:
                z_up = jnp.where(bottom, zhi[c], 0.0) if pair else zhi[c]
            if z > 0:
                z_dn = f[c * depth + z - 1]
            else:
                z_dn = jnp.where(bottom, 0.0, zlo[c]) if pair else zlo[c]
            y_up, y_dn, x_up, x_dn = _rolls(cur[c])
            total = z_up + z_dn
            total = total + y_up + y_dn
            beside.append(total + x_up + x_dn)
        k = masks[z // MB] * mat[z]
        s0 = prof[z] * w[0]
        s1 = prof[z] * w[1]
        real_res = s0 - (diagonal * cur[0] - k * cur[1] - beside[0])
        imag_res = s1 - (diagonal * cur[1] + k * cur[0] - beside[1])
        scaled = factor / (diagonal * diagonal + k * k)
        n0 = jnp.where(keep, cur[0] + scaled * (diagonal * real_res + k * imag_res), 0.0)
        n1 = jnp.where(keep, cur[1] + scaled * (diagonal * imag_res - k * real_res), 0.0)
        if last:
            heat[z] = HEATING * k * (n0 * n0 + n1 * n1)
            own[0, z] = n0[0:height, 0:breadth]
            own[1, z] = n1[0:height, 0:breadth]
        else:
            o[z] = n0
            o[depth + z] = n1
            if z == 0:
                oz0[0] = n0
                oz0[1] = n1
            if z == depth - 1 and pair:
                oz0[0] = jnp.where(bottom, n0, oz0[0])
                oz0[1] = jnp.where(bottom, n1, oz0[1])
            elif z == depth - 1:
                oz1[0] = n0
                oz1[1] = n1


def _heat_kernel(last, pair, depth, totals, pos, fl, t, q, tzlo, tzhi, *outs):
    if last:
        (own,) = outs
    elif pair:
        (o, oz0) = outs
        oz1 = None
    else:
        (o, oz0, oz1) = outs
    bottom = pos[0] == 0
    height, breadth, x_first_block = totals
    rows, lanes = t.shape[1], t.shape[2]
    sy, sx = _selectors(pos, rows, lanes, height, breadth, x_first_block)
    zb_total = fl.shape[0]
    below = pos[0] - 1
    above = pos[0] + depth // MB
    m_below = _cells(fl, jnp.maximum(below, 0), sy, sx) * jnp.where(below >= 0, 1.0, 0.0)
    m_above = _cells(fl, jnp.minimum(above, zb_total - 1), sy, sx) * jnp.where(
        above < zb_total, 1.0, 0.0)
    m_own = [_cells(fl, pos[0] + zo, sy, sx) for zo in range(depth // MB)]
    planes = [m_below] + [m_own[z // MB] for z in range(depth)] + [m_above]
    if pair:
        below_t = jnp.where(bottom, 0.0, tzlo[...])
        above_t = jnp.where(bottom, tzhi[...], 0.0)
    else:
        below_t, above_t = tzlo[...], tzhi[...]
    temps = [below_t] + [t[z] for z in range(depth)] + [above_t]
    kaps = [1.0 / (1.0 + SOFTEN * v * v) for v in temps]
    for z in range(depth):
        c = temps[z + 1]
        centre_kappa = kaps[z + 1]
        y_up, y_dn, x_up, x_dn = _rolls(c)
        ky_up, ky_dn, kx_up, kx_dn = _rolls(centre_kappa)
        mc = planes[z + 1]
        my_up, my_dn, mx_up, mx_dn = _rolls(mc)
        flux = jnp.zeros_like(c)
        for other, kappa, other_mask in (
            (temps[z + 2], kaps[z + 2], planes[z + 2]), (temps[z], kaps[z], planes[z]),
            (y_up, ky_up, my_up), (y_dn, ky_dn, my_dn), (x_up, kx_up, mx_up), (x_dn, kx_dn, mx_dn),
        ):
            flux = flux + other_mask * (centre_kappa + kappa) * (other - c)
        new = c + 0.5 * CONDUCT * mc * flux + q[z]
        if last:
            own[z] = new[0:height, 0:breadth]
        else:
            o[z] = new
            if z == 0:
                oz0[...] = new
            if z == depth - 1 and pair:
                oz0[...] = jnp.where(bottom, new, oz0[...])
            elif z == depth - 1:
                oz1[...] = new


def _vmem_call(kernel, out_shape, n_in, n_smem=0):
    specs = [pl.BlockSpec(memory_space=pltpu.SMEM)] * n_smem
    specs += [pl.BlockSpec(memory_space=pltpu.VMEM)] * (n_in - n_smem)
    return pl.pallas_call(
        kernel,
        out_shape=out_shape,
        in_specs=specs,
        out_specs=[pl.BlockSpec(memory_space=pltpu.VMEM)] * len(out_shape),
    )


def _line_pairs(n, first=0):
    up = [(i, i + 1) for i in range(first, n - 1)]
    down = [(j, i) for i, j in up]
    return up, down


def _broadcast_blocks(own, me, n, first):
    if (n, first) == (4, 1):
        r1 = lax.ppermute(own, "gx", [(2, 0), (3, 1), (1, 2)])
        a = jnp.where((me == 0) | (me == 2), r1, own)
        b = jnp.where((me == 1) | (me == 0), r1, own)
        r2 = lax.ppermute(jnp.stack([a, b]), "gx", [(0, 1), (1, 0), (2, 3), (3, 2)])
        b1 = jnp.where(me == 1, own, jnp.where(me == 2, r1, r2[0]))
        b2 = jnp.where(me == 0, r1, jnp.where(me == 1, r2[0], jnp.where(me == 2, own, r2[1])))
        b3 = jnp.where(me == 0, r2[1], jnp.where(me == 1, r1, jnp.where(me == 2, r2[0], own)))
        return jnp.concatenate([b1, b2, b3], axis=2)
    owners = list(range(first, n))
    held = [own]
    for s in range(1, n):
        held.append(lax.ppermute(own, "gx", [(k, (k + s) % n) for k in owners]))
    held = jnp.stack(held)
    pieces = [lax.dynamic_index_in_dim(held, (me - k) % n, 0, keepdims=False) for k in owners]
    return jnp.concatenate(pieces, axis=2)


def on_device(
    earlier_window_curl_state,
    material_resistivity_inverse,
    winding_current_pattern,
    winding_axial_centre,
    specimen_presence_flags,
    specimen_kelvin_values,
):
    depth, height, breadth = material_resistivity_inverse.shape
    n_gz, n_gy, n_gx = lax.axis_size("gz"), lax.axis_size("gy"), lax.axis_size("gx")
    z_total, y_total, x_total = depth * n_gz, height * n_gy, breadth * n_gx
    gz_i, gy_i, gx_i = lax.axis_index("gz"), lax.axis_index("gy"), lax.axis_index("gx")
    z_start, y_start, x_start = gz_i * depth, gy_i * height, gx_i * breadth
    rows = height + 2 * H
    lanes = -(-(breadth + 2 * H) // 128) * 128
    gap = lanes - breadth - 2 * H
    specimen_columns = specimen_kelvin_values.shape[2]
    offset = x_total - specimen_columns
    assert offset % breadth == 0 and depth % MB == 0 and height % MB == 0 and breadth % MB == 0
    first_owner = offset // breadth

    coil_width = z_total // 4
    axial = (
        (z_start + jnp.arange(depth)).astype(jnp.float32)
        - winding_axial_centre[0].astype(jnp.float32)
    ) / coil_width
    profile = 1.0 / (1.0 + axial * axial)

    stack = jnp.concatenate(
        [earlier_window_curl_state.reshape(2 * depth, height, breadth), material_resistivity_inverse,
         winding_current_pattern], axis=0)
    up_x, down_x = _line_pairs(n_gx)
    from_left = lax.ppermute(jnp.swapaxes(stack[:, :, breadth - H:], 1, 2), "gx", up_x)
    from_right = lax.ppermute(jnp.swapaxes(stack[:, :, :H], 1, 2), "gx", down_x)
    nch = stack.shape[0]
    xext = jnp.concatenate(
        [stack, jnp.swapaxes(from_right, 1, 2), jnp.zeros((nch, height, gap), jnp.float32),
         jnp.swapaxes(from_left, 1, 2)], axis=2)

    j_start = x_start - offset
    kpad = jnp.pad(specimen_kelvin_values, ((0, 0), (0, 0), (H, H)))
    t_body = lax.dynamic_slice_in_dim(kpad, j_start + H, breadth + H, 2)
    t_tail = lax.dynamic_slice_in_dim(kpad, j_start, H, 2)
    t_x = jnp.concatenate([t_body, jnp.zeros((depth, height, gap), jnp.float32), t_tail], axis=2)

    ystack = jnp.concatenate([xext, t_x], axis=0)
    up_y, down_y = _line_pairs(n_gy)
    from_above = lax.ppermute(ystack[:, height - H:, :], "gy", up_y)
    from_below = lax.ppermute(ystack[:, :H, :], "gy", down_y)
    frame = jnp.concatenate([ystack, from_below, from_above], axis=1)
    field = frame[: 2 * depth]
    material = frame[2 * depth: 3 * depth]
    winding = frame[3 * depth: 3 * depth + 2]
    kelvin = frame[3 * depth + 2:]

    fb = specimen_presence_flags.shape
    flags = jnp.pad(specimen_presence_flags.astype(jnp.float32),
                    ((0, 0), (0, 128 - fb[1]), (0, 128 - fb[2])))
    pos = jnp.stack([z_start // MB, y_start // MB, x_start // MB]).astype(jnp.int32)

    up_z, down_z = _line_pairs(n_gz)
    fshape = jax.ShapeDtypeStruct((2 * depth, rows, lanes), jnp.float32)
    plane2 = jax.ShapeDtypeStruct((2, rows, lanes), jnp.float32)
    qshape = jax.ShapeDtypeStruct((depth, rows, lanes), jnp.float32)
    oshape = jax.ShapeDtypeStruct((2, depth, height, breadth), jnp.float32)
    lo_plane = field[jnp.array([0, depth])]
    hi_plane = field[jnp.array([depth - 1, 2 * depth - 1])]
    pair = n_gz == 2
    both = [(0, 1), (1, 0)]

    used = breadth + 2 * H
    dense = (rows * used) % 128 == 0

    def squeeze(p):
        q = jnp.concatenate([p[..., : breadth + H], p[..., lanes - H:]], axis=-1)
        return q.reshape(q.shape[:-2] + (rows * used // 128, 128)) if dense else q

    def unsqueeze(p):
        if dense:
            p = p.reshape(p.shape[:-2] + (rows, used))
        filler = jnp.zeros(p.shape[:-1] + (gap,), jnp.float32)
        return jnp.concatenate([p[..., : breadth + H], filler, p[..., breadth + H:]], axis=-1)

    def exchange(hi, lo, sent):
        if pair:
            got = unsqueeze(lax.ppermute(squeeze(sent), "gz", both))
            return got, got
        return (unsqueeze(lax.ppermute(squeeze(hi), "gz", up_z)),
                unsqueeze(lax.ppermute(squeeze(lo), "gz", down_z)))

    if pair:
        send = jnp.where(gz_i == 0, hi_plane, lo_plane)
    for i, factor in enumerate(WEIGHTS):
        last = i == len(WEIGHTS) - 1
        zlo, zhi = exchange(hi_plane, lo_plane, send if pair else None)
        outs = (qshape, oshape) if last else (fshape, plane2) if pair else (fshape, plane2, plane2)
        res = _vmem_call(
            lambda *r, factor=factor, last=last: _em_kernel(
                factor, last, pair, depth, (height, breadth, y_total, x_total), *r), outs, 8, 2
        )(pos, profile, flags, field, material, winding, zlo, zhi)
        if last:
            heat, field_out = res
        elif pair:
            field, send = res
        else:
            field, lo_plane, hi_plane = res

    tshape = jax.ShapeDtypeStruct((depth, rows, lanes), jnp.float32)
    tplane = jax.ShapeDtypeStruct((rows, lanes), jnp.float32)
    town = jax.ShapeDtypeStruct((depth, height, breadth), jnp.float32)
    lo_t, hi_t = kelvin[0], kelvin[depth - 1]
    if pair:
        send_t = jnp.where(gz_i == 0, hi_t, lo_t)
    for number in range(STEPS):
        last = number == STEPS - 1
        tzlo, tzhi = exchange(hi_t, lo_t, send_t if pair else None)
        outs = (town,) if last else (tshape, tplane) if pair else (tshape, tplane, tplane)
        res = _vmem_call(
            lambda *r, last=last: _heat_kernel(
                last, pair, depth, (height, breadth, offset // MB), *r), outs, 6, 1
        )(pos, flags, kelvin, heat, tzlo, tzhi)
        if last:
            (own_t,) = res
        elif pair:
            kelvin, send_t = res
        else:
            kelvin, lo_t, hi_t = res

    segment_kelvin = _broadcast_blocks(own_t, gx_i, n_gx, first_owner)
    return (field_out, segment_kelvin)


def solution(mesh):
    placed = (
        P(None, "gz", "gy", "gx"),
        P("gz", "gy", "gx"),
        P(None, "gy", "gx"),
        P(),
        P(),
        P("gz", "gy", None),
    )
    return jax.shard_map(
        on_device,
        mesh=mesh,
        in_specs=placed,
        out_specs=(P(None, "gz", "gy", "gx"), P("gz", "gy", None)),
        check_vma=False,
    )
```

```python
import jax
import jax.numpy as jnp
from jax import lax
from jax.experimental import pallas as pl
from jax.experimental.pallas import tpu as pltpu
from jax.sharding import PartitionSpec as P

MB = 8
STEPS = 4


WEIGHTS = (0.8, 1.0, 1.25)
SHIFT = 0.2
HEATING = 0.02
CONDUCT = 0.16
SOFTEN = 0.25

H = MB


def _rolls(a):
    rows, lanes = a.shape
    return (
        pltpu.roll(a, rows - 1, 0), pltpu.roll(a, 1, 0),
        pltpu.roll(a, lanes - 1, 1), pltpu.roll(a, 1, 1),
    )


def _selectors(pos, rows, lanes, height, breadth, x_first_block):
    shift = MB.bit_length() - 1
    r = lax.shift_right_logical(lax.broadcasted_iota(jnp.int32, (rows, 128), 0), shift)
    b = lax.broadcasted_iota(jnp.int32, (rows, 128), 1)
    ty = pos[1] + jnp.where(r < (height + H) // MB, r, r - rows // MB)
    sy = (b == ty).astype(jnp.float32)
    l = lax.shift_right_logical(lax.broadcasted_iota(jnp.int32, (lanes, 128), 0), shift)
    bx = lax.broadcasted_iota(jnp.int32, (lanes, 128), 1)
    far = jnp.where(l >= (lanes - H) // MB, l - lanes // MB, -(10 ** 6))
    tx = pos[2] + jnp.where(l < (breadth + H) // MB, l, far)
    sx = ((bx == tx) & (bx >= x_first_block)).astype(jnp.float32)
    return sy, sx


def _cells(fl, zb, sy, sx):
    a = jnp.dot(sy, fl[zb], preferred_element_type=jnp.float32)
    return lax.dot_general(a, sx, (((1,), (1,)), ((), ())), preferred_element_type=jnp.float32)


def _inside(pos, rows, lanes, height, breadth, y_total, x_total):
    r = lax.broadcasted_iota(jnp.int32, (rows, lanes), 0)
    l = lax.broadcasted_iota(jnp.int32, (rows, lanes), 1)
    y = pos[1] * MB + jnp.where(r < height + H, r, r - rows)
    far = jnp.where(l >= lanes - H, l - lanes, -(10 ** 6))
    x = pos[2] * MB + jnp.where(l < breadth + H, l, far)
    return (y >= 0) & (y < y_total) & (x >= 0) & (x < x_total)


def _em_kernel(factor, last, pair, depth, totals, pos, prof, fl, f, mat, w, zlo, zhi, *outs):
    diagonal = 6.0 + SHIFT
    if last:
        (heat, own) = outs
    elif pair:
        (o, oz0) = outs
        oz1 = None
    else:
        (o, oz0, oz1) = outs
    bottom = pos[0] == 0
    height, breadth, y_total, x_total = totals
    rows, lanes = f.shape[1], f.shape[2]
    keep = _inside(pos, rows, lanes, height, breadth, y_total, x_total)
    sy, sx = _selectors(pos, rows, lanes, height, breadth, 0)
    masks = [_cells(fl, pos[0] + zo, sy, sx) for zo in range(depth // MB)]
    for z in range(depth):
        cur = [f[c * depth + z] for c in range(2)]
        beside = []
        for c in range(2):
            if z + 1 < depth:
                z_up = f[c * depth + z + 1]
            else:
                z_up = jnp.where(bottom, zhi[c], 0.0) if pair else zhi[c]
            if z > 0:
                z_dn = f[c * depth + z - 1]
            else:
                z_dn = jnp.where(bottom, 0.0, zlo[c]) if pair else zlo[c]
            y_up, y_dn, x_up, x_dn = _rolls(cur[c])
            total = z_up + z_dn
            total = total + y_up + y_dn
            beside.append(total + x_up + x_dn)
        k = masks[z // MB] * mat[z]
        s0 = prof[z] * w[0]
        s1 = prof[z] * w[1]
        real_res = s0 - (diagonal * cur[0] - k * cur[1] - beside[0])
        imag_res = s1 - (diagonal * cur[1] + k * cur[0] - beside[1])
        scaled = factor / (diagonal * diagonal + k * k)
        n0 = jnp.where(keep, cur[0] + scaled * (diagonal * real_res + k * imag_res), 0.0)
        n1 = jnp.where(keep, cur[1] + scaled * (diagonal * imag_res - k * real_res), 0.0)
        if last:
            heat[z] = HEATING * k * (n0 * n0 + n1 * n1)
            own[0, z] = n0[0:height, 0:breadth]
            own[1, z] = n1[0:height, 0:breadth]
        else:
            o[z] = n0
            o[depth + z] = n1
            if z == 0:
                oz0[0] = n0
                oz0[1] = n1
            if z == depth - 1 and pair:
                oz0[0] = jnp.where(bottom, n0, oz0[0])
                oz0[1] = jnp.where(bottom, n1, oz0[1])
            elif z == depth - 1:
                oz1[0] = n0
                oz1[1] = n1


def _heat_kernel(last, pair, depth, totals, pos, fl, t, q, tzlo, tzhi, *outs):
    if last:
        (own,) = outs
    elif pair:
        (o, oz0) = outs
        oz1 = None
    else:
        (o, oz0, oz1) = outs
    bottom = pos[0] == 0
    height, breadth, x_first_block = totals
    rows, lanes = t.shape[1], t.shape[2]
    sy, sx = _selectors(pos, rows, lanes, height, breadth, x_first_block)
    zb_total = fl.shape[0]
    below = pos[0] - 1
    above = pos[0] + depth // MB
    m_below = _cells(fl, jnp.maximum(below, 0), sy, sx) * jnp.where(below >= 0, 1.0, 0.0)
    m_above = _cells(fl, jnp.minimum(above, zb_total - 1), sy, sx) * jnp.where(
        above < zb_total, 1.0, 0.0)
    m_own = [_cells(fl, pos[0] + zo, sy, sx) for zo in range(depth // MB)]
    planes = [m_below] + [m_own[z // MB] for z in range(depth)] + [m_above]
    if pair:
        below_t = jnp.where(bottom, 0.0, tzlo[...])
        above_t = jnp.where(bottom, tzhi[...], 0.0)
    else:
        below_t, above_t = tzlo[...], tzhi[...]
    temps = [below_t] + [t[z] for z in range(depth)] + [above_t]
    kaps = [1.0 / (1.0 + SOFTEN * v * v) for v in temps]
    for z in range(depth):
        c = temps[z + 1]
        centre_kappa = kaps[z + 1]
        y_up, y_dn, x_up, x_dn = _rolls(c)
        ky_up, ky_dn, kx_up, kx_dn = _rolls(centre_kappa)
        mc = planes[z + 1]
        my_up, my_dn, mx_up, mx_dn = _rolls(mc)
        flux = jnp.zeros_like(c)
        for other, kappa, other_mask in (
            (temps[z + 2], kaps[z + 2], planes[z + 2]), (temps[z], kaps[z], planes[z]),
            (y_up, ky_up, my_up), (y_dn, ky_dn, my_dn), (x_up, kx_up, mx_up), (x_dn, kx_dn, mx_dn),
        ):
            flux = flux + other_mask * (centre_kappa + kappa) * (other - c)
        new = c + 0.5 * CONDUCT * mc * flux + q[z]
        if last:
            own[z] = new[0:height, 0:breadth]
        else:
            o[z] = new
            if z == 0:
                oz0[...] = new
            if z == depth - 1 and pair:
                oz0[...] = jnp.where(bottom, new, oz0[...])
            elif z == depth - 1:
                oz1[...] = new


def _vmem_call(kernel, out_shape, n_in, n_smem=0):
    specs = [pl.BlockSpec(memory_space=pltpu.SMEM)] * n_smem
    specs += [pl.BlockSpec(memory_space=pltpu.VMEM)] * (n_in - n_smem)
    return pl.pallas_call(
        kernel,
        out_shape=out_shape,
        in_specs=specs,
        out_specs=[pl.BlockSpec(memory_space=pltpu.VMEM)] * len(out_shape),
    )


def _line_pairs(n, first=0):
    up = [(i, i + 1) for i in range(first, n - 1)]
    down = [(j, i) for i, j in up]
    return up, down


def _broadcast_blocks(own, me, n, first):
    if (n, first) == (4, 1):
        r1 = lax.ppermute(own, "gx", [(2, 0), (3, 1), (1, 2)])
        a = jnp.where((me == 0) | (me == 2), r1, own)
        b = jnp.where((me == 1) | (me == 0), r1, own)
        r2 = lax.ppermute(jnp.stack([a, b]), "gx", [(0, 1), (1, 0), (2, 3), (3, 2)])
        b1 = jnp.where(me == 1, own, jnp.where(me == 2, r1, r2[0]))
        b2 = jnp.where(me == 0, r1, jnp.where(me == 1, r2[0], jnp.where(me == 2, own, r2[1])))
        b3 = jnp.where(me == 0, r2[1], jnp.where(me == 1, r1, jnp.where(me == 2, r2[0], own)))
        return jnp.concatenate([b1, b2, b3], axis=2)
    owners = list(range(first, n))
    held = [own]
    for s in range(1, n):
        held.append(lax.ppermute(own, "gx", [(k, (k + s) % n) for k in owners]))
    held = jnp.stack(held)
    pieces = [lax.dynamic_index_in_dim(held, (me - k) % n, 0, keepdims=False) for k in owners]
    return jnp.concatenate(pieces, axis=2)


def on_device(
    earlier_window_curl_state,
    material_resistivity_inverse,
    winding_current_pattern,
    winding_axial_centre,
    specimen_presence_flags,
    specimen_kelvin_values,
):
    depth, height, breadth = material_resistivity_inverse.shape
    n_gz, n_gy, n_gx = lax.axis_size("gz"), lax.axis_size("gy"), lax.axis_size("gx")
    z_total, y_total, x_total = depth * n_gz, height * n_gy, breadth * n_gx
    gz_i, gy_i, gx_i = lax.axis_index("gz"), lax.axis_index("gy"), lax.axis_index("gx")
    z_start, y_start, x_start = gz_i * depth, gy_i * height, gx_i * breadth
    rows = height + 2 * H
    lanes = -(-(breadth + 2 * H) // 128) * 128
    gap = lanes - breadth - 2 * H
    specimen_columns = specimen_kelvin_values.shape[2]
    offset = x_total - specimen_columns
    assert offset % breadth == 0 and depth % MB == 0 and height % MB == 0 and breadth % MB == 0
    first_owner = offset // breadth

    coil_width = z_total // 4
    axial = (
        (z_start + jnp.arange(depth)).astype(jnp.float32)
        - winding_axial_centre[0].astype(jnp.float32)
    ) / coil_width
    profile = 1.0 / (1.0 + axial * axial)

    stack = jnp.concatenate(
        [earlier_window_curl_state.reshape(2 * depth, height, breadth), material_resistivity_inverse,
         winding_current_pattern], axis=0)
    up_x, down_x = _line_pairs(n_gx)
    from_left = lax.ppermute(jnp.swapaxes(stack[:, :, breadth - H:], 1, 2), "gx", up_x)
    from_right = lax.ppermute(jnp.swapaxes(stack[:, :, :H], 1, 2), "gx", down_x)
    nch = stack.shape[0]
    xext = jnp.concatenate(
        [stack, jnp.swapaxes(from_right, 1, 2), jnp.zeros((nch, height, gap), jnp.float32),
         jnp.swapaxes(from_left, 1, 2)], axis=2)

    j_start = x_start - offset
    kpad = jnp.pad(specimen_kelvin_values, ((0, 0), (0, 0), (H, H)))
    t_body = lax.dynamic_slice_in_dim(kpad, j_start + H, breadth + H, 2)
    t_tail = lax.dynamic_slice_in_dim(kpad, j_start, H, 2)
    t_x = jnp.concatenate([t_body, jnp.zeros((depth, height, gap), jnp.float32), t_tail], axis=2)

    ystack = jnp.concatenate([xext, t_x], axis=0)
    up_y, down_y = _line_pairs(n_gy)
    from_above = lax.ppermute(ystack[:, height - H:, :], "gy", up_y)
    from_below = lax.ppermute(ystack[:, :H, :], "gy", down_y)
    frame = jnp.concatenate([ystack, from_below, from_above], axis=1)
    field = frame[: 2 * depth]
    material = frame[2 * depth: 3 * depth]
    winding = frame[3 * depth: 3 * depth + 2]
    kelvin = frame[3 * depth + 2:]

    fb = specimen_presence_flags.shape
    flags = jnp.pad(specimen_presence_flags.astype(jnp.float32),
                    ((0, 0), (0, 128 - fb[1]), (0, 128 - fb[2])))
    pos = jnp.stack([z_start // MB, y_start // MB, x_start // MB]).astype(jnp.int32)

    up_z, down_z = _line_pairs(n_gz)
    fshape = jax.ShapeDtypeStruct((2 * depth, rows, lanes), jnp.float32)
    plane2 = jax.ShapeDtypeStruct((2, rows, lanes), jnp.float32)
    qshape = jax.ShapeDtypeStruct((depth, rows, lanes), jnp.float32)
    oshape = jax.ShapeDtypeStruct((2, depth, height, breadth), jnp.float32)
    tshape = jax.ShapeDtypeStruct((depth, rows, lanes), jnp.float32)
    tplane = jax.ShapeDtypeStruct((rows, lanes), jnp.float32)
    town = jax.ShapeDtypeStruct((depth, height, breadth), jnp.float32)
    em_totals = (height, breadth, y_total, x_total)
    t_totals = (height, breadth, offset // MB)
    lo_idx = jnp.array([0, depth])
    hi_idx = jnp.array([depth - 1, 2 * depth - 1])
    pair = n_gz == 2
    both = [(0, 1), (1, 0)]
    if pair:
        top = gz_i == 0
        first = jnp.concatenate(
            [jnp.where(top, field[hi_idx], field[lo_idx]),
             jnp.where(top, kelvin[depth - 1], kelvin[0])[None]], axis=0)
        got = lax.ppermute(first, "gz", both)
    else:
        lo_plane, hi_plane = field[lo_idx], field[hi_idx]
        tzlo0 = lax.ppermute(kelvin[depth - 1], "gz", up_z)
        tzhi0 = lax.ppermute(kelvin[0], "gz", down_z)
    for i, factor in enumerate(WEIGHTS):
        last = i == len(WEIGHTS) - 1
        if pair:
            zlo = zhi = got if i == 0 else lax.ppermute(send, "gz", both)
        else:
            zlo = lax.ppermute(hi_plane, "gz", up_z)
            zhi = lax.ppermute(lo_plane, "gz", down_z)
        if last:
            outs = (qshape, oshape, tshape, tplane) if pair else (
                qshape, oshape, tshape, tplane, tplane)

            def fused(pos_r, prof_r, fl_r, f_r, mat_r, w_r, zlo_r, zhi_r, t_r, *rest,
                      factor=factor):
                if pair:
                    tzlo_r = tzhi_r = rest[0].at[2]
                    outs_r = rest[1:]
                else:
                    tzlo_r, tzhi_r = rest[0], rest[1]
                    outs_r = rest[2:]
                q_r, own_r = outs_r[0], outs_r[1]
                _em_kernel(factor, True, pair, depth, em_totals, pos_r, prof_r, fl_r, f_r, mat_r,
                           w_r, zlo_r, zhi_r, q_r, own_r)
                _heat_kernel(False, pair, depth, t_totals, pos_r, fl_r, t_r, q_r, tzlo_r, tzhi_r,
                             *outs_r[2:])

            extra = (got,) if pair else (tzlo0, tzhi0)
            res = _vmem_call(fused, outs, 9 + len(extra), 2)(
                pos, profile, flags, field, material, winding, zlo, zhi, kelvin, *extra)
            heat, field_out, kelvin = res[0], res[1], res[2]
            if pair:
                send_t = res[3]
            else:
                lo_t, hi_t = res[3], res[4]
        else:
            outs = (fshape, plane2) if pair else (fshape, plane2, plane2)
            res = _vmem_call(
                lambda *r, factor=factor: _em_kernel(
                    factor, False, pair, depth, em_totals, *r), outs, 8, 2
            )(pos, profile, flags, field, material, winding, zlo, zhi)
            if pair:
                field, send = res
            else:
                field, lo_plane, hi_plane = res

    for number in range(1, STEPS):
        last = number == STEPS - 1
        if pair:
            tzlo = tzhi = lax.ppermute(send_t, "gz", both)
        else:
            tzlo = lax.ppermute(hi_t, "gz", up_z)
            tzhi = lax.ppermute(lo_t, "gz", down_z)
        outs = (town,) if last else (tshape, tplane) if pair else (tshape, tplane, tplane)
        res = _vmem_call(
            lambda *r, last=last: _heat_kernel(last, pair, depth, t_totals, *r), outs, 6, 1
        )(pos, flags, kelvin, heat, tzlo, tzhi)
        if last:
            (own_t,) = res
        elif pair:
            kelvin, send_t = res
        else:
            kelvin, lo_t, hi_t = res

    segment_kelvin = _broadcast_blocks(own_t, gx_i, n_gx, first_owner)
    return (field_out, segment_kelvin)


def solution(mesh):
    placed = (
        P(None, "gz", "gy", "gx"),
        P("gz", "gy", "gx"),
        P(None, "gy", "gx"),
        P(),
        P(),
        P("gz", "gy", None),
    )
    return jax.shard_map(
        on_device,
        mesh=mesh,
        in_specs=placed,
        out_specs=(P(None, "gz", "gy", "gx"), P("gz", "gy", None)),
        check_vma=False,
    )
```

```python
import jax
import jax.numpy as jnp
from jax import lax
from jax.experimental import pallas as pl
from jax.experimental.pallas import tpu as pltpu
from jax.sharding import PartitionSpec as P

MB = 8
STEPS = 4


WEIGHTS = (0.8, 1.0, 1.25)
SHIFT = 0.2
HEATING = 0.02
CONDUCT = 0.16
SOFTEN = 0.25

H = MB


class _Rows:
    def __init__(self, main, after, before, base, count):
        self.parts, self.base = (main, after, before), base
        self.shape = (count, main.shape[1] + after.shape[1] + before.shape[1], main.shape[2])

    def __getitem__(self, i):
        return jnp.concatenate([p[self.base + i] for p in self.parts], axis=0)


def _rolls(a):
    rows, lanes = a.shape
    return (
        pltpu.roll(a, rows - 1, 0), pltpu.roll(a, 1, 0),
        pltpu.roll(a, lanes - 1, 1), pltpu.roll(a, 1, 1),
    )


def _selectors(pos, rows, lanes, height, breadth, x_first_block):
    shift = MB.bit_length() - 1
    r = lax.shift_right_logical(lax.broadcasted_iota(jnp.int32, (rows, 128), 0), shift)
    b = lax.broadcasted_iota(jnp.int32, (rows, 128), 1)
    ty = pos[1] + jnp.where(r < (height + H) // MB, r, r - rows // MB)
    sy = (b == ty).astype(jnp.float32)
    l = lax.shift_right_logical(lax.broadcasted_iota(jnp.int32, (lanes, 128), 0), shift)
    bx = lax.broadcasted_iota(jnp.int32, (lanes, 128), 1)
    far = jnp.where(l >= (lanes - H) // MB, l - lanes // MB, -(10 ** 6))
    tx = pos[2] + jnp.where(l < (breadth + H) // MB, l, far)
    sx = ((bx == tx) & (bx >= x_first_block)).astype(jnp.float32)
    return sy, sx


def _cells(fl, zb, sy, sx):
    a = jnp.dot(sy, fl[zb], preferred_element_type=jnp.float32)
    return lax.dot_general(a, sx, (((1,), (1,)), ((), ())), preferred_element_type=jnp.float32)


def _inside(pos, rows, lanes, height, breadth, y_total, x_total):
    r = lax.broadcasted_iota(jnp.int32, (rows, lanes), 0)
    l = lax.broadcasted_iota(jnp.int32, (rows, lanes), 1)
    y = pos[1] * MB + jnp.where(r < height + H, r, r - rows)
    far = jnp.where(l >= lanes - H, l - lanes, -(10 ** 6))
    x = pos[2] * MB + jnp.where(l < breadth + H, l, far)
    return (y >= 0) & (y < y_total) & (x >= 0) & (x < x_total)


def _em_kernel(factor, last, pair, depth, totals, pos, prof, fl, f, mat, w, zlo, zhi, *outs):
    diagonal = 6.0 + SHIFT
    if last:
        (heat, own) = outs
    elif pair:
        (o, oz0) = outs
        oz1 = None
    else:
        (o, oz0, oz1) = outs
    bottom = pos[0] == 0
    height, breadth, y_total, x_total = totals
    rows, lanes = f.shape[1], f.shape[2]
    keep = _inside(pos, rows, lanes, height, breadth, y_total, x_total)
    sy, sx = _selectors(pos, rows, lanes, height, breadth, 0)
    masks = [_cells(fl, pos[0] + zo, sy, sx) for zo in range(depth // MB)]
    for z in range(depth):
        cur = [f[c * depth + z] for c in range(2)]
        beside = []
        for c in range(2):
            if z + 1 < depth:
                z_up = f[c * depth + z + 1]
            else:
                z_up = jnp.where(bottom, zhi[c], 0.0) if pair else zhi[c]
            if z > 0:
                z_dn = f[c * depth + z - 1]
            else:
                z_dn = jnp.where(bottom, 0.0, zlo[c]) if pair else zlo[c]
            y_up, y_dn, x_up, x_dn = _rolls(cur[c])
            total = z_up + z_dn
            total = total + y_up + y_dn
            beside.append(total + x_up + x_dn)
        k = masks[z // MB] * mat[z]
        s0 = prof[z] * w[0]
        s1 = prof[z] * w[1]
        real_res = s0 - (diagonal * cur[0] - k * cur[1] - beside[0])
        imag_res = s1 - (diagonal * cur[1] + k * cur[0] - beside[1])
        scaled = factor / (diagonal * diagonal + k * k)
        n0 = jnp.where(keep, cur[0] + scaled * (diagonal * real_res + k * imag_res), 0.0)
        n1 = jnp.where(keep, cur[1] + scaled * (diagonal * imag_res - k * real_res), 0.0)
        if last:
            heat[z] = HEATING * k * (n0 * n0 + n1 * n1)
            own[0, z] = n0[0:height, 0:breadth]
            own[1, z] = n1[0:height, 0:breadth]
        else:
            o[z] = n0
            o[depth + z] = n1
            if z == 0:
                oz0[0] = n0
                oz0[1] = n1
            if z == depth - 1 and pair:
                oz0[0] = jnp.where(bottom, n0, oz0[0])
                oz0[1] = jnp.where(bottom, n1, oz0[1])
            elif z == depth - 1:
                oz1[0] = n0
                oz1[1] = n1


def _heat_kernel(last, pair, depth, totals, pos, fl, t, q, tzlo, tzhi, *outs):
    if last:
        (own,) = outs
    elif pair:
        (o, oz0) = outs
        oz1 = None
    else:
        (o, oz0, oz1) = outs
    bottom = pos[0] == 0
    height, breadth, x_first_block = totals
    rows, lanes = t.shape[1], t.shape[2]
    sy, sx = _selectors(pos, rows, lanes, height, breadth, x_first_block)
    zb_total = fl.shape[0]
    below = pos[0] - 1
    above = pos[0] + depth // MB
    m_below = _cells(fl, jnp.maximum(below, 0), sy, sx) * jnp.where(below >= 0, 1.0, 0.0)
    m_above = _cells(fl, jnp.minimum(above, zb_total - 1), sy, sx) * jnp.where(
        above < zb_total, 1.0, 0.0)
    m_own = [_cells(fl, pos[0] + zo, sy, sx) for zo in range(depth // MB)]
    planes = [m_below] + [m_own[z // MB] for z in range(depth)] + [m_above]
    if pair:
        below_t = jnp.where(bottom, 0.0, tzlo[...])
        above_t = jnp.where(bottom, tzhi[...], 0.0)
    else:
        below_t, above_t = tzlo[...], tzhi[...]
    temps = [below_t] + [t[z] for z in range(depth)] + [above_t]
    kaps = [1.0 / (1.0 + SOFTEN * v * v) for v in temps]
    for z in range(depth):
        c = temps[z + 1]
        centre_kappa = kaps[z + 1]
        y_up, y_dn, x_up, x_dn = _rolls(c)
        ky_up, ky_dn, kx_up, kx_dn = _rolls(centre_kappa)
        mc = planes[z + 1]
        my_up, my_dn, mx_up, mx_dn = _rolls(mc)
        flux = jnp.zeros_like(c)
        for other, kappa, other_mask in (
            (temps[z + 2], kaps[z + 2], planes[z + 2]), (temps[z], kaps[z], planes[z]),
            (y_up, ky_up, my_up), (y_dn, ky_dn, my_dn), (x_up, kx_up, mx_up), (x_dn, kx_dn, mx_dn),
        ):
            flux = flux + other_mask * (centre_kappa + kappa) * (other - c)
        new = c + 0.5 * CONDUCT * mc * flux + q[z]
        if last:
            own[z] = new[0:height, 0:breadth]
        else:
            o[z] = new
            if z == 0:
                oz0[...] = new
            if z == depth - 1 and pair:
                oz0[...] = jnp.where(bottom, new, oz0[...])
            elif z == depth - 1:
                oz1[...] = new


def _vmem_call(kernel, out_shape, n_in, n_smem=0):
    specs = [pl.BlockSpec(memory_space=pltpu.SMEM)] * n_smem
    specs += [pl.BlockSpec(memory_space=pltpu.VMEM)] * (n_in - n_smem)
    return pl.pallas_call(
        kernel,
        out_shape=out_shape,
        in_specs=specs,
        out_specs=[pl.BlockSpec(memory_space=pltpu.VMEM)] * len(out_shape),
    )


def _line_pairs(n, first=0):
    up = [(i, i + 1) for i in range(first, n - 1)]
    down = [(j, i) for i, j in up]
    return up, down


def _broadcast_blocks(own, me, n, first):
    if (n, first) == (4, 1):
        r1 = lax.ppermute(own, "gx", [(2, 0), (3, 1), (1, 2)])
        a = jnp.where((me == 0) | (me == 2), r1, own)
        b = jnp.where((me == 1) | (me == 0), r1, own)
        r2 = lax.ppermute(jnp.stack([a, b]), "gx", [(0, 1), (1, 0), (2, 3), (3, 2)])
        b1 = jnp.where(me == 1, own, jnp.where(me == 2, r1, r2[0]))
        b2 = jnp.where(me == 0, r1, jnp.where(me == 1, r2[0], jnp.where(me == 2, own, r2[1])))
        b3 = jnp.where(me == 0, r2[1], jnp.where(me == 1, r1, jnp.where(me == 2, r2[0], own)))
        return jnp.concatenate([b1, b2, b3], axis=2)
    owners = list(range(first, n))
    held = [own]
    for s in range(1, n):
        held.append(lax.ppermute(own, "gx", [(k, (k + s) % n) for k in owners]))
    held = jnp.stack(held)
    pieces = [lax.dynamic_index_in_dim(held, (me - k) % n, 0, keepdims=False) for k in owners]
    return jnp.concatenate(pieces, axis=2)


def on_device(
    earlier_window_curl_state,
    material_resistivity_inverse,
    winding_current_pattern,
    winding_axial_centre,
    specimen_presence_flags,
    specimen_kelvin_values,
):
    depth, height, breadth = material_resistivity_inverse.shape
    n_gz, n_gy, n_gx = lax.axis_size("gz"), lax.axis_size("gy"), lax.axis_size("gx")
    z_total, y_total, x_total = depth * n_gz, height * n_gy, breadth * n_gx
    gz_i, gy_i, gx_i = lax.axis_index("gz"), lax.axis_index("gy"), lax.axis_index("gx")
    z_start, y_start, x_start = gz_i * depth, gy_i * height, gx_i * breadth
    rows = height + 2 * H
    lanes = -(-(breadth + 2 * H) // 128) * 128
    gap = lanes - breadth - 2 * H
    specimen_columns = specimen_kelvin_values.shape[2]
    offset = x_total - specimen_columns
    assert offset % breadth == 0 and depth % MB == 0 and height % MB == 0 and breadth % MB == 0
    first_owner = offset // breadth

    coil_width = z_total // 4
    axial = (
        (z_start + jnp.arange(depth)).astype(jnp.float32)
        - winding_axial_centre[0].astype(jnp.float32)
    ) / coil_width
    profile = 1.0 / (1.0 + axial * axial)

    stack = jnp.concatenate(
        [earlier_window_curl_state.reshape(2 * depth, height, breadth), material_resistivity_inverse,
         winding_current_pattern], axis=0)
    up_x, down_x = _line_pairs(n_gx)
    from_left = lax.ppermute(jnp.swapaxes(stack[:, :, breadth - H:], 1, 2), "gx", up_x)
    from_right = lax.ppermute(jnp.swapaxes(stack[:, :, :H], 1, 2), "gx", down_x)
    nch = stack.shape[0]
    xext = jnp.concatenate(
        [stack, jnp.swapaxes(from_right, 1, 2), jnp.zeros((nch, height, gap), jnp.float32),
         jnp.swapaxes(from_left, 1, 2)], axis=2)

    j_start = x_start - offset
    kpad = jnp.pad(specimen_kelvin_values, ((0, 0), (0, 0), (H, H)))
    t_body = lax.dynamic_slice_in_dim(kpad, j_start + H, breadth + H, 2)
    t_tail = lax.dynamic_slice_in_dim(kpad, j_start, H, 2)
    t_x = jnp.concatenate([t_body, jnp.zeros((depth, height, gap), jnp.float32), t_tail], axis=2)

    ystack = jnp.concatenate([xext, t_x], axis=0)
    up_y, down_y = _line_pairs(n_gy)
    from_above = lax.ppermute(ystack[:, height - H:, :], "gy", up_y)
    from_below = lax.ppermute(ystack[:, :H, :], "gy", down_y)
    pieces = (ystack, from_below, from_above)

    def planes_of(idx):
        return jnp.concatenate([p[idx] for p in pieces], axis=-2)

    fb = specimen_presence_flags.shape
    flags = jnp.pad(specimen_presence_flags.astype(jnp.float32),
                    ((0, 0), (0, 128 - fb[1]), (0, 128 - fb[2])))
    pos = jnp.stack([z_start // MB, y_start // MB, x_start // MB]).astype(jnp.int32)

    up_z, down_z = _line_pairs(n_gz)
    fshape = jax.ShapeDtypeStruct((2 * depth, rows, lanes), jnp.float32)
    plane2 = jax.ShapeDtypeStruct((2, rows, lanes), jnp.float32)
    qshape = jax.ShapeDtypeStruct((depth, rows, lanes), jnp.float32)
    oshape = jax.ShapeDtypeStruct((2, depth, height, breadth), jnp.float32)
    tshape = jax.ShapeDtypeStruct((depth, rows, lanes), jnp.float32)
    tplane = jax.ShapeDtypeStruct((rows, lanes), jnp.float32)
    town = jax.ShapeDtypeStruct((depth, height, breadth), jnp.float32)
    em_totals = (height, breadth, y_total, x_total)
    t_totals = (height, breadth, offset // MB)
    lo_idx = jnp.array([0, depth])
    hi_idx = jnp.array([depth - 1, 2 * depth - 1])
    pair = n_gz == 2
    both = [(0, 1), (1, 0)]
    if pair:
        top = gz_i == 0
        first = planes_of(jnp.where(
            top, jnp.array([depth - 1, 2 * depth - 1, 3 * depth + 2 + depth - 1]),
            jnp.array([0, depth, 3 * depth + 2])))
        got = lax.ppermute(first, "gz", both)
    else:
        lo_plane, hi_plane = planes_of(lo_idx), planes_of(hi_idx)
        tzlo0 = lax.ppermute(planes_of(3 * depth + 2 + depth - 1), "gz", up_z)
        tzhi0 = lax.ppermute(planes_of(3 * depth + 2), "gz", down_z)
    for i, factor in enumerate(WEIGHTS):
        last = i == len(WEIGHTS) - 1
        if pair:
            zlo = zhi = got if i == 0 else lax.ppermute(send, "gz", both)
        else:
            zlo = lax.ppermute(hi_plane, "gz", up_z)
            zhi = lax.ppermute(lo_plane, "gz", down_z)
        if last:
            outs = (qshape, oshape, tshape, tplane) if pair else (
                qshape, oshape, tshape, tplane, tplane)

            def fused(pos_r, prof_r, fl_r, f_r, ys_r, yb_r, ya_r, zlo_r, zhi_r, *rest,
                      factor=factor):
                mat_r = _Rows(ys_r, yb_r, ya_r, 2 * depth, depth)
                w_r = _Rows(ys_r, yb_r, ya_r, 3 * depth, 2)
                t_r = _Rows(ys_r, yb_r, ya_r, 3 * depth + 2, depth)
                if pair:
                    tzlo_r = tzhi_r = rest[0].at[2]
                    outs_r = rest[1:]
                else:
                    tzlo_r, tzhi_r = rest[0], rest[1]
                    outs_r = rest[2:]
                q_r, own_r = outs_r[0], outs_r[1]
                _em_kernel(factor, True, pair, depth, em_totals, pos_r, prof_r, fl_r, f_r, mat_r,
                           w_r, zlo_r, zhi_r, q_r, own_r)
                _heat_kernel(False, pair, depth, t_totals, pos_r, fl_r, t_r, q_r, tzlo_r, tzhi_r,
                             *outs_r[2:])

            extra = (got,) if pair else (tzlo0, tzhi0)
            res = _vmem_call(fused, outs, 9 + len(extra), 2)(
                pos, profile, flags, field, *pieces, zlo, zhi, *extra)
            heat, field_out, kelvin = res[0], res[1], res[2]
            if pair:
                send_t = res[3]
            else:
                lo_t, hi_t = res[3], res[4]
        else:
            outs = (fshape, plane2) if pair else (fshape, plane2, plane2)
            def sweep(pos_r, prof_r, fl_r, *rest, factor=factor, i=i):
                if i == 0:
                    ys_r, yb_r, ya_r = rest[:3]
                    f_r = _Rows(ys_r, yb_r, ya_r, 0, 2 * depth)
                    rest = rest[3:]
                else:
                    f_r, ys_r, yb_r, ya_r = rest[:4]
                    rest = rest[4:]
                mat_r = _Rows(ys_r, yb_r, ya_r, 2 * depth, depth)
                w_r = _Rows(ys_r, yb_r, ya_r, 3 * depth, 2)
                _em_kernel(factor, False, pair, depth, em_totals, pos_r, prof_r, fl_r, f_r, mat_r,
                           w_r, *rest)

            fargs = () if i == 0 else (field,)
            res = _vmem_call(sweep, outs, 8 + len(fargs), 2)(
                pos, profile, flags, *fargs, *pieces, zlo, zhi)
            if pair:
                field, send = res
            else:
                field, lo_plane, hi_plane = res

    for number in range(1, STEPS):
        last = number == STEPS - 1
        if pair:
            tzlo = tzhi = lax.ppermute(send_t, "gz", both)
        else:
            tzlo = lax.ppermute(hi_t, "gz", up_z)
            tzhi = lax.ppermute(lo_t, "gz", down_z)
        outs = (town,) if last else (tshape, tplane) if pair else (tshape, tplane, tplane)
        res = _vmem_call(
            lambda *r, last=last: _heat_kernel(last, pair, depth, t_totals, *r), outs, 6, 1
        )(pos, flags, kelvin, heat, tzlo, tzhi)
        if last:
            (own_t,) = res
        elif pair:
            kelvin, send_t = res
        else:
            kelvin, lo_t, hi_t = res

    segment_kelvin = _broadcast_blocks(own_t, gx_i, n_gx, first_owner)
    return (field_out, segment_kelvin)


def solution(mesh):
    placed = (
        P(None, "gz", "gy", "gx"),
        P("gz", "gy", "gx"),
        P(None, "gy", "gx"),
        P(),
        P(),
        P("gz", "gy", None),
    )
    return jax.shard_map(
        on_device,
        mesh=mesh,
        in_specs=placed,
        out_specs=(P(None, "gz", "gy", "gx"), P("gz", "gy", None)),
        check_vma=False,
    )
```

```python
import jax
import jax.numpy as jnp
from jax import lax
from jax.experimental import pallas as pl
from jax.experimental.pallas import tpu as pltpu
from jax.sharding import PartitionSpec as P

MB = 8
STEPS = 4


WEIGHTS = (0.8, 1.0, 1.25)
SHIFT = 0.2
HEATING = 0.02
CONDUCT = 0.16
SOFTEN = 0.25

H = MB


class _Rows:
    def __init__(self, main, after, before, base, count):
        self.parts, self.base = (main, after, before), base
        self.shape = (count, main.shape[1] + after.shape[1] + before.shape[1], main.shape[2])

    def __getitem__(self, i):
        return jnp.concatenate([p[self.base + i] for p in self.parts], axis=0)


def _rolls(a):
    rows, lanes = a.shape
    return (
        pltpu.roll(a, rows - 1, 0), pltpu.roll(a, 1, 0),
        pltpu.roll(a, lanes - 1, 1), pltpu.roll(a, 1, 1),
    )


def _selectors(pos, rows, lanes, height, breadth, x_first_block):
    shift = MB.bit_length() - 1
    r = lax.shift_right_logical(lax.broadcasted_iota(jnp.int32, (rows, 128), 0), shift)
    b = lax.broadcasted_iota(jnp.int32, (rows, 128), 1)
    ty = pos[1] + jnp.where(r < (height + H) // MB, r, r - rows // MB)
    sy = (b == ty).astype(jnp.float32)
    l = lax.shift_right_logical(lax.broadcasted_iota(jnp.int32, (lanes, 128), 0), shift)
    bx = lax.broadcasted_iota(jnp.int32, (lanes, 128), 1)
    far = jnp.where(l >= (lanes - H) // MB, l - lanes // MB, -(10 ** 6))
    tx = pos[2] + jnp.where(l < (breadth + H) // MB, l, far)
    sx = ((bx == tx) & (bx >= x_first_block)).astype(jnp.float32)
    return sy, sx


def _cells(fl, zb, sy, sx):
    a = jnp.dot(sy, fl[zb], preferred_element_type=jnp.float32)
    return lax.dot_general(a, sx, (((1,), (1,)), ((), ())), preferred_element_type=jnp.float32)


def _inside(pos, rows, lanes, height, breadth, y_total, x_total):
    r = lax.broadcasted_iota(jnp.int32, (rows, lanes), 0)
    l = lax.broadcasted_iota(jnp.int32, (rows, lanes), 1)
    y = pos[1] * MB + jnp.where(r < height + H, r, r - rows)
    far = jnp.where(l >= lanes - H, l - lanes, -(10 ** 6))
    x = pos[2] * MB + jnp.where(l < breadth + H, l, far)
    return (y >= 0) & (y < y_total) & (x >= 0) & (x < x_total)


def _em_kernel(factor, last, pair, depth, totals, pos, prof, fl, f, mat, w, zlo, zhi, *outs):
    diagonal = 6.0 + SHIFT
    if last:
        (heat, own) = outs
    elif pair:
        (o, oz0) = outs
        oz1 = None
    else:
        (o, oz0, oz1) = outs
    bottom = pos[0] == 0
    height, breadth, y_total, x_total = totals
    rows, lanes = f.shape[1], f.shape[2]
    keep = _inside(pos, rows, lanes, height, breadth, y_total, x_total)
    sy, sx = _selectors(pos, rows, lanes, height, breadth, 0)
    masks = [_cells(fl, pos[0] + zo, sy, sx) for zo in range(depth // MB)]
    for z in range(depth):
        cur = [f[c * depth + z] for c in range(2)]
        beside = []
        for c in range(2):
            if z + 1 < depth:
                z_up = f[c * depth + z + 1]
            else:
                z_up = jnp.where(bottom, zhi[c], 0.0) if pair else zhi[c]
            if z > 0:
                z_dn = f[c * depth + z - 1]
            else:
                z_dn = jnp.where(bottom, 0.0, zlo[c]) if pair else zlo[c]
            y_up, y_dn, x_up, x_dn = _rolls(cur[c])
            total = z_up + z_dn
            total = total + y_up + y_dn
            beside.append(total + x_up + x_dn)
        k = masks[z // MB] * mat[z]
        s0 = prof[z] * w[0]
        s1 = prof[z] * w[1]
        real_res = s0 - (diagonal * cur[0] - k * cur[1] - beside[0])
        imag_res = s1 - (diagonal * cur[1] + k * cur[0] - beside[1])
        scaled = factor / (diagonal * diagonal + k * k)
        n0 = jnp.where(keep, cur[0] + scaled * (diagonal * real_res + k * imag_res), 0.0)
        n1 = jnp.where(keep, cur[1] + scaled * (diagonal * imag_res - k * real_res), 0.0)
        if last:
            heat[z] = HEATING * k * (n0 * n0 + n1 * n1)
            own[0, z] = n0[0:height, 0:breadth]
            own[1, z] = n1[0:height, 0:breadth]
        else:
            o[z] = n0
            o[depth + z] = n1
            if z == 0:
                oz0[0] = n0
                oz0[1] = n1
            if z == depth - 1 and pair:
                oz0[0] = jnp.where(bottom, n0, oz0[0])
                oz0[1] = jnp.where(bottom, n1, oz0[1])
            elif z == depth - 1:
                oz1[0] = n0
                oz1[1] = n1


def _heat_kernel(last, pair, depth, totals, pos, fl, t, q, tzlo, tzhi, *outs):
    if last:
        (own,) = outs
    elif pair:
        (o, oz0) = outs
        oz1 = None
    else:
        (o, oz0, oz1) = outs
    bottom = pos[0] == 0
    height, breadth, x_first_block = totals
    rows, lanes = t.shape[1], t.shape[2]
    sy, sx = _selectors(pos, rows, lanes, height, breadth, x_first_block)
    zb_total = fl.shape[0]
    below = pos[0] - 1
    above = pos[0] + depth // MB
    m_below = _cells(fl, jnp.maximum(below, 0), sy, sx) * jnp.where(below >= 0, 1.0, 0.0)
    m_above = _cells(fl, jnp.minimum(above, zb_total - 1), sy, sx) * jnp.where(
        above < zb_total, 1.0, 0.0)
    m_own = [_cells(fl, pos[0] + zo, sy, sx) for zo in range(depth // MB)]
    planes = [m_below] + [m_own[z // MB] for z in range(depth)] + [m_above]
    if pair:
        below_t = jnp.where(bottom, 0.0, tzlo[...])
        above_t = jnp.where(bottom, tzhi[...], 0.0)
    else:
        below_t, above_t = tzlo[...], tzhi[...]
    temps = [below_t] + [t[z] for z in range(depth)] + [above_t]
    kaps = [1.0 / (1.0 + SOFTEN * v * v) for v in temps]
    for z in range(depth):
        c = temps[z + 1]
        centre_kappa = kaps[z + 1]
        y_up, y_dn, x_up, x_dn = _rolls(c)
        ky_up, ky_dn, kx_up, kx_dn = _rolls(centre_kappa)
        mc = planes[z + 1]
        my_up, my_dn, mx_up, mx_dn = _rolls(mc)
        flux = jnp.zeros_like(c)
        for other, kappa, other_mask in (
            (temps[z + 2], kaps[z + 2], planes[z + 2]), (temps[z], kaps[z], planes[z]),
            (y_up, ky_up, my_up), (y_dn, ky_dn, my_dn), (x_up, kx_up, mx_up), (x_dn, kx_dn, mx_dn),
        ):
            flux = flux + other_mask * (centre_kappa + kappa) * (other - c)
        new = c + 0.5 * CONDUCT * mc * flux + q[z]
        if last:
            own[z] = new[0:height, 0:breadth]
        else:
            o[z] = new
            if z == 0:
                oz0[...] = new
            if z == depth - 1 and pair:
                oz0[...] = jnp.where(bottom, new, oz0[...])
            elif z == depth - 1:
                oz1[...] = new


def _vmem_call(kernel, out_shape, n_in, n_smem=0):
    specs = [pl.BlockSpec(memory_space=pltpu.SMEM)] * n_smem
    specs += [pl.BlockSpec(memory_space=pltpu.VMEM)] * (n_in - n_smem)
    return pl.pallas_call(
        kernel,
        out_shape=out_shape,
        in_specs=specs,
        out_specs=[pl.BlockSpec(memory_space=pltpu.VMEM)] * len(out_shape),
    )


def _line_pairs(n, first=0):
    up = [(i, i + 1) for i in range(first, n - 1)]
    down = [(j, i) for i, j in up]
    return up, down


def _broadcast_blocks(own, me, n, first):
    if (n, first) == (4, 1):
        r1 = lax.ppermute(own, "gx", [(2, 0), (3, 1), (1, 2)])
        a = jnp.where((me == 0) | (me == 2), r1, own)
        b = jnp.where((me == 1) | (me == 0), r1, own)
        r2 = lax.ppermute(jnp.stack([a, b]), "gx", [(0, 1), (1, 0), (2, 3), (3, 2)])
        b1 = jnp.where(me == 1, own, jnp.where(me == 2, r1, r2[0]))
        b2 = jnp.where(me == 0, r1, jnp.where(me == 1, r2[0], jnp.where(me == 2, own, r2[1])))
        b3 = jnp.where(me == 0, r2[1], jnp.where(me == 1, r1, jnp.where(me == 2, r2[0], own)))
        return jnp.concatenate([b1, b2, b3], axis=2)
    owners = list(range(first, n))
    held = [own]
    for s in range(1, n):
        held.append(lax.ppermute(own, "gx", [(k, (k + s) % n) for k in owners]))
    held = jnp.stack(held)
    pieces = [lax.dynamic_index_in_dim(held, (me - k) % n, 0, keepdims=False) for k in owners]
    return jnp.concatenate(pieces, axis=2)


def on_device(
    earlier_window_curl_state,
    material_resistivity_inverse,
    winding_current_pattern,
    winding_axial_centre,
    specimen_presence_flags,
    specimen_kelvin_values,
):
    depth, height, breadth = material_resistivity_inverse.shape
    n_gz, n_gy, n_gx = lax.axis_size("gz"), lax.axis_size("gy"), lax.axis_size("gx")
    z_total, y_total, x_total = depth * n_gz, height * n_gy, breadth * n_gx
    gz_i, gy_i, gx_i = lax.axis_index("gz"), lax.axis_index("gy"), lax.axis_index("gx")
    z_start, y_start, x_start = gz_i * depth, gy_i * height, gx_i * breadth
    rows = height + 2 * H
    lanes = -(-(breadth + 2 * H) // 128) * 128
    gap = lanes - breadth - 2 * H
    specimen_columns = specimen_kelvin_values.shape[2]
    offset = x_total - specimen_columns
    assert offset % breadth == 0 and depth % MB == 0 and height % MB == 0 and breadth % MB == 0
    first_owner = offset // breadth

    coil_width = z_total // 4
    axial = (
        (z_start + jnp.arange(depth)).astype(jnp.float32)
        - winding_axial_centre[0].astype(jnp.float32)
    ) / coil_width
    profile = 1.0 / (1.0 + axial * axial)

    stack = jnp.concatenate(
        [earlier_window_curl_state.reshape(2 * depth, height, breadth), material_resistivity_inverse,
         winding_current_pattern], axis=0)
    up_x, down_x = _line_pairs(n_gx)
    from_left = lax.ppermute(jnp.swapaxes(stack[:, :, breadth - H:], 1, 2), "gx", up_x)
    from_right = lax.ppermute(jnp.swapaxes(stack[:, :, :H], 1, 2), "gx", down_x)
    nch = stack.shape[0]
    xext = jnp.concatenate(
        [stack, jnp.swapaxes(from_right, 1, 2), jnp.zeros((nch, height, gap), jnp.float32),
         jnp.swapaxes(from_left, 1, 2)], axis=2)

    j_start = x_start - offset
    kpad = jnp.pad(specimen_kelvin_values, ((0, 0), (0, 0), (H, H)))
    t_body = lax.dynamic_slice_in_dim(kpad, j_start + H, breadth + H, 2)
    t_tail = lax.dynamic_slice_in_dim(kpad, j_start, H, 2)
    t_x = jnp.concatenate([t_body, jnp.zeros((depth, height, gap), jnp.float32), t_tail], axis=2)

    ystack = jnp.concatenate([xext, t_x], axis=0)
    up_y, down_y = _line_pairs(n_gy)
    from_above = lax.ppermute(ystack[:, height - H:, :], "gy", up_y)
    from_below = lax.ppermute(ystack[:, :H, :], "gy", down_y)
    pieces = (ystack, from_below, from_above)

    def planes_of(idx):
        if isinstance(idx, int):
            return jnp.concatenate([p[idx] for p in pieces], axis=0)
        return jnp.stack([planes_of(i) for i in idx])

    fb = specimen_presence_flags.shape
    flags = jnp.pad(specimen_presence_flags.astype(jnp.float32),
                    ((0, 0), (0, 128 - fb[1]), (0, 128 - fb[2])))
    pos = jnp.stack([z_start // MB, y_start // MB, x_start // MB]).astype(jnp.int32)

    up_z, down_z = _line_pairs(n_gz)
    fshape = jax.ShapeDtypeStruct((2 * depth, rows, lanes), jnp.float32)
    plane2 = jax.ShapeDtypeStruct((2, rows, lanes), jnp.float32)
    qshape = jax.ShapeDtypeStruct((depth, rows, lanes), jnp.float32)
    oshape = jax.ShapeDtypeStruct((2, depth, height, breadth), jnp.float32)
    tshape = jax.ShapeDtypeStruct((depth, rows, lanes), jnp.float32)
    tplane = jax.ShapeDtypeStruct((rows, lanes), jnp.float32)
    town = jax.ShapeDtypeStruct((depth, height, breadth), jnp.float32)
    em_totals = (height, breadth, y_total, x_total)
    t_totals = (height, breadth, offset // MB)
    lo_idx = jnp.array([0, depth])
    hi_idx = jnp.array([depth - 1, 2 * depth - 1])
    pair = n_gz == 2
    both = [(0, 1), (1, 0)]
    if pair:
        top = gz_i == 0
        first = jnp.where(top, planes_of([depth - 1, 2 * depth - 1, 3 * depth + 2 + depth - 1]),
                          planes_of([0, depth, 3 * depth + 2]))
        got = lax.ppermute(first, "gz", both)
    else:
        lo_plane, hi_plane = planes_of([0, depth]), planes_of([depth - 1, 2 * depth - 1])
        tzlo0 = lax.ppermute(planes_of(3 * depth + 2 + depth - 1), "gz", up_z)
        tzhi0 = lax.ppermute(planes_of(3 * depth + 2), "gz", down_z)
    for i, factor in enumerate(WEIGHTS):
        last = i == len(WEIGHTS) - 1
        if pair:
            zlo = zhi = got if i == 0 else lax.ppermute(send, "gz", both)
        else:
            zlo = lax.ppermute(hi_plane, "gz", up_z)
            zhi = lax.ppermute(lo_plane, "gz", down_z)
        if last:
            outs = (qshape, oshape, tshape, tplane) if pair else (
                qshape, oshape, tshape, tplane, tplane)

            def fused(pos_r, prof_r, fl_r, f_r, ys_r, yb_r, ya_r, zlo_r, zhi_r, *rest,
                      factor=factor):
                mat_r = _Rows(ys_r, yb_r, ya_r, 2 * depth, depth)
                w_r = _Rows(ys_r, yb_r, ya_r, 3 * depth, 2)
                t_r = _Rows(ys_r, yb_r, ya_r, 3 * depth + 2, depth)
                if pair:
                    tzlo_r = tzhi_r = rest[0].at[2]
                    outs_r = rest[1:]
                else:
                    tzlo_r, tzhi_r = rest[0], rest[1]
                    outs_r = rest[2:]
                q_r, own_r = outs_r[0], outs_r[1]
                _em_kernel(factor, True, pair, depth, em_totals, pos_r, prof_r, fl_r, f_r, mat_r,
                           w_r, zlo_r, zhi_r, q_r, own_r)
                _heat_kernel(False, pair, depth, t_totals, pos_r, fl_r, t_r, q_r, tzlo_r, tzhi_r,
                             *outs_r[2:])

            extra = (got,) if pair else (tzlo0, tzhi0)
            res = _vmem_call(fused, outs, 9 + len(extra), 2)(
                pos, profile, flags, field, *pieces, zlo, zhi, *extra)
            heat, field_out, kelvin = res[0], res[1], res[2]
            if pair:
                send_t = res[3]
            else:
                lo_t, hi_t = res[3], res[4]
        else:
            outs = (fshape, plane2) if pair else (fshape, plane2, plane2)
            def sweep(pos_r, prof_r, fl_r, *rest, factor=factor, i=i):
                if i == 0:
                    ys_r, yb_r, ya_r = rest[:3]
                    f_r = _Rows(ys_r, yb_r, ya_r, 0, 2 * depth)
                    rest = rest[3:]
                else:
                    f_r, ys_r, yb_r, ya_r = rest[:4]
                    rest = rest[4:]
                mat_r = _Rows(ys_r, yb_r, ya_r, 2 * depth, depth)
                w_r = _Rows(ys_r, yb_r, ya_r, 3 * depth, 2)
                _em_kernel(factor, False, pair, depth, em_totals, pos_r, prof_r, fl_r, f_r, mat_r,
                           w_r, *rest)

            fargs = () if i == 0 else (field,)
            res = _vmem_call(sweep, outs, 8 + len(fargs), 2)(
                pos, profile, flags, *fargs, *pieces, zlo, zhi)
            if pair:
                field, send = res
            else:
                field, lo_plane, hi_plane = res

    for number in range(1, STEPS):
        last = number == STEPS - 1
        if pair:
            tzlo = tzhi = lax.ppermute(send_t, "gz", both)
        else:
            tzlo = lax.ppermute(hi_t, "gz", up_z)
            tzhi = lax.ppermute(lo_t, "gz", down_z)
        outs = (town,) if last else (tshape, tplane) if pair else (tshape, tplane, tplane)
        res = _vmem_call(
            lambda *r, last=last: _heat_kernel(last, pair, depth, t_totals, *r), outs, 6, 1
        )(pos, flags, kelvin, heat, tzlo, tzhi)
        if last:
            (own_t,) = res
        elif pair:
            kelvin, send_t = res
        else:
            kelvin, lo_t, hi_t = res

    segment_kelvin = _broadcast_blocks(own_t, gx_i, n_gx, first_owner)
    return (field_out, segment_kelvin)


def solution(mesh):
    placed = (
        P(None, "gz", "gy", "gx"),
        P("gz", "gy", "gx"),
        P(None, "gy", "gx"),
        P(),
        P(),
        P("gz", "gy", None),
    )
    return jax.shard_map(
        on_device,
        mesh=mesh,
        in_specs=placed,
        out_specs=(P(None, "gz", "gy", "gx"), P("gz", "gy", None)),
        check_vma=False,
    )
```

```python
import jax
import jax.numpy as jnp
from jax import lax
from jax.experimental import pallas as pl
from jax.experimental.pallas import tpu as pltpu
from jax.sharding import PartitionSpec as P

MB = 8
STEPS = 4


WEIGHTS = (0.8, 1.0, 1.25)
SHIFT = 0.2
HEATING = 0.02
CONDUCT = 0.16
SOFTEN = 0.25

H = MB


class _Rows:
    def __init__(self, main, after, before, base, count):
        self.parts, self.base = (main, after, before), base
        self.shape = (count, main.shape[1] + after.shape[1] + before.shape[1], main.shape[2])

    def __getitem__(self, i):
        return jnp.concatenate([p[self.base + i] for p in self.parts], axis=0)


def _rolls(a):
    rows, lanes = a.shape
    return (
        pltpu.roll(a, rows - 1, 0), pltpu.roll(a, 1, 0),
        pltpu.roll(a, lanes - 1, 1), pltpu.roll(a, 1, 1),
    )


def _selectors(pos, rows, lanes, height, breadth, x_first_block):
    shift = MB.bit_length() - 1
    r = lax.shift_right_logical(lax.broadcasted_iota(jnp.int32, (rows, 128), 0), shift)
    b = lax.broadcasted_iota(jnp.int32, (rows, 128), 1)
    ty = pos[1] + jnp.where(r < (height + H) // MB, r, r - rows // MB)
    sy = (b == ty).astype(jnp.float32)
    l = lax.shift_right_logical(lax.broadcasted_iota(jnp.int32, (lanes, 128), 0), shift)
    bx = lax.broadcasted_iota(jnp.int32, (lanes, 128), 1)
    far = jnp.where(l >= (lanes - H) // MB, l - lanes // MB, -(10 ** 6))
    tx = pos[2] + jnp.where(l < (breadth + H) // MB, l, far)
    sx = ((bx == tx) & (bx >= x_first_block)).astype(jnp.float32)
    return sy, sx


def _cells(fl, zb, sy, sx):
    a = jnp.dot(sy, fl[zb], preferred_element_type=jnp.float32)
    return lax.dot_general(a, sx, (((1,), (1,)), ((), ())), preferred_element_type=jnp.float32)


def _inside(pos, rows, lanes, height, breadth, y_total, x_total):
    r = lax.broadcasted_iota(jnp.int32, (rows, lanes), 0)
    l = lax.broadcasted_iota(jnp.int32, (rows, lanes), 1)
    y = pos[1] * MB + jnp.where(r < height + H, r, r - rows)
    far = jnp.where(l >= lanes - H, l - lanes, -(10 ** 6))
    x = pos[2] * MB + jnp.where(l < breadth + H, l, far)
    return (y >= 0) & (y < y_total) & (x >= 0) & (x < x_total)


def _em_kernel(factor, last, pair, depth, totals, pos, prof, fl, f, mat, w, zlo, zhi, *outs):
    diagonal = 6.0 + SHIFT
    if last:
        (heat, own) = outs
    elif pair:
        (o, oz0) = outs
        oz1 = None
    else:
        (o, oz0, oz1) = outs
    bottom = pos[0] == 0
    height, breadth, y_total, x_total = totals
    rows, lanes = f.shape[1], f.shape[2]
    keep = _inside(pos, rows, lanes, height, breadth, y_total, x_total)
    sy, sx = _selectors(pos, rows, lanes, height, breadth, 0)
    masks = [_cells(fl, pos[0] + zo, sy, sx) for zo in range(depth // MB)]
    for z in range(depth):
        cur = [f[c * depth + z] for c in range(2)]
        beside = []
        for c in range(2):
            if z + 1 < depth:
                z_up = f[c * depth + z + 1]
            else:
                z_up = jnp.where(bottom, zhi[c], 0.0) if pair else zhi[c]
            if z > 0:
                z_dn = f[c * depth + z - 1]
            else:
                z_dn = jnp.where(bottom, 0.0, zlo[c]) if pair else zlo[c]
            y_up, y_dn, x_up, x_dn = _rolls(cur[c])
            total = z_up + z_dn
            total = total + y_up + y_dn
            beside.append(total + x_up + x_dn)
        k = masks[z // MB] * mat[z]
        s0 = prof[z] * w[0]
        s1 = prof[z] * w[1]
        real_res = s0 - (diagonal * cur[0] - k * cur[1] - beside[0])
        imag_res = s1 - (diagonal * cur[1] + k * cur[0] - beside[1])
        scaled = factor / (diagonal * diagonal + k * k)
        n0 = jnp.where(keep, cur[0] + scaled * (diagonal * real_res + k * imag_res), 0.0)
        n1 = jnp.where(keep, cur[1] + scaled * (diagonal * imag_res - k * real_res), 0.0)
        if last:
            heat[z] = HEATING * k * (n0 * n0 + n1 * n1)
            own[0, z] = n0[0:height, 0:breadth]
            own[1, z] = n1[0:height, 0:breadth]
        else:
            o[z] = n0
            o[depth + z] = n1
            if z == 0:
                oz0[0] = n0
                oz0[1] = n1
            if z == depth - 1 and pair:
                oz0[0] = jnp.where(bottom, n0, oz0[0])
                oz0[1] = jnp.where(bottom, n1, oz0[1])
            elif z == depth - 1:
                oz1[0] = n0
                oz1[1] = n1


def _heat_kernel(last, pair, depth, totals, pos, fl, t, q, tzlo, tzhi, *outs):
    if last:
        (own,) = outs
    elif pair:
        (o, oz0) = outs
        oz1 = None
    else:
        (o, oz0, oz1) = outs
    bottom = pos[0] == 0
    height, breadth, x_first_block = totals
    rows, lanes = t.shape[1], t.shape[2]
    sy, sx = _selectors(pos, rows, lanes, height, breadth, x_first_block)
    zb_total = fl.shape[0]
    below = pos[0] - 1
    above = pos[0] + depth // MB
    m_below = _cells(fl, jnp.maximum(below, 0), sy, sx) * jnp.where(below >= 0, 1.0, 0.0)
    m_above = _cells(fl, jnp.minimum(above, zb_total - 1), sy, sx) * jnp.where(
        above < zb_total, 1.0, 0.0)
    m_own = [_cells(fl, pos[0] + zo, sy, sx) for zo in range(depth // MB)]
    planes = [m_below] + [m_own[z // MB] for z in range(depth)] + [m_above]
    if pair:
        below_t = jnp.where(bottom, 0.0, tzlo[...])
        above_t = jnp.where(bottom, tzhi[...], 0.0)
    else:
        below_t, above_t = tzlo[...], tzhi[...]
    temps = [below_t] + [t[z] for z in range(depth)] + [above_t]
    kaps = [1.0 / (1.0 + SOFTEN * v * v) for v in temps]
    for z in range(depth):
        c = temps[z + 1]
        centre_kappa = kaps[z + 1]
        y_up, y_dn, x_up, x_dn = _rolls(c)
        ky_up, ky_dn, kx_up, kx_dn = _rolls(centre_kappa)
        mc = planes[z + 1]
        my_up, my_dn, mx_up, mx_dn = _rolls(mc)
        flux = jnp.zeros_like(c)
        for other, kappa, other_mask in (
            (temps[z + 2], kaps[z + 2], planes[z + 2]), (temps[z], kaps[z], planes[z]),
            (y_up, ky_up, my_up), (y_dn, ky_dn, my_dn), (x_up, kx_up, mx_up), (x_dn, kx_dn, mx_dn),
        ):
            flux = flux + other_mask * (centre_kappa + kappa) * (other - c)
        new = c + 0.5 * CONDUCT * mc * flux + q[z]
        if last:
            own[z] = new[0:height, 0:breadth]
        else:
            o[z] = new
            if z == 0:
                oz0[...] = new
            if z == depth - 1 and pair:
                oz0[...] = jnp.where(bottom, new, oz0[...])
            elif z == depth - 1:
                oz1[...] = new


def _vmem_call(kernel, out_shape, n_in, n_smem=0):
    specs = [pl.BlockSpec(memory_space=pltpu.SMEM)] * n_smem
    specs += [pl.BlockSpec(memory_space=pltpu.VMEM)] * (n_in - n_smem)
    return pl.pallas_call(
        kernel,
        out_shape=out_shape,
        in_specs=specs,
        out_specs=[pl.BlockSpec(memory_space=pltpu.VMEM)] * len(out_shape),
    )


def _line_pairs(n, first=0):
    up = [(i, i + 1) for i in range(first, n - 1)]
    down = [(j, i) for i, j in up]
    return up, down


def _broadcast_blocks(own, me, n, first):
    if (n, first) == (4, 1):
        r1 = lax.ppermute(own, "gx", [(2, 0), (3, 1), (1, 2)])
        a = jnp.where((me == 0) | (me == 2), r1, own)
        b = jnp.where((me == 1) | (me == 0), r1, own)
        r2 = lax.ppermute(jnp.stack([a, b]), "gx", [(0, 1), (1, 0), (2, 3), (3, 2)])
        b1 = jnp.where(me == 1, own, jnp.where(me == 2, r1, r2[0]))
        b2 = jnp.where(me == 0, r1, jnp.where(me == 1, r2[0], jnp.where(me == 2, own, r2[1])))
        b3 = jnp.where(me == 0, r2[1], jnp.where(me == 1, r1, jnp.where(me == 2, r2[0], own)))
        return jnp.concatenate([b1, b2, b3], axis=2)
    owners = list(range(first, n))
    held = [own]
    for s in range(1, n):
        held.append(lax.ppermute(own, "gx", [(k, (k + s) % n) for k in owners]))
    held = jnp.stack(held)
    pieces = [lax.dynamic_index_in_dim(held, (me - k) % n, 0, keepdims=False) for k in owners]
    return jnp.concatenate(pieces, axis=2)


def on_device(
    earlier_window_curl_state,
    material_resistivity_inverse,
    winding_current_pattern,
    winding_axial_centre,
    specimen_presence_flags,
    specimen_kelvin_values,
):
    depth, height, breadth = material_resistivity_inverse.shape
    n_gz, n_gy, n_gx = lax.axis_size("gz"), lax.axis_size("gy"), lax.axis_size("gx")
    z_total, y_total, x_total = depth * n_gz, height * n_gy, breadth * n_gx
    gz_i, gy_i, gx_i = lax.axis_index("gz"), lax.axis_index("gy"), lax.axis_index("gx")
    z_start, y_start, x_start = gz_i * depth, gy_i * height, gx_i * breadth
    rows = height + 2 * H
    lanes = -(-(breadth + 2 * H) // 128) * 128
    gap = lanes - breadth - 2 * H
    specimen_columns = specimen_kelvin_values.shape[2]
    offset = x_total - specimen_columns
    assert offset % breadth == 0 and depth % MB == 0 and height % MB == 0 and breadth % MB == 0
    first_owner = offset // breadth

    coil_width = z_total // 4
    axial = (
        (z_start + jnp.arange(depth)).astype(jnp.float32)
        - winding_axial_centre[0].astype(jnp.float32)
    ) / coil_width
    profile = 1.0 / (1.0 + axial * axial)

    stack = jnp.concatenate(
        [earlier_window_curl_state.reshape(2 * depth, height, breadth), material_resistivity_inverse,
         winding_current_pattern], axis=0)
    up_x, down_x = _line_pairs(n_gx)
    from_left = lax.ppermute(jnp.swapaxes(stack[:, :, breadth - H:], 1, 2), "gx", up_x)
    from_right = lax.ppermute(jnp.swapaxes(stack[:, :, :H], 1, 2), "gx", down_x)
    nch = stack.shape[0]
    xext = jnp.concatenate(
        [stack, jnp.swapaxes(from_right, 1, 2), jnp.zeros((nch, height, gap), jnp.float32),
         jnp.swapaxes(from_left, 1, 2)], axis=2)

    j_start = x_start - offset
    kpad = jnp.pad(specimen_kelvin_values, ((0, 0), (0, 0), (H, H)))
    t_body = lax.dynamic_slice_in_dim(kpad, j_start + H, breadth + H, 2)
    t_tail = lax.dynamic_slice_in_dim(kpad, j_start, H, 2)
    t_x = jnp.concatenate([t_body, jnp.zeros((depth, height, gap), jnp.float32), t_tail], axis=2)

    ystack = jnp.concatenate([xext, t_x], axis=0)
    up_y, down_y = _line_pairs(n_gy)
    from_above = lax.ppermute(ystack[:, height - H:, :], "gy", up_y)
    from_below = lax.ppermute(ystack[:, :H, :], "gy", down_y)
    pieces = (ystack, from_below, from_above)

    def planes_of(idx):
        return jnp.concatenate([p[idx] for p in pieces], axis=-2)

    fb = specimen_presence_flags.shape
    flags = jnp.pad(specimen_presence_flags.astype(jnp.float32),
                    ((0, 0), (0, 128 - fb[1]), (0, 128 - fb[2])))
    pos = jnp.stack([z_start // MB, y_start // MB, x_start // MB]).astype(jnp.int32)

    up_z, down_z = _line_pairs(n_gz)
    fshape = jax.ShapeDtypeStruct((2 * depth, rows, lanes), jnp.float32)
    plane2 = jax.ShapeDtypeStruct((2, rows, lanes), jnp.float32)
    qshape = jax.ShapeDtypeStruct((depth, rows, lanes), jnp.float32)
    oshape = jax.ShapeDtypeStruct((2, depth, height, breadth), jnp.float32)
    tshape = jax.ShapeDtypeStruct((depth, rows, lanes), jnp.float32)
    tplane = jax.ShapeDtypeStruct((rows, lanes), jnp.float32)
    town = jax.ShapeDtypeStruct((depth, height, breadth), jnp.float32)
    em_totals = (height, breadth, y_total, x_total)
    t_totals = (height, breadth, offset // MB)
    lo_idx = jnp.array([0, depth])
    hi_idx = jnp.array([depth - 1, 2 * depth - 1])
    pair = n_gz == 2
    both = [(0, 1), (1, 0)]
    if pair:
        top = gz_i == 0
        first = planes_of(jnp.where(
            top, jnp.array([depth - 1, 2 * depth - 1, 3 * depth + 2 + depth - 1]),
            jnp.array([0, depth, 3 * depth + 2])))
        got = lax.ppermute(first[:2], "gz", both)
        got_t = lax.ppermute(first[2:], "gz", both)
    else:
        lo_plane, hi_plane = planes_of(lo_idx), planes_of(hi_idx)
        tzlo0 = lax.ppermute(planes_of(3 * depth + 2 + depth - 1), "gz", up_z)
        tzhi0 = lax.ppermute(planes_of(3 * depth + 2), "gz", down_z)
    for i, factor in enumerate(WEIGHTS):
        last = i == len(WEIGHTS) - 1
        if pair:
            zlo = zhi = got if i == 0 else lax.ppermute(send, "gz", both)
        else:
            zlo = lax.ppermute(hi_plane, "gz", up_z)
            zhi = lax.ppermute(lo_plane, "gz", down_z)
        if last:
            outs = (qshape, oshape, tshape, tplane) if pair else (
                qshape, oshape, tshape, tplane, tplane)

            def fused(pos_r, prof_r, fl_r, f_r, ys_r, yb_r, ya_r, zlo_r, zhi_r, *rest,
                      factor=factor):
                mat_r = _Rows(ys_r, yb_r, ya_r, 2 * depth, depth)
                w_r = _Rows(ys_r, yb_r, ya_r, 3 * depth, 2)
                t_r = _Rows(ys_r, yb_r, ya_r, 3 * depth + 2, depth)
                if pair:
                    tzlo_r = tzhi_r = rest[0].at[0]
                    outs_r = rest[1:]
                else:
                    tzlo_r, tzhi_r = rest[0], rest[1]
                    outs_r = rest[2:]
                q_r, own_r = outs_r[0], outs_r[1]
                _em_kernel(factor, True, pair, depth, em_totals, pos_r, prof_r, fl_r, f_r, mat_r,
                           w_r, zlo_r, zhi_r, q_r, own_r)
                _heat_kernel(False, pair, depth, t_totals, pos_r, fl_r, t_r, q_r, tzlo_r, tzhi_r,
                             *outs_r[2:])

            extra = (got_t,) if pair else (tzlo0, tzhi0)
            res = _vmem_call(fused, outs, 9 + len(extra), 2)(
                pos, profile, flags, field, *pieces, zlo, zhi, *extra)
            heat, field_out, kelvin = res[0], res[1], res[2]
            if pair:
                send_t = res[3]
            else:
                lo_t, hi_t = res[3], res[4]
        else:
            outs = (fshape, plane2) if pair else (fshape, plane2, plane2)
            def sweep(pos_r, prof_r, fl_r, *rest, factor=factor, i=i):
                if i == 0:
                    ys_r, yb_r, ya_r = rest[:3]
                    f_r = _Rows(ys_r, yb_r, ya_r, 0, 2 * depth)
                    rest = rest[3:]
                else:
                    f_r, ys_r, yb_r, ya_r = rest[:4]
                    rest = rest[4:]
                mat_r = _Rows(ys_r, yb_r, ya_r, 2 * depth, depth)
                w_r = _Rows(ys_r, yb_r, ya_r, 3 * depth, 2)
                _em_kernel(factor, False, pair, depth, em_totals, pos_r, prof_r, fl_r, f_r, mat_r,
                           w_r, *rest)

            fargs = () if i == 0 else (field,)
            res = _vmem_call(sweep, outs, 8 + len(fargs), 2)(
                pos, profile, flags, *fargs, *pieces, zlo, zhi)
            if pair:
                field, send = res
            else:
                field, lo_plane, hi_plane = res

    for number in range(1, STEPS):
        last = number == STEPS - 1
        if pair:
            tzlo = tzhi = lax.ppermute(send_t, "gz", both)
        else:
            tzlo = lax.ppermute(hi_t, "gz", up_z)
            tzhi = lax.ppermute(lo_t, "gz", down_z)
        outs = (town,) if last else (tshape, tplane) if pair else (tshape, tplane, tplane)
        res = _vmem_call(
            lambda *r, last=last: _heat_kernel(last, pair, depth, t_totals, *r), outs, 6, 1
        )(pos, flags, kelvin, heat, tzlo, tzhi)
        if last:
            (own_t,) = res
        elif pair:
            kelvin, send_t = res
        else:
            kelvin, lo_t, hi_t = res

    segment_kelvin = _broadcast_blocks(own_t, gx_i, n_gx, first_owner)
    return (field_out, segment_kelvin)


def solution(mesh):
    placed = (
        P(None, "gz", "gy", "gx"),
        P("gz", "gy", "gx"),
        P(None, "gy", "gx"),
        P(),
        P(),
        P("gz", "gy", None),
    )
    return jax.shard_map(
        on_device,
        mesh=mesh,
        in_specs=placed,
        out_specs=(P(None, "gz", "gy", "gx"), P("gz", "gy", None)),
        check_vma=False,
    )
```

```python
import jax
import jax.numpy as jnp
from jax import lax
from jax.experimental import pallas as pl
from jax.experimental.pallas import tpu as pltpu
from jax.sharding import PartitionSpec as P

MB = 8
STEPS = 4


WEIGHTS = (0.8, 1.0, 1.25)
SHIFT = 0.2
HEATING = 0.02
CONDUCT = 0.16
SOFTEN = 0.25

H = MB


class _Rows:
    def __init__(self, main, after, before, base, count):
        self.parts, self.base = (main, after, before), base
        self.shape = (count, main.shape[1] + after.shape[1] + before.shape[1], main.shape[2])

    def __getitem__(self, i):
        return jnp.concatenate([p[self.base + i] for p in self.parts], axis=0)


def _rolls(a):
    rows, lanes = a.shape
    return (
        pltpu.roll(a, rows - 1, 0), pltpu.roll(a, 1, 0),
        pltpu.roll(a, lanes - 1, 1), pltpu.roll(a, 1, 1),
    )


def _selectors(pos, rows, lanes, height, breadth, x_first_block):
    shift = MB.bit_length() - 1
    r = lax.shift_right_logical(lax.broadcasted_iota(jnp.int32, (rows, 128), 0), shift)
    b = lax.broadcasted_iota(jnp.int32, (rows, 128), 1)
    ty = pos[1] + jnp.where(r < (height + H) // MB, r, r - rows // MB)
    sy = (b == ty).astype(jnp.float32)
    l = lax.shift_right_logical(lax.broadcasted_iota(jnp.int32, (lanes, 128), 0), shift)
    bx = lax.broadcasted_iota(jnp.int32, (lanes, 128), 1)
    far = jnp.where(l >= (lanes - H) // MB, l - lanes // MB, -(10 ** 6))
    tx = pos[2] + jnp.where(l < (breadth + H) // MB, l, far)
    sx = ((bx == tx) & (bx >= x_first_block)).astype(jnp.float32)
    return sy, sx


def _cells(fl, zb, sy, sx):
    a = jnp.dot(sy, fl[zb], preferred_element_type=jnp.float32)
    return lax.dot_general(a, sx, (((1,), (1,)), ((), ())), preferred_element_type=jnp.float32)


def _inside(pos, rows, lanes, height, breadth, y_total, x_total):
    r = lax.broadcasted_iota(jnp.int32, (rows, lanes), 0)
    l = lax.broadcasted_iota(jnp.int32, (rows, lanes), 1)
    y = pos[1] * MB + jnp.where(r < height + H, r, r - rows)
    far = jnp.where(l >= lanes - H, l - lanes, -(10 ** 6))
    x = pos[2] * MB + jnp.where(l < breadth + H, l, far)
    return (y >= 0) & (y < y_total) & (x >= 0) & (x < x_total)


def _em_kernel(factor, last, pair, depth, totals, pos, prof, fl, f, mat, w, zlo, zhi, *outs):
    diagonal = 6.0 + SHIFT
    if last:
        (heat, own) = outs
    elif pair:
        (o, oz0) = outs
        oz1 = None
    else:
        (o, oz0, oz1) = outs
    bottom = pos[0] == 0
    height, breadth, y_total, x_total = totals
    rows, lanes = f.shape[1], f.shape[2]
    keep = _inside(pos, rows, lanes, height, breadth, y_total, x_total)
    sy, sx = _selectors(pos, rows, lanes, height, breadth, 0)
    masks = [_cells(fl, pos[0] + zo, sy, sx) for zo in range(depth // MB)]
    for z in range(depth):
        cur = [f[c * depth + z] for c in range(2)]
        beside = []
        for c in range(2):
            if z + 1 < depth:
                z_up = f[c * depth + z + 1]
            else:
                z_up = jnp.where(bottom, zhi[c], 0.0) if pair else zhi[c]
            if z > 0:
                z_dn = f[c * depth + z - 1]
            else:
                z_dn = jnp.where(bottom, 0.0, zlo[c]) if pair else zlo[c]
            y_up, y_dn, x_up, x_dn = _rolls(cur[c])
            total = z_up + z_dn
            total = total + y_up + y_dn
            beside.append(total + x_up + x_dn)
        k = masks[z // MB] * mat[z]
        s0 = prof[z] * w[0]
        s1 = prof[z] * w[1]
        real_res = s0 - (diagonal * cur[0] - k * cur[1] - beside[0])
        imag_res = s1 - (diagonal * cur[1] + k * cur[0] - beside[1])
        scaled = factor / (diagonal * diagonal + k * k)
        n0 = jnp.where(keep, cur[0] + scaled * (diagonal * real_res + k * imag_res), 0.0)
        n1 = jnp.where(keep, cur[1] + scaled * (diagonal * imag_res - k * real_res), 0.0)
        if last:
            heat[z] = HEATING * k * (n0 * n0 + n1 * n1)
            own[0, z] = n0[0:height, 0:breadth]
            own[1, z] = n1[0:height, 0:breadth]
        else:
            o[z] = n0
            o[depth + z] = n1
            if z == 0:
                oz0[0] = n0
                oz0[1] = n1
            if z == depth - 1 and pair:
                oz0[0] = jnp.where(bottom, n0, oz0[0])
                oz0[1] = jnp.where(bottom, n1, oz0[1])
            elif z == depth - 1:
                oz1[0] = n0
                oz1[1] = n1


def _heat_kernel(last, pair, depth, totals, pos, fl, t, q, tzlo, tzhi, *outs):
    if last:
        (own,) = outs
    elif pair:
        (o, oz0) = outs
        oz1 = None
    else:
        (o, oz0, oz1) = outs
    bottom = pos[0] == 0
    height, breadth, x_first_block = totals
    rows, lanes = t.shape[1], t.shape[2]
    sy, sx = _selectors(pos, rows, lanes, height, breadth, x_first_block)
    zb_total = fl.shape[0]
    below = pos[0] - 1
    above = pos[0] + depth // MB
    m_below = _cells(fl, jnp.maximum(below, 0), sy, sx) * jnp.where(below >= 0, 1.0, 0.0)
    m_above = _cells(fl, jnp.minimum(above, zb_total - 1), sy, sx) * jnp.where(
        above < zb_total, 1.0, 0.0)
    m_own = [_cells(fl, pos[0] + zo, sy, sx) for zo in range(depth // MB)]
    planes = [m_below] + [m_own[z // MB] for z in range(depth)] + [m_above]
    if pair:
        below_t = jnp.where(bottom, 0.0, tzlo[...])
        above_t = jnp.where(bottom, tzhi[...], 0.0)
    else:
        below_t, above_t = tzlo[...], tzhi[...]
    temps = [below_t] + [t[z] for z in range(depth)] + [above_t]
    kaps = [1.0 / (1.0 + SOFTEN * v * v) for v in temps]
    for z in range(depth):
        c = temps[z + 1]
        centre_kappa = kaps[z + 1]
        y_up, y_dn, x_up, x_dn = _rolls(c)
        ky_up, ky_dn, kx_up, kx_dn = _rolls(centre_kappa)
        mc = planes[z + 1]
        my_up, my_dn, mx_up, mx_dn = _rolls(mc)
        cut = (lambda v: v[0:height, 0:breadth]) if last else (lambda v: v)
        c, centre_kappa, mc = cut(c), cut(centre_kappa), cut(mc)
        flux = jnp.zeros_like(c)
        for other, kappa, other_mask in (
            (temps[z + 2], kaps[z + 2], planes[z + 2]), (temps[z], kaps[z], planes[z]),
            (y_up, ky_up, my_up), (y_dn, ky_dn, my_dn), (x_up, kx_up, mx_up), (x_dn, kx_dn, mx_dn),
        ):
            flux = flux + cut(other_mask) * (centre_kappa + cut(kappa)) * (cut(other) - c)
        new = c + 0.5 * CONDUCT * mc * flux + cut(q[z])
        if last:
            own[z] = new
        else:
            o[z] = new
            if z == 0:
                oz0[...] = new
            if z == depth - 1 and pair:
                oz0[...] = jnp.where(bottom, new, oz0[...])
            elif z == depth - 1:
                oz1[...] = new


def _vmem_call(kernel, out_shape, n_in, n_smem=0):
    specs = [pl.BlockSpec(memory_space=pltpu.SMEM)] * n_smem
    specs += [pl.BlockSpec(memory_space=pltpu.VMEM)] * (n_in - n_smem)
    return pl.pallas_call(
        kernel,
        out_shape=out_shape,
        in_specs=specs,
        out_specs=[pl.BlockSpec(memory_space=pltpu.VMEM)] * len(out_shape),
    )


def _line_pairs(n, first=0):
    up = [(i, i + 1) for i in range(first, n - 1)]
    down = [(j, i) for i, j in up]
    return up, down


def _broadcast_blocks(own, me, n, first):
    if (n, first) == (4, 1):
        r1 = lax.ppermute(own, "gx", [(2, 0), (3, 1), (1, 2)])
        a = jnp.where((me == 0) | (me == 2), r1, own)
        b = jnp.where((me == 1) | (me == 0), r1, own)
        r2 = lax.ppermute(jnp.stack([a, b]), "gx", [(0, 1), (1, 0), (2, 3), (3, 2)])
        b1 = jnp.where(me == 1, own, jnp.where(me == 2, r1, r2[0]))
        b2 = jnp.where(me == 0, r1, jnp.where(me == 1, r2[0], jnp.where(me == 2, own, r2[1])))
        b3 = jnp.where(me == 0, r2[1], jnp.where(me == 1, r1, jnp.where(me == 2, r2[0], own)))
        return jnp.concatenate([b1, b2, b3], axis=2)
    owners = list(range(first, n))
    held = [own]
    for s in range(1, n):
        held.append(lax.ppermute(own, "gx", [(k, (k + s) % n) for k in owners]))
    held = jnp.stack(held)
    pieces = [lax.dynamic_index_in_dim(held, (me - k) % n, 0, keepdims=False) for k in owners]
    return jnp.concatenate(pieces, axis=2)


def on_device(
    earlier_window_curl_state,
    material_resistivity_inverse,
    winding_current_pattern,
    winding_axial_centre,
    specimen_presence_flags,
    specimen_kelvin_values,
):
    depth, height, breadth = material_resistivity_inverse.shape
    n_gz, n_gy, n_gx = lax.axis_size("gz"), lax.axis_size("gy"), lax.axis_size("gx")
    z_total, y_total, x_total = depth * n_gz, height * n_gy, breadth * n_gx
    gz_i, gy_i, gx_i = lax.axis_index("gz"), lax.axis_index("gy"), lax.axis_index("gx")
    z_start, y_start, x_start = gz_i * depth, gy_i * height, gx_i * breadth
    rows = height + 2 * H
    lanes = -(-(breadth + 2 * H) // 128) * 128
    gap = lanes - breadth - 2 * H
    specimen_columns = specimen_kelvin_values.shape[2]
    offset = x_total - specimen_columns
    assert offset % breadth == 0 and depth % MB == 0 and height % MB == 0 and breadth % MB == 0
    first_owner = offset // breadth

    coil_width = z_total // 4
    axial = (
        (z_start + jnp.arange(depth)).astype(jnp.float32)
        - winding_axial_centre[0].astype(jnp.float32)
    ) / coil_width
    profile = 1.0 / (1.0 + axial * axial)

    stack = jnp.concatenate(
        [earlier_window_curl_state.reshape(2 * depth, height, breadth), material_resistivity_inverse,
         winding_current_pattern], axis=0)
    up_x, down_x = _line_pairs(n_gx)
    from_left = lax.ppermute(jnp.swapaxes(stack[:, :, breadth - H:], 1, 2), "gx", up_x)
    from_right = lax.ppermute(jnp.swapaxes(stack[:, :, :H], 1, 2), "gx", down_x)
    nch = stack.shape[0]
    xext = jnp.concatenate(
        [stack, jnp.swapaxes(from_right, 1, 2), jnp.zeros((nch, height, gap), jnp.float32),
         jnp.swapaxes(from_left, 1, 2)], axis=2)

    j_start = x_start - offset
    kpad = jnp.pad(specimen_kelvin_values, ((0, 0), (0, 0), (H, H)))
    t_body = lax.dynamic_slice_in_dim(kpad, j_start + H, breadth + H, 2)
    t_tail = lax.dynamic_slice_in_dim(kpad, j_start, H, 2)
    t_x = jnp.concatenate([t_body, jnp.zeros((depth, height, gap), jnp.float32), t_tail], axis=2)

    ystack = jnp.concatenate([xext, t_x], axis=0)
    up_y, down_y = _line_pairs(n_gy)
    from_above = lax.ppermute(ystack[:, height - H:, :], "gy", up_y)
    from_below = lax.ppermute(ystack[:, :H, :], "gy", down_y)
    pieces = (ystack, from_below, from_above)

    def planes_of(idx):
        return jnp.concatenate([p[idx] for p in pieces], axis=-2)

    fb = specimen_presence_flags.shape
    flags = jnp.pad(specimen_presence_flags.astype(jnp.float32),
                    ((0, 0), (0, 128 - fb[1]), (0, 128 - fb[2])))
    pos = jnp.stack([z_start // MB, y_start // MB, x_start // MB]).astype(jnp.int32)

    up_z, down_z = _line_pairs(n_gz)
    fshape = jax.ShapeDtypeStruct((2 * depth, rows, lanes), jnp.float32)
    plane2 = jax.ShapeDtypeStruct((2, rows, lanes), jnp.float32)
    qshape = jax.ShapeDtypeStruct((depth, rows, lanes), jnp.float32)
    oshape = jax.ShapeDtypeStruct((2, depth, height, breadth), jnp.float32)
    tshape = jax.ShapeDtypeStruct((depth, rows, lanes), jnp.float32)
    tplane = jax.ShapeDtypeStruct((rows, lanes), jnp.float32)
    town = jax.ShapeDtypeStruct((depth, height, breadth), jnp.float32)
    em_totals = (height, breadth, y_total, x_total)
    t_totals = (height, breadth, offset // MB)
    lo_idx = jnp.array([0, depth])
    hi_idx = jnp.array([depth - 1, 2 * depth - 1])
    pair = n_gz == 2
    both = [(0, 1), (1, 0)]
    if pair:
        top = gz_i == 0
        first = planes_of(jnp.where(
            top, jnp.array([depth - 1, 2 * depth - 1, 3 * depth + 2 + depth - 1]),
            jnp.array([0, depth, 3 * depth + 2])))
        got = lax.ppermute(first[:2], "gz", both)
        got_t = lax.ppermute(first[2:], "gz", both)
    else:
        lo_plane, hi_plane = planes_of(lo_idx), planes_of(hi_idx)
        tzlo0 = lax.ppermute(planes_of(3 * depth + 2 + depth - 1), "gz", up_z)
        tzhi0 = lax.ppermute(planes_of(3 * depth + 2), "gz", down_z)
    for i, factor in enumerate(WEIGHTS):
        last = i == len(WEIGHTS) - 1
        if pair:
            zlo = zhi = got if i == 0 else lax.ppermute(send, "gz", both)
        else:
            zlo = lax.ppermute(hi_plane, "gz", up_z)
            zhi = lax.ppermute(lo_plane, "gz", down_z)
        if last:
            outs = (qshape, oshape, tshape, tplane) if pair else (
                qshape, oshape, tshape, tplane, tplane)

            def fused(pos_r, prof_r, fl_r, f_r, ys_r, yb_r, ya_r, zlo_r, zhi_r, *rest,
                      factor=factor):
                mat_r = _Rows(ys_r, yb_r, ya_r, 2 * depth, depth)
                w_r = _Rows(ys_r, yb_r, ya_r, 3 * depth, 2)
                t_r = _Rows(ys_r, yb_r, ya_r, 3 * depth + 2, depth)
                if pair:
                    tzlo_r = tzhi_r = rest[0].at[0]
                    outs_r = rest[1:]
                else:
                    tzlo_r, tzhi_r = rest[0], rest[1]
                    outs_r = rest[2:]
                q_r, own_r = outs_r[0], outs_r[1]
                _em_kernel(factor, True, pair, depth, em_totals, pos_r, prof_r, fl_r, f_r, mat_r,
                           w_r, zlo_r, zhi_r, q_r, own_r)
                _heat_kernel(False, pair, depth, t_totals, pos_r, fl_r, t_r, q_r, tzlo_r, tzhi_r,
                             *outs_r[2:])

            extra = (got_t,) if pair else (tzlo0, tzhi0)
            res = _vmem_call(fused, outs, 9 + len(extra), 2)(
                pos, profile, flags, field, *pieces, zlo, zhi, *extra)
            heat, field_out, kelvin = res[0], res[1], res[2]
            if pair:
                send_t = res[3]
            else:
                lo_t, hi_t = res[3], res[4]
        else:
            outs = (fshape, plane2) if pair else (fshape, plane2, plane2)
            def sweep(pos_r, prof_r, fl_r, *rest, factor=factor, i=i):
                if i == 0:
                    ys_r, yb_r, ya_r = rest[:3]
                    f_r = _Rows(ys_r, yb_r, ya_r, 0, 2 * depth)
                    rest = rest[3:]
                else:
                    f_r, ys_r, yb_r, ya_r = rest[:4]
                    rest = rest[4:]
                mat_r = _Rows(ys_r, yb_r, ya_r, 2 * depth, depth)
                w_r = _Rows(ys_r, yb_r, ya_r, 3 * depth, 2)
                _em_kernel(factor, False, pair, depth, em_totals, pos_r, prof_r, fl_r, f_r, mat_r,
                           w_r, *rest)

            fargs = () if i == 0 else (field,)
            res = _vmem_call(sweep, outs, 8 + len(fargs), 2)(
                pos, profile, flags, *fargs, *pieces, zlo, zhi)
            if pair:
                field, send = res
            else:
                field, lo_plane, hi_plane = res

    for number in range(1, STEPS):
        last = number == STEPS - 1
        if pair:
            tzlo = tzhi = lax.ppermute(send_t, "gz", both)
        else:
            tzlo = lax.ppermute(hi_t, "gz", up_z)
            tzhi = lax.ppermute(lo_t, "gz", down_z)
        outs = (town,) if last else (tshape, tplane) if pair else (tshape, tplane, tplane)
        res = _vmem_call(
            lambda *r, last=last: _heat_kernel(last, pair, depth, t_totals, *r), outs, 6, 1
        )(pos, flags, kelvin, heat, tzlo, tzhi)
        if last:
            (own_t,) = res
        elif pair:
            kelvin, send_t = res
        else:
            kelvin, lo_t, hi_t = res

    segment_kelvin = _broadcast_blocks(own_t, gx_i, n_gx, first_owner)
    return (field_out, segment_kelvin)


def solution(mesh):
    placed = (
        P(None, "gz", "gy", "gx"),
        P("gz", "gy", "gx"),
        P(None, "gy", "gx"),
        P(),
        P(),
        P("gz", "gy", None),
    )
    return jax.shard_map(
        on_device,
        mesh=mesh,
        in_specs=placed,
        out_specs=(P(None, "gz", "gy", "gx"), P("gz", "gy", None)),
        check_vma=False,
    )
```

```python
import jax
import jax.numpy as jnp
from jax import lax
from jax.experimental import pallas as pl
from jax.experimental.pallas import tpu as pltpu
from jax.sharding import PartitionSpec as P

MB = 8
STEPS = 4


WEIGHTS = (0.8, 1.0, 1.25)
SHIFT = 0.2
HEATING = 0.02
CONDUCT = 0.16
SOFTEN = 0.25

H = MB


class _Rows:
    def __init__(self, main, after, before, base, count):
        self.parts, self.base = (main, after, before), base
        self.shape = (count, main.shape[1] + after.shape[1] + before.shape[1], main.shape[2])

    def __getitem__(self, i):
        return jnp.concatenate([p[self.base + i] for p in self.parts], axis=0)


def _rolls(a):
    rows, lanes = a.shape
    return (
        pltpu.roll(a, rows - 1, 0), pltpu.roll(a, 1, 0),
        pltpu.roll(a, lanes - 1, 1), pltpu.roll(a, 1, 1),
    )


def _selectors(pos, rows, lanes, height, breadth, x_first_block):
    shift = MB.bit_length() - 1
    r = lax.shift_right_logical(lax.broadcasted_iota(jnp.int32, (rows, 128), 0), shift)
    b = lax.broadcasted_iota(jnp.int32, (rows, 128), 1)
    ty = pos[1] + jnp.where(r < (height + H) // MB, r, r - rows // MB)
    sy = (b == ty).astype(jnp.float32)
    l = lax.shift_right_logical(lax.broadcasted_iota(jnp.int32, (lanes, 128), 0), shift)
    bx = lax.broadcasted_iota(jnp.int32, (lanes, 128), 1)
    far = jnp.where(l >= (lanes - H) // MB, l - lanes // MB, -(10 ** 6))
    tx = pos[2] + jnp.where(l < (breadth + H) // MB, l, far)
    sx = ((bx == tx) & (bx >= x_first_block)).astype(jnp.float32)
    return sy, sx


def _cells(fl, zb, sy, sx):
    a = jnp.dot(sy, fl[zb], preferred_element_type=jnp.float32)
    return lax.dot_general(a, sx, (((1,), (1,)), ((), ())), preferred_element_type=jnp.float32)


def _inside(pos, rows, lanes, height, breadth, y_total, x_total):
    r = lax.broadcasted_iota(jnp.int32, (rows, lanes), 0)
    l = lax.broadcasted_iota(jnp.int32, (rows, lanes), 1)
    y = pos[1] * MB + jnp.where(r < height + H, r, r - rows)
    far = jnp.where(l >= lanes - H, l - lanes, -(10 ** 6))
    x = pos[2] * MB + jnp.where(l < breadth + H, l, far)
    return (y >= 0) & (y < y_total) & (x >= 0) & (x < x_total)


def _em_kernel(factor, last, pair, depth, totals, pos, prof, fl, f, mat, w, zlo, zhi, *outs):
    diagonal = 6.0 + SHIFT
    if last:
        (heat, own) = outs
    elif pair:
        (o, oz0) = outs
        oz1 = None
    else:
        (o, oz0, oz1) = outs
    bottom = pos[0] == 0
    height, breadth, y_total, x_total = totals
    rows, lanes = f.shape[1], f.shape[2]
    keep = _inside(pos, rows, lanes, height, breadth, y_total, x_total)
    sy, sx = _selectors(pos, rows, lanes, height, breadth, 0)
    masks = [_cells(fl, pos[0] + zo, sy, sx) for zo in range(depth // MB)]
    for z in range(depth):
        cur = [f[c * depth + z] for c in range(2)]
        beside = []
        for c in range(2):
            if z + 1 < depth:
                z_up = f[c * depth + z + 1]
            else:
                z_up = jnp.where(bottom, zhi[c], 0.0) if pair else zhi[c]
            if z > 0:
                z_dn = f[c * depth + z - 1]
            else:
                z_dn = jnp.where(bottom, 0.0, zlo[c]) if pair else zlo[c]
            y_up, y_dn, x_up, x_dn = _rolls(cur[c])
            total = z_up + z_dn
            total = total + y_up + y_dn
            beside.append(total + x_up + x_dn)
        k = masks[z // MB] * mat[z]
        s0 = prof[z] * w[0]
        s1 = prof[z] * w[1]
        real_res = s0 - (diagonal * cur[0] - k * cur[1] - beside[0])
        imag_res = s1 - (diagonal * cur[1] + k * cur[0] - beside[1])
        scaled = factor / (diagonal * diagonal + k * k)
        n0 = jnp.where(keep, cur[0] + scaled * (diagonal * real_res + k * imag_res), 0.0)
        n1 = jnp.where(keep, cur[1] + scaled * (diagonal * imag_res - k * real_res), 0.0)
        if last:
            heat[z] = HEATING * k * (n0 * n0 + n1 * n1)
            own[0, z] = n0[0:height, 0:breadth]
            own[1, z] = n1[0:height, 0:breadth]
        else:
            o[z] = n0
            o[depth + z] = n1
            if z == 0:
                oz0[0] = n0
                oz0[1] = n1
            if z == depth - 1 and pair:
                oz0[0] = jnp.where(bottom, n0, oz0[0])
                oz0[1] = jnp.where(bottom, n1, oz0[1])
            elif z == depth - 1:
                oz1[0] = n0
                oz1[1] = n1


def _heat_kernel(last, pair, depth, totals, pos, fl, t, q, tzlo, tzhi, *outs):
    if last:
        (own,) = outs
    elif pair:
        (o, oz0) = outs
        oz1 = None
    else:
        (o, oz0, oz1) = outs
    bottom = pos[0] == 0
    height, breadth, x_first_block = totals
    rows, lanes = t.shape[1], t.shape[2]
    sy, sx = _selectors(pos, rows, lanes, height, breadth, x_first_block)
    zb_total = fl.shape[0]
    below = pos[0] - 1
    above = pos[0] + depth // MB
    m_below = _cells(fl, jnp.maximum(below, 0), sy, sx) * jnp.where(below >= 0, 1.0, 0.0)
    m_above = _cells(fl, jnp.minimum(above, zb_total - 1), sy, sx) * jnp.where(
        above < zb_total, 1.0, 0.0)
    m_own = [_cells(fl, pos[0] + zo, sy, sx) for zo in range(depth // MB)]
    planes = [m_below] + [m_own[z // MB] for z in range(depth)] + [m_above]
    if pair:
        below_t = jnp.where(bottom, 0.0, tzlo[...])
        above_t = jnp.where(bottom, tzhi[...], 0.0)
    else:
        below_t, above_t = tzlo[...], tzhi[...]
    temps = [below_t] + [t[z] for z in range(depth)] + [above_t]
    kaps = [1.0 / (1.0 + SOFTEN * v * v) for v in temps]
    for z in range(depth):
        c = temps[z + 1]
        centre_kappa = kaps[z + 1]
        y_up, y_dn, x_up, x_dn = _rolls(c)
        ky_up, ky_dn, kx_up, kx_dn = _rolls(centre_kappa)
        mc = planes[z + 1]
        my_up, my_dn, mx_up, mx_dn = _rolls(mc)
        flux = jnp.zeros_like(c)
        for other, kappa, other_mask in (
            (temps[z + 2], kaps[z + 2], planes[z + 2]), (temps[z], kaps[z], planes[z]),
            (y_up, ky_up, my_up), (y_dn, ky_dn, my_dn), (x_up, kx_up, mx_up), (x_dn, kx_dn, mx_dn),
        ):
            flux = flux + other_mask * (centre_kappa + kappa) * (other - c)
        new = c + 0.5 * CONDUCT * mc * flux + q[z]
        if last:
            own[z] = new[0:height, 0:breadth]
        else:
            o[z] = new
            if z == 0:
                oz0[...] = new
            if z == depth - 1 and pair:
                oz0[...] = jnp.where(bottom, new, oz0[...])
            elif z == depth - 1:
                oz1[...] = new


def _vmem_call(kernel, out_shape, n_in, n_smem=0):
    specs = [pl.BlockSpec(memory_space=pltpu.SMEM)] * n_smem
    specs += [pl.BlockSpec(memory_space=pltpu.VMEM)] * (n_in - n_smem)
    return pl.pallas_call(
        kernel,
        out_shape=out_shape,
        in_specs=specs,
        out_specs=[pl.BlockSpec(memory_space=pltpu.VMEM)] * len(out_shape),
    )


def _line_pairs(n, first=0):
    up = [(i, i + 1) for i in range(first, n - 1)]
    down = [(j, i) for i, j in up]
    return up, down


def _broadcast_blocks(own, me, n, first):
    if (n, first) == (4, 1):
        r1 = lax.ppermute(own, "gx", [(2, 0), (3, 1), (1, 2)])
        a = jnp.where((me == 0) | (me == 2), r1, own)
        b = jnp.where((me == 1) | (me == 0), r1, own)
        r2 = lax.ppermute(jnp.stack([a, b]), "gx", [(0, 1), (1, 0), (2, 3), (3, 2)])
        b1 = jnp.where(me == 1, own, jnp.where(me == 2, r1, r2[0]))
        b2 = jnp.where(me == 0, r1, jnp.where(me == 1, r2[0], jnp.where(me == 2, own, r2[1])))
        b3 = jnp.where(me == 0, r2[1], jnp.where(me == 1, r1, jnp.where(me == 2, r2[0], own)))
        return jnp.concatenate([b1, b2, b3], axis=2)
    owners = list(range(first, n))
    held = [own]
    for s in range(1, n):
        held.append(lax.ppermute(own, "gx", [(k, (k + s) % n) for k in owners]))
    held = jnp.stack(held)
    pieces = [lax.dynamic_index_in_dim(held, (me - k) % n, 0, keepdims=False) for k in owners]
    return jnp.concatenate(pieces, axis=2)


def on_device(
    earlier_window_curl_state,
    material_resistivity_inverse,
    winding_current_pattern,
    winding_axial_centre,
    specimen_presence_flags,
    specimen_kelvin_values,
):
    depth, height, breadth = material_resistivity_inverse.shape
    n_gz, n_gy, n_gx = lax.axis_size("gz"), lax.axis_size("gy"), lax.axis_size("gx")
    z_total, y_total, x_total = depth * n_gz, height * n_gy, breadth * n_gx
    gz_i, gy_i, gx_i = lax.axis_index("gz"), lax.axis_index("gy"), lax.axis_index("gx")
    z_start, y_start, x_start = gz_i * depth, gy_i * height, gx_i * breadth
    rows = height + 2 * H
    lanes = -(-(breadth + 2 * H) // 128) * 128
    gap = lanes - breadth - 2 * H
    specimen_columns = specimen_kelvin_values.shape[2]
    offset = x_total - specimen_columns
    assert offset % breadth == 0 and depth % MB == 0 and height % MB == 0 and breadth % MB == 0
    first_owner = offset // breadth

    coil_width = z_total // 4
    axial = (
        (z_start + jnp.arange(depth)).astype(jnp.float32)
        - winding_axial_centre[0].astype(jnp.float32)
    ) / coil_width
    profile = 1.0 / (1.0 + axial * axial)

    stack = jnp.concatenate(
        [earlier_window_curl_state.reshape(2 * depth, height, breadth), material_resistivity_inverse,
         winding_current_pattern], axis=0)
    up_x, down_x = _line_pairs(n_gx)
    from_left = lax.ppermute(jnp.swapaxes(stack[:, :, breadth - H:], 1, 2), "gx", up_x)
    from_right = lax.ppermute(jnp.swapaxes(stack[:, :, :H], 1, 2), "gx", down_x)
    nch = stack.shape[0]
    xext = jnp.concatenate(
        [stack, jnp.swapaxes(from_right, 1, 2), jnp.zeros((nch, height, gap), jnp.float32),
         jnp.swapaxes(from_left, 1, 2)], axis=2)

    j_start = x_start - offset
    t_own = lax.dynamic_slice_in_dim(specimen_kelvin_values, j_start, breadth, 2)
    t_after = lax.dynamic_slice_in_dim(specimen_kelvin_values, j_start + breadth, H, 2)
    t_tail = lax.dynamic_slice_in_dim(specimen_kelvin_values, j_start - H, H, 2)
    t_x = jnp.concatenate(
        [t_own, t_after, jnp.zeros((depth, height, gap), jnp.float32), t_tail], axis=2)

    ystack = jnp.concatenate([xext, t_x], axis=0)
    up_y, down_y = _line_pairs(n_gy)
    from_above = lax.ppermute(ystack[:, height - H:, :], "gy", up_y)
    from_below = lax.ppermute(ystack[:, :H, :], "gy", down_y)
    pieces = (ystack, from_below, from_above)

    def planes_of(idx):
        return jnp.concatenate([p[idx] for p in pieces], axis=-2)

    fb = specimen_presence_flags.shape
    flags = jnp.pad(specimen_presence_flags.astype(jnp.float32),
                    ((0, 0), (0, 128 - fb[1]), (0, 128 - fb[2])))
    pos = jnp.stack([z_start // MB, y_start // MB, x_start // MB]).astype(jnp.int32)

    up_z, down_z = _line_pairs(n_gz)
    fshape = jax.ShapeDtypeStruct((2 * depth, rows, lanes), jnp.float32)
    plane2 = jax.ShapeDtypeStruct((2, rows, lanes), jnp.float32)
    qshape = jax.ShapeDtypeStruct((depth, rows, lanes), jnp.float32)
    oshape = jax.ShapeDtypeStruct((2, depth, height, breadth), jnp.float32)
    tshape = jax.ShapeDtypeStruct((depth, rows, lanes), jnp.float32)
    tplane = jax.ShapeDtypeStruct((rows, lanes), jnp.float32)
    town = jax.ShapeDtypeStruct((depth, height, breadth), jnp.float32)
    em_totals = (height, breadth, y_total, x_total)
    t_totals = (height, breadth, offset // MB)
    lo_idx = jnp.array([0, depth])
    hi_idx = jnp.array([depth - 1, 2 * depth - 1])
    pair = n_gz == 2
    both = [(0, 1), (1, 0)]
    if pair:
        top = gz_i == 0
        first = planes_of(jnp.where(
            top, jnp.array([depth - 1, 2 * depth - 1, 3 * depth + 2 + depth - 1]),
            jnp.array([0, depth, 3 * depth + 2])))
        got = lax.ppermute(first[:2], "gz", both)
        got_t = lax.ppermute(first[2:], "gz", both)
    else:
        lo_plane, hi_plane = planes_of(lo_idx), planes_of(hi_idx)
        tzlo0 = lax.ppermute(planes_of(3 * depth + 2 + depth - 1), "gz", up_z)
        tzhi0 = lax.ppermute(planes_of(3 * depth + 2), "gz", down_z)
    for i, factor in enumerate(WEIGHTS):
        last = i == len(WEIGHTS) - 1
        if pair:
            zlo = zhi = got if i == 0 else lax.ppermute(send, "gz", both)
        else:
            zlo = lax.ppermute(hi_plane, "gz", up_z)
            zhi = lax.ppermute(lo_plane, "gz", down_z)
        if last:
            outs = (qshape, oshape, tshape, tplane) if pair else (
                qshape, oshape, tshape, tplane, tplane)

            def fused(pos_r, prof_r, fl_r, f_r, ys_r, yb_r, ya_r, zlo_r, zhi_r, *rest,
                      factor=factor):
                mat_r = _Rows(ys_r, yb_r, ya_r, 2 * depth, depth)
                w_r = _Rows(ys_r, yb_r, ya_r, 3 * depth, 2)
                t_r = _Rows(ys_r, yb_r, ya_r, 3 * depth + 2, depth)
                if pair:
                    tzlo_r = tzhi_r = rest[0].at[0]
                    outs_r = rest[1:]
                else:
                    tzlo_r, tzhi_r = rest[0], rest[1]
                    outs_r = rest[2:]
                q_r, own_r = outs_r[0], outs_r[1]
                _em_kernel(factor, True, pair, depth, em_totals, pos_r, prof_r, fl_r, f_r, mat_r,
                           w_r, zlo_r, zhi_r, q_r, own_r)
                _heat_kernel(False, pair, depth, t_totals, pos_r, fl_r, t_r, q_r, tzlo_r, tzhi_r,
                             *outs_r[2:])

            extra = (got_t,) if pair else (tzlo0, tzhi0)
            res = _vmem_call(fused, outs, 9 + len(extra), 2)(
                pos, profile, flags, field, *pieces, zlo, zhi, *extra)
            heat, field_out, kelvin = res[0], res[1], res[2]
            if pair:
                send_t = res[3]
            else:
                lo_t, hi_t = res[3], res[4]
        else:
            outs = (fshape, plane2) if pair else (fshape, plane2, plane2)
            def sweep(pos_r, prof_r, fl_r, *rest, factor=factor, i=i):
                if i == 0:
                    ys_r, yb_r, ya_r = rest[:3]
                    f_r = _Rows(ys_r, yb_r, ya_r, 0, 2 * depth)
                    rest = rest[3:]
                else:
                    f_r, ys_r, yb_r, ya_r = rest[:4]
                    rest = rest[4:]
                mat_r = _Rows(ys_r, yb_r, ya_r, 2 * depth, depth)
                w_r = _Rows(ys_r, yb_r, ya_r, 3 * depth, 2)
                _em_kernel(factor, False, pair, depth, em_totals, pos_r, prof_r, fl_r, f_r, mat_r,
                           w_r, *rest)

            fargs = () if i == 0 else (field,)
            res = _vmem_call(sweep, outs, 8 + len(fargs), 2)(
                pos, profile, flags, *fargs, *pieces, zlo, zhi)
            if pair:
                field, send = res
            else:
                field, lo_plane, hi_plane = res

    for number in range(1, STEPS):
        last = number == STEPS - 1
        if pair:
            tzlo = tzhi = lax.ppermute(send_t, "gz", both)
        else:
            tzlo = lax.ppermute(hi_t, "gz", up_z)
            tzhi = lax.ppermute(lo_t, "gz", down_z)
        outs = (town,) if last else (tshape, tplane) if pair else (tshape, tplane, tplane)
        res = _vmem_call(
            lambda *r, last=last: _heat_kernel(last, pair, depth, t_totals, *r), outs, 6, 1
        )(pos, flags, kelvin, heat, tzlo, tzhi)
        if last:
            (own_t,) = res
        elif pair:
            kelvin, send_t = res
        else:
            kelvin, lo_t, hi_t = res

    segment_kelvin = _broadcast_blocks(own_t, gx_i, n_gx, first_owner)
    return (field_out, segment_kelvin)


def solution(mesh):
    placed = (
        P(None, "gz", "gy", "gx"),
        P("gz", "gy", "gx"),
        P(None, "gy", "gx"),
        P(),
        P(),
        P("gz", "gy", None),
    )
    return jax.shard_map(
        on_device,
        mesh=mesh,
        in_specs=placed,
        out_specs=(P(None, "gz", "gy", "gx"), P("gz", "gy", None)),
        check_vma=False,
    )
```

```python
import jax
import jax.numpy as jnp
from jax import lax
from jax.experimental import pallas as pl
from jax.experimental.pallas import tpu as pltpu
from jax.sharding import PartitionSpec as P

MB = 8
STEPS = 4


WEIGHTS = (0.8, 1.0, 1.25)
SHIFT = 0.2
HEATING = 0.02
CONDUCT = 0.16
SOFTEN = 0.25

H = MB


class _Rows:
    def __init__(self, main, after, before, base, count):
        self.parts, self.base = (main, after, before), base
        self.shape = (count, main.shape[1] + after.shape[1] + before.shape[1], main.shape[2])

    def __getitem__(self, i):
        return jnp.concatenate([p[self.base + i] for p in self.parts], axis=0)


def _rolls(a):
    rows, lanes = a.shape
    return (
        pltpu.roll(a, rows - 1, 0), pltpu.roll(a, 1, 0),
        pltpu.roll(a, lanes - 1, 1), pltpu.roll(a, 1, 1),
    )


def _selectors(pos, rows, lanes, height, breadth, x_first_block):
    shift = MB.bit_length() - 1
    r = lax.shift_right_logical(lax.broadcasted_iota(jnp.int32, (rows, 128), 0), shift)
    b = lax.broadcasted_iota(jnp.int32, (rows, 128), 1)
    ty = pos[1] + jnp.where(r < (height + H) // MB, r, r - rows // MB)
    sy = (b == ty).astype(jnp.float32)
    l = lax.shift_right_logical(lax.broadcasted_iota(jnp.int32, (lanes, 128), 0), shift)
    bx = lax.broadcasted_iota(jnp.int32, (lanes, 128), 1)
    far = jnp.where(l >= (lanes - H) // MB, l - lanes // MB, -(10 ** 6))
    tx = pos[2] + jnp.where(l < (breadth + H) // MB, l, far)
    sx = ((bx == tx) & (bx >= x_first_block)).astype(jnp.float32)
    return sy, sx


def _cells(fl, zb, sy, sx):
    a = jnp.dot(sy, fl[zb], preferred_element_type=jnp.float32)
    return lax.dot_general(a, sx, (((1,), (1,)), ((), ())), preferred_element_type=jnp.float32)


def _inside(pos, rows, lanes, height, breadth, y_total, x_total):
    r = lax.broadcasted_iota(jnp.int32, (rows, lanes), 0)
    l = lax.broadcasted_iota(jnp.int32, (rows, lanes), 1)
    y = pos[1] * MB + jnp.where(r < height + H, r, r - rows)
    far = jnp.where(l >= lanes - H, l - lanes, -(10 ** 6))
    x = pos[2] * MB + jnp.where(l < breadth + H, l, far)
    return (y >= 0) & (y < y_total) & (x >= 0) & (x < x_total)


def _em_kernel(factor, last, pair, depth, totals, pos, prof, fl, f, mat, w, zlo, zhi, *outs):
    diagonal = 6.0 + SHIFT
    if last:
        (heat, own) = outs
    elif pair:
        (o, oz0) = outs
        oz1 = None
    else:
        (o, oz0, oz1) = outs
    bottom = pos[0] == 0
    height, breadth, y_total, x_total = totals
    rows, lanes = f.shape[1], f.shape[2]
    keep = _inside(pos, rows, lanes, height, breadth, y_total, x_total)
    sy, sx = _selectors(pos, rows, lanes, height, breadth, 0)
    masks = [_cells(fl, pos[0] + zo, sy, sx) for zo in range(depth // MB)]
    for z in range(depth):
        cur = [f[c * depth + z] for c in range(2)]
        beside = []
        for c in range(2):
            if z + 1 < depth:
                z_up = f[c * depth + z + 1]
            else:
                z_up = jnp.where(bottom, zhi[c], 0.0) if pair else zhi[c]
            if z > 0:
                z_dn = f[c * depth + z - 1]
            else:
                z_dn = jnp.where(bottom, 0.0, zlo[c]) if pair else zlo[c]
            y_up, y_dn, x_up, x_dn = _rolls(cur[c])
            total = z_up + z_dn
            total = total + y_up + y_dn
            beside.append(total + x_up + x_dn)
        k = masks[z // MB] * mat[z]
        s0 = prof[z] * w[0]
        s1 = prof[z] * w[1]
        real_res = s0 - (diagonal * cur[0] - k * cur[1] - beside[0])
        imag_res = s1 - (diagonal * cur[1] + k * cur[0] - beside[1])
        scaled = factor / (diagonal * diagonal + k * k)
        n0 = jnp.where(keep, cur[0] + scaled * (diagonal * real_res + k * imag_res), 0.0)
        n1 = jnp.where(keep, cur[1] + scaled * (diagonal * imag_res - k * real_res), 0.0)
        if last:
            heat[z] = HEATING * k * (n0 * n0 + n1 * n1)
            own[0, z] = n0[0:height, 0:breadth]
            own[1, z] = n1[0:height, 0:breadth]
        else:
            o[z] = n0
            o[depth + z] = n1
            if z == 0:
                oz0[0] = n0
                oz0[1] = n1
            if z == depth - 1 and pair:
                oz0[0] = jnp.where(bottom, n0, oz0[0])
                oz0[1] = jnp.where(bottom, n1, oz0[1])
            elif z == depth - 1:
                oz1[0] = n0
                oz1[1] = n1


def _heat_kernel(last, pair, depth, totals, pos, fl, t, q, tzlo, tzhi, *outs):
    if last:
        (own,) = outs
    elif pair:
        (o, oz0) = outs
        oz1 = None
    else:
        (o, oz0, oz1) = outs
    bottom = pos[0] == 0
    height, breadth, x_first_block = totals
    rows, lanes = t.shape[1], t.shape[2]
    sy, sx = _selectors(pos, rows, lanes, height, breadth, x_first_block)
    zb_total = fl.shape[0]
    below = pos[0] - 1
    above = pos[0] + depth // MB
    m_below = _cells(fl, jnp.maximum(below, 0), sy, sx) * jnp.where(below >= 0, 1.0, 0.0)
    m_above = _cells(fl, jnp.minimum(above, zb_total - 1), sy, sx) * jnp.where(
        above < zb_total, 1.0, 0.0)
    m_own = [_cells(fl, pos[0] + zo, sy, sx) for zo in range(depth // MB)]
    planes = [m_below] + [m_own[z // MB] for z in range(depth)] + [m_above]
    if pair:
        below_t = jnp.where(bottom, 0.0, tzlo[...])
        above_t = jnp.where(bottom, tzhi[...], 0.0)
    else:
        below_t, above_t = tzlo[...], tzhi[...]
    temps = [below_t] + [t[z] for z in range(depth)] + [above_t]
    kaps = [1.0 / (1.0 + SOFTEN * v * v) for v in temps]
    for z in range(depth):
        c = temps[z + 1]
        centre_kappa = kaps[z + 1]
        y_up, y_dn, x_up, x_dn = _rolls(c)
        ky_up, ky_dn, kx_up, kx_dn = _rolls(centre_kappa)
        mc = planes[z + 1]
        my_up, my_dn, mx_up, mx_dn = _rolls(mc)
        flux = jnp.zeros_like(c)
        for other, kappa, other_mask in (
            (temps[z + 2], kaps[z + 2], planes[z + 2]), (temps[z], kaps[z], planes[z]),
            (y_up, ky_up, my_up), (y_dn, ky_dn, my_dn), (x_up, kx_up, mx_up), (x_dn, kx_dn, mx_dn),
        ):
            flux = flux + other_mask * (centre_kappa + kappa) * (other - c)
        new = c + 0.5 * CONDUCT * mc * flux + q[z]
        if last:
            own[z] = new[0:height, 0:breadth]
        else:
            o[z] = new
            if z == 0:
                oz0[...] = new
            if z == depth - 1 and pair:
                oz0[...] = jnp.where(bottom, new, oz0[...])
            elif z == depth - 1:
                oz1[...] = new


def _vmem_call(kernel, out_shape, n_in, n_smem=0):
    specs = [pl.BlockSpec(memory_space=pltpu.SMEM)] * n_smem
    specs += [pl.BlockSpec(memory_space=pltpu.VMEM)] * (n_in - n_smem)
    return pl.pallas_call(
        kernel,
        out_shape=out_shape,
        in_specs=specs,
        out_specs=[pl.BlockSpec(memory_space=pltpu.VMEM)] * len(out_shape),
    )


def _line_pairs(n, first=0):
    up = [(i, i + 1) for i in range(first, n - 1)]
    down = [(j, i) for i, j in up]
    return up, down


def _broadcast_blocks(own, me, n, first):
    if (n, first) == (4, 1):
        r1 = lax.ppermute(own, "gx", [(2, 0), (3, 1), (1, 2)])
        r2 = lax.ppermute(jnp.stack([own, r1]), "gx", [(0, 1), (1, 0), (2, 3), (3, 2)])
        b1 = jnp.where(me == 1, own, jnp.where(me == 2, r1, jnp.where(me == 0, r2[0], r2[1])))
        b2 = jnp.where(me == 0, r1, jnp.where(me == 1, r2[1], jnp.where(me == 2, own, r2[0])))
        b3 = jnp.where(me == 0, r2[1], jnp.where(me == 1, r1, jnp.where(me == 2, r2[0], own)))
        return jnp.concatenate([b1, b2, b3], axis=2)
    owners = list(range(first, n))
    held = [own]
    for s in range(1, n):
        held.append(lax.ppermute(own, "gx", [(k, (k + s) % n) for k in owners]))
    held = jnp.stack(held)
    pieces = [lax.dynamic_index_in_dim(held, (me - k) % n, 0, keepdims=False) for k in owners]
    return jnp.concatenate(pieces, axis=2)


def on_device(
    earlier_window_curl_state,
    material_resistivity_inverse,
    winding_current_pattern,
    winding_axial_centre,
    specimen_presence_flags,
    specimen_kelvin_values,
):
    depth, height, breadth = material_resistivity_inverse.shape
    n_gz, n_gy, n_gx = lax.axis_size("gz"), lax.axis_size("gy"), lax.axis_size("gx")
    z_total, y_total, x_total = depth * n_gz, height * n_gy, breadth * n_gx
    gz_i, gy_i, gx_i = lax.axis_index("gz"), lax.axis_index("gy"), lax.axis_index("gx")
    z_start, y_start, x_start = gz_i * depth, gy_i * height, gx_i * breadth
    rows = height + 2 * H
    lanes = -(-(breadth + 2 * H) // 128) * 128
    gap = lanes - breadth - 2 * H
    specimen_columns = specimen_kelvin_values.shape[2]
    offset = x_total - specimen_columns
    assert offset % breadth == 0 and depth % MB == 0 and height % MB == 0 and breadth % MB == 0
    first_owner = offset // breadth

    coil_width = z_total // 4
    axial = (
        (z_start + jnp.arange(depth)).astype(jnp.float32)
        - winding_axial_centre[0].astype(jnp.float32)
    ) / coil_width
    profile = 1.0 / (1.0 + axial * axial)

    stack = jnp.concatenate(
        [earlier_window_curl_state.reshape(2 * depth, height, breadth), material_resistivity_inverse,
         winding_current_pattern], axis=0)
    up_x, down_x = _line_pairs(n_gx)
    from_left = lax.ppermute(jnp.swapaxes(stack[:, :, breadth - H:], 1, 2), "gx", up_x)
    from_right = lax.ppermute(jnp.swapaxes(stack[:, :, :H], 1, 2), "gx", down_x)
    nch = stack.shape[0]
    xext = jnp.concatenate(
        [stack, jnp.swapaxes(from_right, 1, 2), jnp.zeros((nch, height, gap), jnp.float32),
         jnp.swapaxes(from_left, 1, 2)], axis=2)

    j_start = x_start - offset
    kpad = jnp.pad(specimen_kelvin_values, ((0, 0), (0, 0), (H, H)))
    t_body = lax.dynamic_slice_in_dim(kpad, j_start + H, breadth + H, 2)
    t_tail = lax.dynamic_slice_in_dim(kpad, j_start, H, 2)
    t_x = jnp.concatenate([t_body, jnp.zeros((depth, height, gap), jnp.float32), t_tail], axis=2)

    ystack = jnp.concatenate([xext, t_x], axis=0)
    up_y, down_y = _line_pairs(n_gy)
    from_above = lax.ppermute(ystack[:, height - H:, :], "gy", up_y)
    from_below = lax.ppermute(ystack[:, :H, :], "gy", down_y)
    pieces = (ystack, from_below, from_above)

    def planes_of(idx):
        return jnp.concatenate([p[idx] for p in pieces], axis=-2)

    fb = specimen_presence_flags.shape
    flags = jnp.pad(specimen_presence_flags.astype(jnp.float32),
                    ((0, 0), (0, 128 - fb[1]), (0, 128 - fb[2])))
    pos = jnp.stack([z_start // MB, y_start // MB, x_start // MB]).astype(jnp.int32)

    up_z, down_z = _line_pairs(n_gz)
    fshape = jax.ShapeDtypeStruct((2 * depth, rows, lanes), jnp.float32)
    plane2 = jax.ShapeDtypeStruct((2, rows, lanes), jnp.float32)
    qshape = jax.ShapeDtypeStruct((depth, rows, lanes), jnp.float32)
    oshape = jax.ShapeDtypeStruct((2, depth, height, breadth), jnp.float32)
    tshape = jax.ShapeDtypeStruct((depth, rows, lanes), jnp.float32)
    tplane = jax.ShapeDtypeStruct((rows, lanes), jnp.float32)
    town = jax.ShapeDtypeStruct((depth, height, breadth), jnp.float32)
    em_totals = (height, breadth, y_total, x_total)
    t_totals = (height, breadth, offset // MB)
    lo_idx = jnp.array([0, depth])
    hi_idx = jnp.array([depth - 1, 2 * depth - 1])
    pair = n_gz == 2
    both = [(0, 1), (1, 0)]
    if pair:
        top = gz_i == 0
        first = planes_of(jnp.where(
            top, jnp.array([depth - 1, 2 * depth - 1, 3 * depth + 2 + depth - 1]),
            jnp.array([0, depth, 3 * depth + 2])))
        got = lax.ppermute(first[:2], "gz", both)
        got_t = lax.ppermute(first[2:], "gz", both)
    else:
        lo_plane, hi_plane = planes_of(lo_idx), planes_of(hi_idx)
        tzlo0 = lax.ppermute(planes_of(3 * depth + 2 + depth - 1), "gz", up_z)
        tzhi0 = lax.ppermute(planes_of(3 * depth + 2), "gz", down_z)
    for i, factor in enumerate(WEIGHTS):
        last = i == len(WEIGHTS) - 1
        if pair:
            zlo = zhi = got if i == 0 else lax.ppermute(send, "gz", both)
        else:
            zlo = lax.ppermute(hi_plane, "gz", up_z)
            zhi = lax.ppermute(lo_plane, "gz", down_z)
        if last:
            outs = (qshape, oshape, tshape, tplane) if pair else (
                qshape, oshape, tshape, tplane, tplane)

            def fused(pos_r, prof_r, fl_r, f_r, ys_r, yb_r, ya_r, zlo_r, zhi_r, *rest,
                      factor=factor):
                mat_r = _Rows(ys_r, yb_r, ya_r, 2 * depth, depth)
                w_r = _Rows(ys_r, yb_r, ya_r, 3 * depth, 2)
                t_r = _Rows(ys_r, yb_r, ya_r, 3 * depth + 2, depth)
                if pair:
                    tzlo_r = tzhi_r = rest[0].at[0]
                    outs_r = rest[1:]
                else:
                    tzlo_r, tzhi_r = rest[0], rest[1]
                    outs_r = rest[2:]
                q_r, own_r = outs_r[0], outs_r[1]
                _em_kernel(factor, True, pair, depth, em_totals, pos_r, prof_r, fl_r, f_r, mat_r,
                           w_r, zlo_r, zhi_r, q_r, own_r)
                _heat_kernel(False, pair, depth, t_totals, pos_r, fl_r, t_r, q_r, tzlo_r, tzhi_r,
                             *outs_r[2:])

            extra = (got_t,) if pair else (tzlo0, tzhi0)
            res = _vmem_call(fused, outs, 9 + len(extra), 2)(
                pos, profile, flags, field, *pieces, zlo, zhi, *extra)
            heat, field_out, kelvin = res[0], res[1], res[2]
            if pair:
                send_t = res[3]
            else:
                lo_t, hi_t = res[3], res[4]
        else:
            outs = (fshape, plane2) if pair else (fshape, plane2, plane2)
            def sweep(pos_r, prof_r, fl_r, *rest, factor=factor, i=i):
                if i == 0:
                    ys_r, yb_r, ya_r = rest[:3]
                    f_r = _Rows(ys_r, yb_r, ya_r, 0, 2 * depth)
                    rest = rest[3:]
                else:
                    f_r, ys_r, yb_r, ya_r = rest[:4]
                    rest = rest[4:]
                mat_r = _Rows(ys_r, yb_r, ya_r, 2 * depth, depth)
                w_r = _Rows(ys_r, yb_r, ya_r, 3 * depth, 2)
                _em_kernel(factor, False, pair, depth, em_totals, pos_r, prof_r, fl_r, f_r, mat_r,
                           w_r, *rest)

            fargs = () if i == 0 else (field,)
            res = _vmem_call(sweep, outs, 8 + len(fargs), 2)(
                pos, profile, flags, *fargs, *pieces, zlo, zhi)
            if pair:
                field, send = res
            else:
                field, lo_plane, hi_plane = res

    for number in range(1, STEPS):
        last = number == STEPS - 1
        if pair:
            tzlo = tzhi = lax.ppermute(send_t, "gz", both)
        else:
            tzlo = lax.ppermute(hi_t, "gz", up_z)
            tzhi = lax.ppermute(lo_t, "gz", down_z)
        outs = (town,) if last else (tshape, tplane) if pair else (tshape, tplane, tplane)
        res = _vmem_call(
            lambda *r, last=last: _heat_kernel(last, pair, depth, t_totals, *r), outs, 6, 1
        )(pos, flags, kelvin, heat, tzlo, tzhi)
        if last:
            (own_t,) = res
        elif pair:
            kelvin, send_t = res
        else:
            kelvin, lo_t, hi_t = res

    segment_kelvin = _broadcast_blocks(own_t, gx_i, n_gx, first_owner)
    return (field_out, segment_kelvin)


def solution(mesh):
    placed = (
        P(None, "gz", "gy", "gx"),
        P("gz", "gy", "gx"),
        P(None, "gy", "gx"),
        P(),
        P(),
        P("gz", "gy", None),
    )
    return jax.shard_map(
        on_device,
        mesh=mesh,
        in_specs=placed,
        out_specs=(P(None, "gz", "gy", "gx"), P("gz", "gy", None)),
        check_vma=False,
    )
```

```python
import jax
import jax.numpy as jnp
from jax import lax
from jax.experimental import pallas as pl
from jax.experimental.pallas import tpu as pltpu
from jax.sharding import PartitionSpec as P

MB = 8
STEPS = 4


WEIGHTS = (0.8, 1.0, 1.25)
SHIFT = 0.2
HEATING = 0.02
CONDUCT = 0.16
SOFTEN = 0.25

H = MB


class _Rows:
    def __init__(self, main, after, before, base, count):
        self.parts, self.base = (main, after, before), base
        self.shape = (count, main.shape[1] + after.shape[1] + before.shape[1], main.shape[2])

    def __getitem__(self, i):
        return jnp.concatenate([p[self.base + i] for p in self.parts], axis=0)


def _rolls(a):
    rows, lanes = a.shape
    return (
        pltpu.roll(a, rows - 1, 0), pltpu.roll(a, 1, 0),
        pltpu.roll(a, lanes - 1, 1), pltpu.roll(a, 1, 1),
    )


def _selectors(pos, rows, lanes, height, breadth, x_first_block):
    shift = MB.bit_length() - 1
    r = lax.shift_right_logical(lax.broadcasted_iota(jnp.int32, (rows, 128), 0), shift)
    b = lax.broadcasted_iota(jnp.int32, (rows, 128), 1)
    ty = pos[1] + jnp.where(r < (height + H) // MB, r, r - rows // MB)
    sy = (b == ty).astype(jnp.float32)
    l = lax.shift_right_logical(lax.broadcasted_iota(jnp.int32, (lanes, 128), 0), shift)
    bx = lax.broadcasted_iota(jnp.int32, (lanes, 128), 1)
    far = jnp.where(l >= (lanes - H) // MB, l - lanes // MB, -(10 ** 6))
    tx = pos[2] + jnp.where(l < (breadth + H) // MB, l, far)
    sx = ((bx == tx) & (bx >= x_first_block)).astype(jnp.float32)
    return sy, sx


def _cells(fl, zb, sy, sx):
    a = jnp.dot(sy, fl[zb], preferred_element_type=jnp.float32)
    return lax.dot_general(a, sx, (((1,), (1,)), ((), ())), preferred_element_type=jnp.float32)


def _inside(pos, rows, lanes, height, breadth, y_total, x_total):
    r = lax.broadcasted_iota(jnp.int32, (rows, lanes), 0)
    l = lax.broadcasted_iota(jnp.int32, (rows, lanes), 1)
    y = pos[1] * MB + jnp.where(r < height + H, r, r - rows)
    far = jnp.where(l >= lanes - H, l - lanes, -(10 ** 6))
    x = pos[2] * MB + jnp.where(l < breadth + H, l, far)
    return (y >= 0) & (y < y_total) & (x >= 0) & (x < x_total)


def _em_kernel(factor, last, pair, depth, totals, pos, prof, fl, f, mat, w, zlo, zhi, *outs):
    diagonal = 6.0 + SHIFT
    if last:
        (heat, own) = outs
    elif pair:
        (o, oz0) = outs
        oz1 = None
    else:
        (o, oz0, oz1) = outs
    bottom = pos[0] == 0
    height, breadth, y_total, x_total = totals
    rows, lanes = f.shape[1], f.shape[2]
    keep = _inside(pos, rows, lanes, height, breadth, y_total, x_total)
    sy, sx = _selectors(pos, rows, lanes, height, breadth, 0)
    masks = [_cells(fl, pos[0] + zo, sy, sx) for zo in range(depth // MB)]
    for z in range(depth):
        cur = [f[c * depth + z] for c in range(2)]
        beside = []
        for c in range(2):
            if z + 1 < depth:
                z_up = f[c * depth + z + 1]
            else:
                z_up = jnp.where(bottom, zhi[c], 0.0) if pair else zhi[c]
            if z > 0:
                z_dn = f[c * depth + z - 1]
            else:
                z_dn = jnp.where(bottom, 0.0, zlo[c]) if pair else zlo[c]
            y_up, y_dn, x_up, x_dn = _rolls(cur[c])
            total = z_up + z_dn
            total = total + y_up + y_dn
            beside.append(total + x_up + x_dn)
        k = masks[z // MB] * mat[z]
        s0 = prof[z] * w[0]
        s1 = prof[z] * w[1]
        real_res = s0 - (diagonal * cur[0] - k * cur[1] - beside[0])
        imag_res = s1 - (diagonal * cur[1] + k * cur[0] - beside[1])
        scaled = factor / (diagonal * diagonal + k * k)
        n0 = jnp.where(keep, cur[0] + scaled * (diagonal * real_res + k * imag_res), 0.0)
        n1 = jnp.where(keep, cur[1] + scaled * (diagonal * imag_res - k * real_res), 0.0)
        if last:
            heat[z] = HEATING * k * (n0 * n0 + n1 * n1)
            own[0, z] = n0[0:height, 0:breadth]
            own[1, z] = n1[0:height, 0:breadth]
        else:
            o[z] = n0
            o[depth + z] = n1
            if z == 0:
                oz0[0] = n0
                oz0[1] = n1
            if z == depth - 1 and pair:
                oz0[0] = jnp.where(bottom, n0, oz0[0])
                oz0[1] = jnp.where(bottom, n1, oz0[1])
            elif z == depth - 1:
                oz1[0] = n0
                oz1[1] = n1


def _heat_kernel(last, pair, depth, totals, pos, fl, t, q, tzlo, tzhi, *outs, masks_in=None,
                 masks_out=None):
    if last:
        (own,) = outs
    elif pair:
        (o, oz0) = outs
        oz1 = None
    else:
        (o, oz0, oz1) = outs
    bottom = pos[0] == 0
    height, breadth, x_first_block = totals
    rows, lanes = t.shape[1], t.shape[2]
    nb = depth // MB
    if masks_in is not None:
        m_below, m_above = masks_in[0], masks_in[nb + 1]
        m_own = [masks_in[1 + zo] for zo in range(nb)]
    else:
        sy, sx = _selectors(pos, rows, lanes, height, breadth, x_first_block)
        zb_total = fl.shape[0]
        below = pos[0] - 1
        above = pos[0] + nb
        m_below = _cells(fl, jnp.maximum(below, 0), sy, sx) * jnp.where(below >= 0, 1.0, 0.0)
        m_above = _cells(fl, jnp.minimum(above, zb_total - 1), sy, sx) * jnp.where(
            above < zb_total, 1.0, 0.0)
        m_own = [_cells(fl, pos[0] + zo, sy, sx) for zo in range(nb)]
        if masks_out is not None:
            for j, m in enumerate([m_below] + m_own + [m_above]):
                masks_out[j] = m
    planes = [m_below] + [m_own[z // MB] for z in range(depth)] + [m_above]
    if pair:
        below_t = jnp.where(bottom, 0.0, tzlo[...])
        above_t = jnp.where(bottom, tzhi[...], 0.0)
    else:
        below_t, above_t = tzlo[...], tzhi[...]
    temps = [below_t] + [t[z] for z in range(depth)] + [above_t]
    kaps = [1.0 / (1.0 + SOFTEN * v * v) for v in temps]
    for z in range(depth):
        c = temps[z + 1]
        centre_kappa = kaps[z + 1]
        y_up, y_dn, x_up, x_dn = _rolls(c)
        ky_up, ky_dn, kx_up, kx_dn = _rolls(centre_kappa)
        mc = planes[z + 1]
        my_up, my_dn, mx_up, mx_dn = _rolls(mc)
        flux = jnp.zeros_like(c)
        for other, kappa, other_mask in (
            (temps[z + 2], kaps[z + 2], planes[z + 2]), (temps[z], kaps[z], planes[z]),
            (y_up, ky_up, my_up), (y_dn, ky_dn, my_dn), (x_up, kx_up, mx_up), (x_dn, kx_dn, mx_dn),
        ):
            flux = flux + other_mask * (centre_kappa + kappa) * (other - c)
        new = c + 0.5 * CONDUCT * mc * flux + q[z]
        if last:
            own[z] = new[0:height, 0:breadth]
        else:
            o[z] = new
            if z == 0:
                oz0[...] = new
            if z == depth - 1 and pair:
                oz0[...] = jnp.where(bottom, new, oz0[...])
            elif z == depth - 1:
                oz1[...] = new


def _vmem_call(kernel, out_shape, n_in, n_smem=0):
    specs = [pl.BlockSpec(memory_space=pltpu.SMEM)] * n_smem
    specs += [pl.BlockSpec(memory_space=pltpu.VMEM)] * (n_in - n_smem)
    return pl.pallas_call(
        kernel,
        out_shape=out_shape,
        in_specs=specs,
        out_specs=[pl.BlockSpec(memory_space=pltpu.VMEM)] * len(out_shape),
    )


def _line_pairs(n, first=0):
    up = [(i, i + 1) for i in range(first, n - 1)]
    down = [(j, i) for i, j in up]
    return up, down


def _broadcast_blocks(own, me, n, first):
    if (n, first) == (4, 1):
        r1 = lax.ppermute(own, "gx", [(2, 0), (3, 1), (1, 2)])
        a = jnp.where((me == 0) | (me == 2), r1, own)
        b = jnp.where((me == 1) | (me == 0), r1, own)
        r2 = lax.ppermute(jnp.stack([a, b]), "gx", [(0, 1), (1, 0), (2, 3), (3, 2)])
        b1 = jnp.where(me == 1, own, jnp.where(me == 2, r1, r2[0]))
        b2 = jnp.where(me == 0, r1, jnp.where(me == 1, r2[0], jnp.where(me == 2, own, r2[1])))
        b3 = jnp.where(me == 0, r2[1], jnp.where(me == 1, r1, jnp.where(me == 2, r2[0], own)))
        return jnp.concatenate([b1, b2, b3], axis=2)
    owners = list(range(first, n))
    held = [own]
    for s in range(1, n):
        held.append(lax.ppermute(own, "gx", [(k, (k + s) % n) for k in owners]))
    held = jnp.stack(held)
    pieces = [lax.dynamic_index_in_dim(held, (me - k) % n, 0, keepdims=False) for k in owners]
    return jnp.concatenate(pieces, axis=2)


def on_device(
    earlier_window_curl_state,
    material_resistivity_inverse,
    winding_current_pattern,
    winding_axial_centre,
    specimen_presence_flags,
    specimen_kelvin_values,
):
    depth, height, breadth = material_resistivity_inverse.shape
    n_gz, n_gy, n_gx = lax.axis_size("gz"), lax.axis_size("gy"), lax.axis_size("gx")
    z_total, y_total, x_total = depth * n_gz, height * n_gy, breadth * n_gx
    gz_i, gy_i, gx_i = lax.axis_index("gz"), lax.axis_index("gy"), lax.axis_index("gx")
    z_start, y_start, x_start = gz_i * depth, gy_i * height, gx_i * breadth
    rows = height + 2 * H
    lanes = -(-(breadth + 2 * H) // 128) * 128
    gap = lanes - breadth - 2 * H
    specimen_columns = specimen_kelvin_values.shape[2]
    offset = x_total - specimen_columns
    assert offset % breadth == 0 and depth % MB == 0 and height % MB == 0 and breadth % MB == 0
    first_owner = offset // breadth

    coil_width = z_total // 4
    axial = (
        (z_start + jnp.arange(depth)).astype(jnp.float32)
        - winding_axial_centre[0].astype(jnp.float32)
    ) / coil_width
    profile = 1.0 / (1.0 + axial * axial)

    stack = jnp.concatenate(
        [earlier_window_curl_state.reshape(2 * depth, height, breadth), material_resistivity_inverse,
         winding_current_pattern], axis=0)
    up_x, down_x = _line_pairs(n_gx)
    from_left = lax.ppermute(jnp.swapaxes(stack[:, :, breadth - H:], 1, 2), "gx", up_x)
    from_right = lax.ppermute(jnp.swapaxes(stack[:, :, :H], 1, 2), "gx", down_x)
    nch = stack.shape[0]
    xext = jnp.concatenate(
        [stack, jnp.swapaxes(from_right, 1, 2), jnp.zeros((nch, height, gap), jnp.float32),
         jnp.swapaxes(from_left, 1, 2)], axis=2)

    j_start = x_start - offset
    kpad = jnp.pad(specimen_kelvin_values, ((0, 0), (0, 0), (H, H)))
    t_body = lax.dynamic_slice_in_dim(kpad, j_start + H, breadth + H, 2)
    t_tail = lax.dynamic_slice_in_dim(kpad, j_start, H, 2)
    t_x = jnp.concatenate([t_body, jnp.zeros((depth, height, gap), jnp.float32), t_tail], axis=2)

    ystack = jnp.concatenate([xext, t_x], axis=0)
    up_y, down_y = _line_pairs(n_gy)
    from_above = lax.ppermute(ystack[:, height - H:, :], "gy", up_y)
    from_below = lax.ppermute(ystack[:, :H, :], "gy", down_y)
    pieces = (ystack, from_below, from_above)

    def planes_of(idx):
        return jnp.concatenate([p[idx] for p in pieces], axis=-2)

    fb = specimen_presence_flags.shape
    flags = jnp.pad(specimen_presence_flags.astype(jnp.float32),
                    ((0, 0), (0, 128 - fb[1]), (0, 128 - fb[2])))
    pos = jnp.stack([z_start // MB, y_start // MB, x_start // MB]).astype(jnp.int32)

    up_z, down_z = _line_pairs(n_gz)
    fshape = jax.ShapeDtypeStruct((2 * depth, rows, lanes), jnp.float32)
    plane2 = jax.ShapeDtypeStruct((2, rows, lanes), jnp.float32)
    qshape = jax.ShapeDtypeStruct((depth, rows, lanes), jnp.float32)
    oshape = jax.ShapeDtypeStruct((2, depth, height, breadth), jnp.float32)
    tshape = jax.ShapeDtypeStruct((depth, rows, lanes), jnp.float32)
    tplane = jax.ShapeDtypeStruct((rows, lanes), jnp.float32)
    town = jax.ShapeDtypeStruct((depth, height, breadth), jnp.float32)
    em_totals = (height, breadth, y_total, x_total)
    t_totals = (height, breadth, offset // MB)
    lo_idx = jnp.array([0, depth])
    hi_idx = jnp.array([depth - 1, 2 * depth - 1])
    pair = n_gz == 2
    both = [(0, 1), (1, 0)]
    if pair:
        top = gz_i == 0
        first = planes_of(jnp.where(
            top, jnp.array([depth - 1, 2 * depth - 1, 3 * depth + 2 + depth - 1]),
            jnp.array([0, depth, 3 * depth + 2])))
        got = lax.ppermute(first[:2], "gz", both)
        got_t = lax.ppermute(first[2:], "gz", both)
    else:
        lo_plane, hi_plane = planes_of(lo_idx), planes_of(hi_idx)
        tzlo0 = lax.ppermute(planes_of(3 * depth + 2 + depth - 1), "gz", up_z)
        tzhi0 = lax.ppermute(planes_of(3 * depth + 2), "gz", down_z)
    for i, factor in enumerate(WEIGHTS):
        last = i == len(WEIGHTS) - 1
        if pair:
            zlo = zhi = got if i == 0 else lax.ppermute(send, "gz", both)
        else:
            zlo = lax.ppermute(hi_plane, "gz", up_z)
            zhi = lax.ppermute(lo_plane, "gz", down_z)
        if last:
            mshape = jax.ShapeDtypeStruct((depth // MB + 2, rows, lanes), jnp.float32)
            outs = (qshape, oshape, tshape, tplane, mshape) if pair else (
                qshape, oshape, tshape, tplane, tplane, mshape)

            def fused(pos_r, prof_r, fl_r, f_r, ys_r, yb_r, ya_r, zlo_r, zhi_r, *rest,
                      factor=factor):
                mat_r = _Rows(ys_r, yb_r, ya_r, 2 * depth, depth)
                w_r = _Rows(ys_r, yb_r, ya_r, 3 * depth, 2)
                t_r = _Rows(ys_r, yb_r, ya_r, 3 * depth + 2, depth)
                if pair:
                    tzlo_r = tzhi_r = rest[0].at[0]
                    outs_r = rest[1:]
                else:
                    tzlo_r, tzhi_r = rest[0], rest[1]
                    outs_r = rest[2:]
                q_r, own_r = outs_r[0], outs_r[1]
                _em_kernel(factor, True, pair, depth, em_totals, pos_r, prof_r, fl_r, f_r, mat_r,
                           w_r, zlo_r, zhi_r, q_r, own_r)
                _heat_kernel(False, pair, depth, t_totals, pos_r, fl_r, t_r, q_r, tzlo_r, tzhi_r,
                             *outs_r[2:-1], masks_out=outs_r[-1])

            extra = (got_t,) if pair else (tzlo0, tzhi0)
            res = _vmem_call(fused, outs, 9 + len(extra), 2)(
                pos, profile, flags, field, *pieces, zlo, zhi, *extra)
            heat, field_out, kelvin, t_masks = res[0], res[1], res[2], res[-1]
            if pair:
                send_t = res[3]
            else:
                lo_t, hi_t = res[3], res[4]
        else:
            outs = (fshape, plane2) if pair else (fshape, plane2, plane2)
            def sweep(pos_r, prof_r, fl_r, *rest, factor=factor, i=i):
                if i == 0:
                    ys_r, yb_r, ya_r = rest[:3]
                    f_r = _Rows(ys_r, yb_r, ya_r, 0, 2 * depth)
                    rest = rest[3:]
                else:
                    f_r, ys_r, yb_r, ya_r = rest[:4]
                    rest = rest[4:]
                mat_r = _Rows(ys_r, yb_r, ya_r, 2 * depth, depth)
                w_r = _Rows(ys_r, yb_r, ya_r, 3 * depth, 2)
                _em_kernel(factor, False, pair, depth, em_totals, pos_r, prof_r, fl_r, f_r, mat_r,
                           w_r, *rest)

            fargs = () if i == 0 else (field,)
            res = _vmem_call(sweep, outs, 8 + len(fargs), 2)(
                pos, profile, flags, *fargs, *pieces, zlo, zhi)
            if pair:
                field, send = res
            else:
                field, lo_plane, hi_plane = res

    for number in range(1, STEPS):
        last = number == STEPS - 1
        if pair:
            tzlo = tzhi = lax.ppermute(send_t, "gz", both)
        else:
            tzlo = lax.ppermute(hi_t, "gz", up_z)
            tzhi = lax.ppermute(lo_t, "gz", down_z)
        outs = (town,) if last else (tshape, tplane) if pair else (tshape, tplane, tplane)
        res = _vmem_call(
            lambda *r, last=last: _heat_kernel(
                last, pair, depth, t_totals, *r[:6], *r[7:], masks_in=r[6]), outs, 7, 1
        )(pos, flags, kelvin, heat, tzlo, tzhi, t_masks)
        if last:
            (own_t,) = res
        elif pair:
            kelvin, send_t = res
        else:
            kelvin, lo_t, hi_t = res

    segment_kelvin = _broadcast_blocks(own_t, gx_i, n_gx, first_owner)
    return (field_out, segment_kelvin)


def solution(mesh):
    placed = (
        P(None, "gz", "gy", "gx"),
        P("gz", "gy", "gx"),
        P(None, "gy", "gx"),
        P(),
        P(),
        P("gz", "gy", None),
    )
    return jax.shard_map(
        on_device,
        mesh=mesh,
        in_specs=placed,
        out_specs=(P(None, "gz", "gy", "gx"), P("gz", "gy", None)),
        check_vma=False,
    )
```
